32 devices in a mesh: groups: 2 (over x), seq: 16 (over z, y, core).
Axes of the slice: x: 2, y: 2, z: 4, core: 2. Of those that a mesh axis runs over, the one named last changes fastest.
Arguments:
- queries: bfloat16 [16384, 768], P(('groups', 'seq')), parts along dimension 0, may hold values from -8 to 8
- keys: bfloat16 [16384, 768], P(('groups', 'seq')), parts along dimension 0, may hold values from -8 to 8
- values: bfloat16 [16384, 768], P(('groups', 'seq')), parts along dimension 0, may hold values from -6 to 6
- d_out: bfloat16 [16384, 768], P(('groups', 'seq')), parts along dimension 0, may hold values from -6 to 6
- glob_pos: int32 [256], P('groups'), parts along dimension 0, may hold values from 0 to 8141, as said below
- block_len: int32 [256], P('groups'), parts along dimension 0, may hold values from 16 to 64
Outputs:
- out: bfloat16 [16384, 768], P(('groups', 'seq')), parts along dimension 0
- d_queries: bfloat16 [16384, 768], P(('groups', 'seq')), parts along dimension 0
- d_keys: bfloat16 [16384, 768], P(('groups', 'seq')), parts along dimension 0
- d_values: bfloat16 [16384, 768], P(('groups', 'seq')), parts along dimension 0
The draws below stay inside these ranges and needn't reach their ends.
There are 2 independent parts, one for each index of `groups`. The reference program is written for one: setup_inputs(seed, part) draws one part's arguments, and reference() takes and returns one part's arrays. A program takes and returns all parts, laid end to end along the dimension named above; each array names one. Nothing has to cross between parts.
Inputs may be any that keep to these rules, and one draw needn't show every extreme that they name: `glob_pos`: 128 distinct positions, no two in the same block of 64 tokens, each at an offset below 14 in its block.
All inputs are finite; a program needn't handle non-finite values.
Results may differ from the reference program's by a relative error of at most 0.0039.
The reference program's roundings to bfloat16 on the way (of `weight` and `dscore`) count: a program that leaves them out, or rounds other values in their place, can miss the bound.
Values may be sent and summed in bfloat16 or wider, within the bound.
No kernel may reach another device: no remote copies, remote signals or barrier semaphores. Data moves between devices by JAX's collectives and lax.ppermute only.
A program may use at most 256 MiB of HBM per device.

```python
import jax
import jax.numpy as jnp
from jax import lax

D = 768
HEADS = 12
BLOCK = 64
REACH = 3
GLOBALS = 128
HEAD_DIM = 64
TOKENS = 8192
NBLOCKS = 128


def glob_layout(key):
    source = jax.random.fold_in(key, 7)
    middle = 1 + jax.random.permutation(jax.random.fold_in(source, 1), NBLOCKS - 2)[:GLOBALS - 2]
    order = jnp.concatenate([jnp.array([0, NBLOCKS - 1], dtype=jnp.int32), middle.astype(jnp.int32)])
    offsets = jax.random.randint(jax.random.fold_in(source, 2), (GLOBALS,), 0, BLOCK // 4 - 2)
    offsets = offsets.at[0].set(0).at[1].set(BLOCK // 4 - 3)
    return (order * BLOCK + offsets).astype(jnp.int32)


def base_field(key, salt):
    return jnp.clip(jax.random.normal(jax.random.fold_in(key, salt), (TOKENS, D), jnp.float32) * 1.7, -8.0, 8.0)


def draw_queries(key, part):
    field = base_field(key, 1)
    return field.astype(jnp.bfloat16)


def draw_keys(key, part):
    field = base_field(key, 2)
    return field.astype(jnp.bfloat16)


def draw_glob_pos(key, part):
    return glob_layout(key)


def draw_block_len(key, part):
    cut = jax.random.randint(jax.random.fold_in(key, 21), (NBLOCKS,), 0, BLOCK - BLOCK // 4 + 1)
    which = jax.random.randint(jax.random.fold_in(key, 22), (NBLOCKS,), 0, 3) == 0
    lens = BLOCK - jnp.where(which, cut, 0)
    lens = lens.at[0].set(BLOCK).at[1].set(BLOCK // 4)
    return lens.astype(jnp.int32)


def level_of(key, shape, cuts, least, largest):
    loudness = 1.0
    for dim, blocks in cuts:
        heights = jax.random.uniform(jax.random.fold_in(jax.random.fold_in(key, 6), dim), (blocks,), jnp.float32, least / len(cuts), largest / len(cuts))
        loudness = loudness * jnp.repeat(jnp.exp(heights), shape[dim] // blocks).reshape((-1,) + (1,) * (len(shape) - 1 - dim))
    return loudness


def noise(rng, shape, deviation, reach, split=(), kind=jnp.bfloat16):
    gain = level_of(rng, shape, split, -0.22, 0.18) if split else 1.0
    values = jax.random.normal(rng, shape, jnp.float32) * deviation * gain
    return jnp.minimum(jnp.maximum(values, -reach), reach).astype(kind)


def setup_inputs(seed: int = 0, part: int = 0) -> dict:
    splits = jax.random.split(jax.random.key(seed), 7)
    own_keys = jax.random.split(jax.random.fold_in(splits[6], part), 7)
    return {
        "queries": draw_queries(jax.random.fold_in(jax.random.fold_in(splits[6], part), 71), part),
        "keys": draw_keys(jax.random.fold_in(jax.random.fold_in(splits[6], part), 71), part),
        "values": noise(own_keys[2], (TOKENS, D), 1.0, 6.0, ((0, 16),)),
        "d_out": noise(own_keys[3], (TOKENS, D), 1.0, 6.0, ((0, 16),)),
        "glob_pos": draw_glob_pos(jax.random.fold_in(jax.random.fold_in(splits[6], part), 71), part),
        "block_len": draw_block_len(jax.random.fold_in(jax.random.fold_in(splits[6], part), 71), part),
    }


neg_large = -1.0e30


def mixed(form, left, right):
    return jnp.einsum(form, left.astype(jnp.float32), right.astype(jnp.float32), precision=lax.Precision.HIGHEST)


def by_head(array):
    return array.reshape(array.shape[:-1] + (HEADS, HEAD_DIM))


def key_flags(first_pos, span_len, glob_pos, lens_wide):
    places = first_pos + jnp.arange(span_len, dtype=jnp.int32)
    begin = jnp.asarray(first_pos // BLOCK + 2 * REACH, dtype=jnp.int32)
    lens = lax.dynamic_slice_in_dim(lens_wide, begin, span_len // BLOCK)
    inside = (jnp.arange(BLOCK, dtype=jnp.int32)[None, :] < lens[:, None]).reshape(span_len)
    marked = jnp.any(glob_pos[:, None] == places[None, :], axis=0)
    return inside, marked


def windows(wide, blocks):
    extent = 2 * REACH + 1
    pieces = [wide[offset * BLOCK:offset * BLOCK + blocks * BLOCK].reshape((blocks, 1, BLOCK) + wide.shape[1:]) for offset in range(extent)]
    return jnp.concatenate(pieces, axis=1).reshape((blocks, extent * BLOCK) + wide.shape[1:])


def unfold(window, blocks):
    extent = 2 * REACH + 1
    pieces = window.reshape((blocks, extent, BLOCK) + window.shape[2:])
    total = jnp.zeros((blocks + extent - 1, BLOCK) + window.shape[2:], window.dtype)
    for offset in range(extent):
        total = total.at[offset:offset + blocks].add(pieces[:, offset])
    return total.reshape(((blocks + extent - 1) * BLOCK,) + window.shape[2:])


def forward_rows(query_blk, key_win, value_win, allowed_win, key_glob, value_glob):
    scale = HEAD_DIM ** -0.5
    heads_q = by_head(query_blk)
    band_score = mixed("nqhe,nkhe->nhqk", heads_q, by_head(key_win)) * scale
    band_score = jnp.where(allowed_win[:, None, None, :], band_score, neg_large)
    glob_score = mixed("nqhe,ghe->nhqg", heads_q, by_head(key_glob)) * scale
    top_score = jnp.maximum(jnp.max(band_score, axis=-1), jnp.max(glob_score, axis=-1))[..., None]
    norm_sum = jnp.sum(jnp.exp(band_score - top_score), axis=-1) + jnp.sum(jnp.exp(glob_score - top_score), axis=-1)
    log_norm = top_score + jnp.log(norm_sum)[..., None]
    band_weight = jnp.exp(band_score - log_norm).astype(jnp.bfloat16)
    glob_weight = jnp.exp(glob_score - log_norm).astype(jnp.bfloat16)
    result = mixed("nhqk,nkhe->nqhe", band_weight, by_head(value_win)) + mixed("nhqg,ghe->nqhe", glob_weight, by_head(value_glob))
    blocks = query_blk.shape[0]
    return result.reshape(blocks * BLOCK, D), jnp.transpose(log_norm[..., 0], (0, 2, 1)).reshape(blocks * BLOCK, HEADS)


def band_grads(query_blk, dout_blk, lse_blk, delta_blk, marked_blk, key_win, value_win, allowed_win):
    scale = HEAD_DIM ** -0.5
    heads_q = by_head(query_blk)
    heads_do = by_head(dout_blk)
    heads_k = by_head(key_win)
    heads_v = by_head(value_win)
    score = mixed("nqhe,nkhe->nhqk", heads_q, heads_k) * scale
    keep = allowed_win[:, None, None, :] & jnp.logical_not(marked_blk)[:, None, :, None]
    lse_t = jnp.transpose(lse_blk, (0, 2, 1))[..., None]
    delta_t = jnp.transpose(delta_blk, (0, 2, 1))[..., None]
    prob = jnp.where(keep, jnp.exp(score - lse_t), 0.0)
    weight = prob.astype(jnp.bfloat16)
    dprob = mixed("nqhe,nkhe->nhqk", heads_do, heads_v)
    dscore = (prob * (dprob - delta_t)).astype(jnp.bfloat16)
    grad_q = mixed("nhqk,nkhe->nqhe", dscore, heads_k) * scale
    grad_k = mixed("nhqk,nqhe->nkhe", dscore, heads_q) * scale
    grad_v = mixed("nhqk,nqhe->nkhe", weight, heads_do)
    blocks = query_blk.shape[0]
    return grad_q.reshape(blocks * BLOCK, D), grad_k.reshape(blocks, -1, D), grad_v.reshape(blocks, -1, D)


def glob_key_grads(queries, d_out, lse_rows, delta, marked_rows, key_glob, value_glob):
    scale = HEAD_DIM ** -0.5
    score = mixed("rhe,ghe->rhg", by_head(queries), by_head(key_glob)) * scale
    prob = jnp.where(marked_rows[:, None, None], 0.0, jnp.exp(score - lse_rows[..., None]))
    weight = prob.astype(jnp.bfloat16)
    dprob = mixed("rhe,ghe->rhg", by_head(d_out), by_head(value_glob))
    dscore = (prob * (dprob - delta[..., None])).astype(jnp.bfloat16)
    grad_q = mixed("rhg,ghe->rhe", dscore, by_head(key_glob)) * scale
    grad_k = mixed("rhg,rhe->ghe", dscore, by_head(queries)) * scale
    grad_v = mixed("rhg,rhe->ghe", weight, by_head(d_out))
    return grad_q.reshape(-1, D), grad_k.reshape(GLOBALS, D), grad_v.reshape(GLOBALS, D)


def glob_row_scores(query_glob, key_rows, inside):
    scale = HEAD_DIM ** -0.5
    score = mixed("ghe,rhe->hgr", by_head(query_glob), by_head(key_rows)) * scale
    return jnp.where(inside[None, None, :], score, neg_large)


def glob_row_grads(score, lse_glob, dout_glob, out_glob, key_rows, value_rows, query_glob):
    scale = HEAD_DIM ** -0.5
    prob = jnp.exp(score - lse_glob[..., None])
    weight = prob.astype(jnp.bfloat16)
    delta_glob = jnp.transpose(jnp.sum(by_head(dout_glob).astype(jnp.float32) * by_head(out_glob).astype(jnp.float32), axis=-1))
    dprob = mixed("ghe,rhe->hgr", by_head(dout_glob), by_head(value_rows))
    dscore = (prob * (dprob - delta_glob[..., None])).astype(jnp.bfloat16)
    grad_q = mixed("hgr,rhe->ghe", dscore, by_head(key_rows)) * scale
    grad_k = mixed("hgr,ghe->rhe", dscore, by_head(query_glob)) * scale
    grad_v = mixed("hgr,ghe->rhe", weight, by_head(dout_glob))
    return grad_q.reshape(GLOBALS, D), grad_k.reshape(-1, D), grad_v.reshape(-1, D)


def reference(queries, keys, values, d_out, glob_pos, block_len):
    row_count = TOKENS
    reach_rows = REACH * BLOCK
    group_blocks = 8
    group_rows = group_blocks * BLOCK
    group_count = row_count // group_rows
    span_rows = group_rows + 2 * reach_rows
    lens_wide = jnp.pad(block_len, 2 * REACH)
    places = jnp.arange(row_count, dtype=jnp.int32)
    marked_rows = jnp.any(glob_pos[:, None] == places[None, :], axis=0)
    inside_rows = (places % BLOCK) < jnp.repeat(block_len, BLOCK)
    query_glob = queries[glob_pos]
    key_glob = keys[glob_pos]
    value_glob = values[glob_pos]
    dout_glob = d_out[glob_pos]
    padding = ((reach_rows, reach_rows), (0, 0))
    key_wide = jnp.pad(keys, padding)
    value_wide = jnp.pad(values, padding)
    inside_wide, marked_wide = key_flags(-reach_rows, row_count + 2 * reach_rows, glob_pos, lens_wide)
    allowed_wide = inside_wide & jnp.logical_not(marked_wide)

    def forward_group(index):
        first = (index * group_rows).astype(jnp.int32)
        query_blk = lax.dynamic_slice_in_dim(queries, first, group_rows).reshape(group_blocks, BLOCK, D)
        key_win = windows(lax.dynamic_slice_in_dim(key_wide, first, span_rows), group_blocks)
        value_win = windows(lax.dynamic_slice_in_dim(value_wide, first, span_rows), group_blocks)
        allowed_win = windows(lax.dynamic_slice_in_dim(allowed_wide, first, span_rows), group_blocks)
        return forward_rows(query_blk, key_win, value_win, allowed_win, key_glob, value_glob)

    band_out, lse_rows = lax.map(forward_group, jnp.arange(group_count, dtype=jnp.int32))
    band_out = band_out.reshape(row_count, D)
    lse_rows = lse_rows.reshape(row_count, HEADS)

    glob_score = glob_row_scores(query_glob, keys, inside_rows)
    top_glob = jnp.max(glob_score, axis=-1)
    lse_glob = top_glob + jnp.log(jnp.sum(jnp.exp(glob_score - top_glob[..., None]), axis=-1))
    glob_weight = jnp.exp(glob_score - lse_glob[..., None]).astype(jnp.bfloat16)
    out_glob = mixed("hgr,rhe->ghe", glob_weight, by_head(values)).reshape(GLOBALS, D)
    out_full = band_out.at[glob_pos].set(out_glob).astype(jnp.bfloat16)
    out_glob16 = out_full[glob_pos]

    delta = jnp.sum(by_head(d_out).astype(jnp.float32) * by_head(out_full).astype(jnp.float32), axis=-1)

    def backward_group(carry, index):
        grad_kw, grad_vw = carry
        first = (index * group_rows).astype(jnp.int32)
        query_blk = lax.dynamic_slice_in_dim(queries, first, group_rows).reshape(group_blocks, BLOCK, D)
        dout_blk = lax.dynamic_slice_in_dim(d_out, first, group_rows).reshape(group_blocks, BLOCK, D)
        lse_blk = lax.dynamic_slice_in_dim(lse_rows, first, group_rows).reshape(group_blocks, BLOCK, HEADS)
        delta_blk = lax.dynamic_slice_in_dim(delta, first, group_rows).reshape(group_blocks, BLOCK, HEADS)
        marked_blk = lax.dynamic_slice_in_dim(marked_rows, first, group_rows).reshape(group_blocks, BLOCK)
        key_win = windows(lax.dynamic_slice_in_dim(key_wide, first, span_rows), group_blocks)
        value_win = windows(lax.dynamic_slice_in_dim(value_wide, first, span_rows), group_blocks)
        allowed_win = windows(lax.dynamic_slice_in_dim(allowed_wide, first, span_rows), group_blocks)
        grad_q, grad_k, grad_v = band_grads(query_blk, dout_blk, lse_blk, delta_blk, marked_blk, key_win, value_win, allowed_win)
        grad_kw = lax.dynamic_update_slice_in_dim(grad_kw, lax.dynamic_slice_in_dim(grad_kw, first, span_rows) + unfold(grad_k, group_blocks), first, 0)
        grad_vw = lax.dynamic_update_slice_in_dim(grad_vw, lax.dynamic_slice_in_dim(grad_vw, first, span_rows) + unfold(grad_v, group_blocks), first, 0)
        return (grad_kw, grad_vw), grad_q

    zeros_wide = jnp.zeros((row_count + 2 * reach_rows, D), jnp.float32)
    (grad_kw, grad_vw), band_dq = lax.scan(backward_group, (zeros_wide, zeros_wide), jnp.arange(group_count, dtype=jnp.int32))
    band_dq = band_dq.reshape(row_count, D)
    band_dk = grad_kw[reach_rows:reach_rows + row_count]
    band_dv = grad_vw[reach_rows:reach_rows + row_count]

    key_dq, glob_dk, glob_dv = glob_key_grads(queries, d_out, lse_rows, delta, marked_rows, key_glob, value_glob)
    row_dq, part_dk, part_dv = glob_row_grads(glob_score, lse_glob, dout_glob, out_glob16, keys, values, query_glob)

    d_queries = (band_dq + key_dq).at[glob_pos].add(row_dq)
    d_keys = (band_dk + part_dk).at[glob_pos].add(glob_dk)
    d_values = (band_dv + part_dv).at[glob_pos].add(glob_dv)
    return out_full, d_queries.astype(jnp.bfloat16), d_keys.astype(jnp.bfloat16), d_values.astype(jnp.bfloat16)
```

```python
import jax
import jax.numpy as jnp
from jax import lax
from jax.sharding import PartitionSpec as P

D = 768
HEADS = 12
BLOCK = 64
REACH = 3
GLOBALS = 128
HEAD_DIM = 64
TILE_BLOCKS = 2

neg_large = -1e30


def mixed(form, left, right):
    return jnp.einsum(form, left, right, preferred_element_type=jnp.float32)


def to_heads(array):
    rows = array.shape[0]
    return jnp.transpose(array.reshape(rows, HEADS, HEAD_DIM), (1, 0, 2))


def from_heads(array):
    rows = array.shape[1]
    return jnp.transpose(array, (1, 0, 2)).reshape(rows, D)


def halo(cells, width):
    count = lax.axis_size("seq")
    ends = count - 1
    head = lax.slice_in_dim(cells, 0, width, axis=1)
    tail = lax.slice_in_dim(cells, cells.shape[1] - width, cells.shape[1], axis=1)
    from_left = lax.ppermute(tail, "seq", [(i, i + 1) for i in range(ends)])
    from_right = lax.ppermute(head, "seq", [(i + 1, i) for i in range(ends)])
    return from_left, from_right


def key_flags(first_pos, span_len, glob_pos, lens_wide):
    places = first_pos + jnp.arange(span_len, dtype=jnp.int32)
    begin = jnp.asarray(first_pos // BLOCK + 2 * REACH, dtype=jnp.int32)
    lens = lax.dynamic_slice_in_dim(lens_wide, begin, span_len // BLOCK)
    inside = (jnp.arange(BLOCK, dtype=jnp.int32)[None, :] < lens[:, None]).reshape(span_len)
    marked = jnp.any(glob_pos[:, None] == places[None, :], axis=0)
    return (inside, marked)


def local(queries, keys, values, d_out, glob_pos, block_len):
    scale = HEAD_DIM ** (-0.5)
    rows = queries.shape[0]
    reach_rows = REACH * BLOCK
    tile_rows = TILE_BLOCKS * BLOCK
    tiles = rows // tile_rows
    win_rows = tile_rows + 2 * reach_rows
    wide_rows = rows + 2 * reach_rows
    first_row = lax.axis_index("seq") * rows
    lens_wide = jnp.pad(block_len, 2 * REACH)

    places = first_row + jnp.arange(rows, dtype=jnp.int32)
    marked_rows = jnp.any(glob_pos[:, None] == places[None, :], axis=0)
    local_pos = glob_pos - first_row
    is_local = (local_pos >= 0) & (local_pos < rows)
    local_index = jnp.where(is_local, local_pos, rows)
    inside_rows, _ = key_flags(first_row, rows, glob_pos, lens_wide)

    stacked = jnp.stack([queries, keys, values, d_out])
    picked = jnp.take(stacked, jnp.clip(local_pos, 0, rows - 1), axis=1)
    picked = jnp.where(is_local[None, :, None], picked, jnp.zeros_like(picked))
    shared = lax.psum(picked, "seq")
    qg = to_heads(shared[0])
    kg = to_heads(shared[1])
    vg = to_heads(shared[2])
    dog = to_heads(shared[3])

    pair = jnp.stack([keys, values])
    from_left, from_right = halo(pair, reach_rows)
    pair_wide = jnp.concatenate([from_left, pair, from_right], axis=1)
    kw_h = to_heads(pair_wide[0])
    vw_h = to_heads(pair_wide[1])
    q_h = to_heads(queries)
    do_h = to_heads(d_out)
    k_h = to_heads(keys)
    v_h = to_heads(values)

    inside_wide, marked_wide = key_flags(first_row - reach_rows, wide_rows, glob_pos, lens_wide)
    allowed_wide = inside_wide & jnp.logical_not(marked_wide)

    def window(array):
        return jnp.stack(
            [lax.slice_in_dim(array, t * tile_rows, t * tile_rows + win_rows, axis=1) for t in range(tiles)],
            axis=1,
        )

    def with_glob(win, glob):
        glob_b = jnp.broadcast_to(glob[:, None], (HEADS, tiles) + glob.shape[1:])
        return jnp.concatenate([win, glob_b], axis=2)

    k_t = with_glob(window(kw_h), kg)
    v_t = with_glob(window(vw_h), vg)
    q_t = q_h.reshape(HEADS, tiles, tile_rows, HEAD_DIM)
    do_t = do_h.reshape(HEADS, tiles, tile_rows, HEAD_DIM)

    allowed_t = jnp.stack(
        [lax.slice_in_dim(allowed_wide, t * tile_rows, t * tile_rows + win_rows) for t in range(tiles)]
    )
    q_block = (jnp.arange(rows, dtype=jnp.int32) // BLOCK).reshape(tiles, tile_rows)
    k_block = jnp.stack(
        [t * TILE_BLOCKS + jnp.arange(win_rows, dtype=jnp.int32) // BLOCK - REACH for t in range(tiles)]
    )
    near = jnp.abs(q_block[:, :, None] - k_block[:, None, :]) <= REACH
    band_mask = near & allowed_t[:, None, :]
    mask = jnp.concatenate([band_mask, jnp.ones((tiles, tile_rows, GLOBALS), bool)], axis=2)

    score = mixed("htqe,htke->htqk", q_t, k_t) * scale
    score = jnp.where(mask[None], score, neg_large)
    top = jnp.max(score, axis=-1, keepdims=True)
    norm = jnp.sum(jnp.exp(score - top), axis=-1, keepdims=True)
    lse = top + jnp.log(norm)
    prob = jnp.exp(score - lse)
    weight = prob.astype(jnp.bfloat16)
    out_t = mixed("htqk,htke->htqe", weight, v_t)
    band_out = from_heads(out_t.reshape(HEADS, rows, HEAD_DIM))

    g_score = mixed("hge,hre->hgr", qg, k_h) * scale
    g_score = jnp.where(inside_rows[None, None, :], g_score, neg_large)
    g_top = jnp.max(g_score, axis=-1)
    g_sum = jnp.sum(jnp.exp(g_score - g_top[..., None]), axis=-1)
    stats = lax.all_gather(jnp.stack([g_top, g_sum]), "seq")
    all_top = stats[:, 0]
    top_glob = jnp.max(all_top, axis=0)
    sum_glob = jnp.sum(stats[:, 1] * jnp.exp(all_top - top_glob[None]), axis=0)
    lse_glob = top_glob + jnp.log(sum_glob)
    g_prob = jnp.exp(g_score - lse_glob[..., None])
    g_weight = g_prob.astype(jnp.bfloat16)
    out_glob_h = lax.psum(mixed("hgr,hre->hge", g_weight, v_h), "seq")
    out_glob = from_heads(out_glob_h)
    out_full = band_out.at[local_index].set(out_glob, mode="drop").astype(jnp.bfloat16)

    delta = jnp.sum(
        do_h.astype(jnp.float32) * to_heads(out_full).astype(jnp.float32), axis=-1
    ).reshape(HEADS, tiles, tile_rows, 1)
    keep_row = jnp.logical_not(marked_rows).reshape(1, tiles, tile_rows, 1)
    prob_b = jnp.where(keep_row, prob, 0.0)
    weight_b = prob_b.astype(jnp.bfloat16)
    dprob = mixed("htqe,htke->htqk", do_t, v_t)
    dscore = (prob_b * (dprob - delta)).astype(jnp.bfloat16)
    dq_t = mixed("htqk,htke->htqe", dscore, k_t) * scale
    dk_t = mixed("htqk,htqe->htke", dscore, q_t) * scale
    dv_t = mixed("htqk,htqe->htke", weight_b, do_t)

    def fold(grad_t):
        band = grad_t[:, :, :win_rows]
        wide = sum(
            jnp.pad(band[:, t], ((0, 0), (t * tile_rows, (tiles - 1 - t) * tile_rows), (0, 0)))
            for t in range(tiles)
        )
        glob = jnp.sum(grad_t[:, :, win_rows:], axis=1)
        return wide, glob

    dk_wide, dk_glob = fold(dk_t)
    dv_wide, dv_glob = fold(dv_t)
    band_dq = from_heads(dq_t.reshape(HEADS, rows, HEAD_DIM))
    grad_wide = jnp.stack([from_heads(dk_wide), from_heads(dv_wide)])
    rims = jnp.concatenate(
        [grad_wide[:, :reach_rows], grad_wide[:, wide_rows - reach_rows :]], axis=1
    )
    back_left, back_right = halo(rims, reach_rows)
    center = grad_wide[:, reach_rows : reach_rows + rows]
    center = center.at[:, :reach_rows].add(back_left).at[:, rows - reach_rows :].add(back_right)

    delta_g = jnp.sum(dog.astype(jnp.float32) * to_heads(out_glob.astype(jnp.bfloat16)).astype(jnp.float32), axis=-1)
    g_dprob = mixed("hge,hre->hgr", dog, v_h)
    g_dscore = (g_prob * (g_dprob - delta_g[..., None])).astype(jnp.bfloat16)
    row_dq = mixed("hgr,hre->hge", g_dscore, k_h) * scale
    part_dk = mixed("hgr,hge->hre", g_dscore, qg) * scale
    part_dv = mixed("hgr,hge->hre", g_weight, dog)

    totals = lax.psum(jnp.stack([from_heads(row_dq), from_heads(dk_glob), from_heads(dv_glob)]), "seq")
    d_queries = band_dq.at[local_index].add(totals[0], mode="drop")
    d_keys = (center[0] + from_heads(part_dk)).at[local_index].add(totals[1], mode="drop")
    d_values = (center[1] + from_heads(part_dv)).at[local_index].add(totals[2], mode="drop")
    return (
        out_full,
        d_queries.astype(jnp.bfloat16),
        d_keys.astype(jnp.bfloat16),
        d_values.astype(jnp.bfloat16),
    )


def solution(mesh):
    rows = P(("groups", "seq"), None)
    return jax.shard_map(
        local,
        mesh=mesh,
        in_specs=(rows, rows, rows, rows, P("groups"), P("groups")),
        out_specs=(rows, rows, rows, rows),
        check_vma=False,
    )
```

```python
import jax
import jax.numpy as jnp
from jax import lax
from jax.sharding import PartitionSpec as P

D = 768
HEADS = 12
BLOCK = 64
REACH = 3
GLOBALS = 128
HEAD_DIM = 64
TILE_BLOCKS = 2

neg_large = -1e30


def mixed(form, left, right):
    return jnp.einsum(form, left, right, preferred_element_type=jnp.float32)


def to_heads(array):
    rows = array.shape[0]
    return jnp.transpose(array.reshape(rows, HEADS, HEAD_DIM), (1, 0, 2))


def from_heads(array):
    rows = array.shape[1]
    return jnp.transpose(array, (1, 0, 2)).reshape(rows, D)


def halo(cells, width):
    count = lax.axis_size("seq")
    ends = count - 1
    head = lax.slice_in_dim(cells, 0, width, axis=1)
    tail = lax.slice_in_dim(cells, cells.shape[1] - width, cells.shape[1], axis=1)
    from_left = lax.ppermute(tail, "seq", [(i, i + 1) for i in range(ends)])
    from_right = lax.ppermute(head, "seq", [(i + 1, i) for i in range(ends)])
    return from_left, from_right


def by_head(array):
    return array.reshape(array.shape[:-1] + (HEADS, HEAD_DIM))


def gather_small(part):
    count = lax.axis_size("seq")
    spread = jnp.broadcast_to(part[None], (count,) + part.shape)
    return lax.all_to_all(spread, "seq", 0, 0)


def reduce_own(full):
    count = lax.axis_size("seq")
    split = full.reshape((count, full.shape[0] // count) + full.shape[1:])
    return jnp.sum(lax.all_to_all(split, "seq", 0, 0), axis=0)


def key_flags(first_pos, span_len, glob_pos, lens_wide):
    places = first_pos + jnp.arange(span_len, dtype=jnp.int32)
    begin = jnp.asarray(first_pos // BLOCK + 2 * REACH, dtype=jnp.int32)
    lens = lax.dynamic_slice_in_dim(lens_wide, begin, span_len // BLOCK)
    inside = (jnp.arange(BLOCK, dtype=jnp.int32)[None, :] < lens[:, None]).reshape(span_len)
    marked = jnp.any(glob_pos[:, None] == places[None, :], axis=0)
    return (inside, marked)


def local(queries, keys, values, d_out, glob_pos, block_len):
    scale = HEAD_DIM ** (-0.5)
    rows = queries.shape[0]
    reach_rows = REACH * BLOCK
    tile_rows = TILE_BLOCKS * BLOCK
    tiles = rows // tile_rows
    win_rows = tile_rows + 2 * reach_rows
    wide_rows = rows + 2 * reach_rows
    first_row = lax.axis_index("seq") * rows
    lens_wide = jnp.pad(block_len, 2 * REACH)

    places = first_row + jnp.arange(rows, dtype=jnp.int32)
    marked_rows = jnp.any(glob_pos[:, None] == places[None, :], axis=0)
    local_pos = glob_pos - first_row
    is_local = (local_pos >= 0) & (local_pos < rows)
    local_index = jnp.where(is_local, local_pos, rows)
    inside_rows, _ = key_flags(first_row, rows, glob_pos, lens_wide)

    count = lax.axis_size("seq")
    own_blocks = rows // BLOCK
    slots = own_blocks * count
    glob_block = glob_pos // BLOCK
    slot_valid = jnp.zeros((slots,), bool).at[glob_block].set(True, mode="drop")
    own_slot = lax.axis_index("seq") * own_blocks + jnp.arange(own_blocks, dtype=jnp.int32)
    own_match = glob_block[None, :] == own_slot[:, None]
    own_has = jnp.any(own_match, axis=1)
    own_pos = jnp.sum(jnp.where(own_match, glob_pos[None, :], 0), axis=1) - first_row
    own_index = jnp.where(own_has, own_pos, rows)

    stacked = jnp.stack([queries, keys, values, d_out])
    picked = jnp.take(stacked, jnp.clip(own_pos, 0, rows - 1), axis=1)
    picked = jnp.where(own_has[None, :, None], picked, jnp.zeros_like(picked))
    shared = jnp.transpose(lax.all_gather(picked, "seq"), (1, 0, 2, 3)).reshape(4, slots, D)
    qg = to_heads(shared[0])
    kg = to_heads(shared[1])
    vg = to_heads(shared[2])
    dog = to_heads(shared[3])

    pair = jnp.stack([keys, values])
    from_left, from_right = halo(pair, reach_rows)
    pair_wide = jnp.concatenate([from_left, pair, from_right], axis=1)
    kw_h = to_heads(pair_wide[0])
    vw_h = to_heads(pair_wide[1])
    q_h = to_heads(queries)
    do_h = to_heads(d_out)
    k_h = to_heads(keys)
    v_h = to_heads(values)

    inside_wide, marked_wide = key_flags(first_row - reach_rows, wide_rows, glob_pos, lens_wide)
    allowed_wide = inside_wide & jnp.logical_not(marked_wide)

    def window(array):
        return jnp.stack(
            [lax.slice_in_dim(array, t * tile_rows, t * tile_rows + win_rows, axis=1) for t in range(tiles)],
            axis=1,
        )

    def with_glob(win, glob):
        glob_b = jnp.broadcast_to(glob[:, None], (HEADS, tiles) + glob.shape[1:])
        return jnp.concatenate([win, glob_b], axis=2)

    k_t = with_glob(window(kw_h), kg)
    v_t = with_glob(window(vw_h), vg)
    q_t = q_h.reshape(HEADS, tiles, tile_rows, HEAD_DIM)
    do_t = do_h.reshape(HEADS, tiles, tile_rows, HEAD_DIM)

    allowed_t = jnp.stack(
        [lax.slice_in_dim(allowed_wide, t * tile_rows, t * tile_rows + win_rows) for t in range(tiles)]
    )
    q_block = (jnp.arange(rows, dtype=jnp.int32) // BLOCK).reshape(tiles, tile_rows)
    k_block = jnp.stack(
        [t * TILE_BLOCKS + jnp.arange(win_rows, dtype=jnp.int32) // BLOCK - REACH for t in range(tiles)]
    )
    near = jnp.abs(q_block[:, :, None] - k_block[:, None, :]) <= REACH
    band_mask = near & allowed_t[:, None, :]
    glob_mask = jnp.broadcast_to(slot_valid[None, None, :], (tiles, tile_rows, slots))
    mask = jnp.concatenate([band_mask, glob_mask], axis=2)

    score = mixed("htqe,htke->htqk", q_t, k_t) * scale
    score = jnp.where(mask[None], score, neg_large)
    top = jnp.max(score, axis=-1, keepdims=True)
    norm = jnp.sum(jnp.exp(score - top), axis=-1, keepdims=True)
    lse = top + jnp.log(norm)
    prob = jnp.exp(score - lse)
    weight = prob.astype(jnp.bfloat16)
    out_t = mixed("htqk,htke->htqe", weight, v_t)
    band_out = from_heads(out_t.reshape(HEADS, rows, HEAD_DIM))

    g_score = mixed("hge,hre->hgr", qg, k_h) * scale
    g_score = jnp.where(inside_rows[None, None, :], g_score, neg_large)
    g_top = jnp.max(g_score, axis=-1)
    g_sum = jnp.sum(jnp.exp(g_score - g_top[..., None]), axis=-1)
    stats = gather_small(jnp.stack([g_top, g_sum]))
    all_top = stats[:, 0]
    top_glob = jnp.max(all_top, axis=0)
    sum_glob = jnp.sum(stats[:, 1] * jnp.exp(all_top - top_glob[None]), axis=0)
    lse_glob = top_glob + jnp.log(sum_glob)
    g_prob = jnp.where(slot_valid[None, :, None], jnp.exp(g_score - lse_glob[..., None]), 0.0)
    g_weight = g_prob.astype(jnp.bfloat16)
    out_own = reduce_own(from_heads(mixed("hgr,hre->hge", g_weight, v_h)))
    out_own16 = out_own.astype(jnp.bfloat16)
    delta_own = jnp.sum(
        by_head(picked[3]).astype(jnp.float32) * by_head(out_own16).astype(jnp.float32), axis=-1
    )
    delta_g = jnp.transpose(gather_small(delta_own).reshape(slots, HEADS))
    band_out16 = band_out.astype(jnp.bfloat16)
    out_full = band_out16.at[own_index].set(out_own16, mode="drop")

    delta = jnp.sum(
        do_h.astype(jnp.float32) * to_heads(band_out16).astype(jnp.float32), axis=-1
    ).reshape(HEADS, tiles, tile_rows, 1)
    keep_row = jnp.logical_not(marked_rows).reshape(1, tiles, tile_rows, 1)
    prob_b = jnp.where(keep_row, prob, 0.0)
    weight_b = prob_b.astype(jnp.bfloat16)
    dprob = mixed("htqe,htke->htqk", do_t, v_t)
    dscore = (prob_b * (dprob - delta)).astype(jnp.bfloat16)
    dq_t = mixed("htqk,htke->htqe", dscore, k_t) * scale
    dk_t = mixed("htqk,htqe->htke", dscore, q_t) * scale
    dv_t = mixed("htqk,htqe->htke", weight_b, do_t)

    def fold(grad_t):
        band = grad_t[:, :, :win_rows]
        wide = sum(
            jnp.pad(band[:, t], ((0, 0), (t * tile_rows, (tiles - 1 - t) * tile_rows), (0, 0)))
            for t in range(tiles)
        )
        glob = jnp.sum(grad_t[:, :, win_rows:], axis=1)
        return wide, glob

    dk_wide, dk_glob = fold(dk_t)
    dv_wide, dv_glob = fold(dv_t)
    band_dq = from_heads(dq_t.reshape(HEADS, rows, HEAD_DIM))
    grad_wide = jnp.stack([from_heads(dk_wide), from_heads(dv_wide)])
    rims = jnp.concatenate(
        [grad_wide[:, :reach_rows], grad_wide[:, wide_rows - reach_rows :]], axis=1
    )
    back_left, back_right = halo(rims, reach_rows)
    center = grad_wide[:, reach_rows : reach_rows + rows]
    center = center.at[:, :reach_rows].add(back_left).at[:, rows - reach_rows :].add(back_right)

    g_dprob = mixed("hge,hre->hgr", dog, v_h)
    g_dscore = (g_prob * (g_dprob - delta_g[..., None])).astype(jnp.bfloat16)
    row_dq = mixed("hgr,hre->hge", g_dscore, k_h) * scale
    part_dk = mixed("hgr,hge->hre", g_dscore, qg) * scale
    part_dv = mixed("hgr,hge->hre", g_weight, dog)

    totals = reduce_own(
        jnp.concatenate([from_heads(row_dq), from_heads(dk_glob), from_heads(dv_glob)], axis=1)
    )
    d_queries = band_dq.at[own_index].add(totals[:, :D], mode="drop")
    d_keys = (center[0] + from_heads(part_dk)).at[own_index].add(totals[:, D : 2 * D], mode="drop")
    d_values = (center[1] + from_heads(part_dv)).at[own_index].add(totals[:, 2 * D :], mode="drop")
    return (
        out_full,
        d_queries.astype(jnp.bfloat16),
        d_keys.astype(jnp.bfloat16),
        d_values.astype(jnp.bfloat16),
    )


def solution(mesh):
    rows = P(("groups", "seq"), None)
    return jax.shard_map(
        local,
        mesh=mesh,
        in_specs=(rows, rows, rows, rows, P("groups"), P("groups")),
        out_specs=(rows, rows, rows, rows),
        check_vma=False,
    )
```

```python
import jax
import jax.numpy as jnp
from jax import lax
from jax.sharding import PartitionSpec as P
from jax.experimental import pallas as pl
from jax.experimental.pallas import tpu as pltpu

D = 768
HEADS = 12
BLOCK = 64
REACH = 3
GLOBALS = 128
HEAD_DIM = 64
TILE_BLOCKS = 2

neg_large = -1e30


def mixed(form, left, right):
    return jnp.einsum(form, left, right, preferred_element_type=jnp.float32)


def to_heads(array):
    rows = array.shape[0]
    return jnp.transpose(array.reshape(rows, HEADS, HEAD_DIM), (1, 0, 2))


def from_heads(array):
    rows = array.shape[1]
    return jnp.transpose(array, (1, 0, 2)).reshape(rows, D)


def halo(cells, width):
    count = lax.axis_size("seq")
    ends = count - 1
    head = lax.slice_in_dim(cells, 0, width, axis=1)
    tail = lax.slice_in_dim(cells, cells.shape[1] - width, cells.shape[1], axis=1)
    from_left = lax.ppermute(tail, "seq", [(i, i + 1) for i in range(ends)])
    from_right = lax.ppermute(head, "seq", [(i + 1, i) for i in range(ends)])
    return from_left, from_right


def by_head(array):
    return array.reshape(array.shape[:-1] + (HEADS, HEAD_DIM))


def gather_small(part):
    count = lax.axis_size("seq")
    spread = jnp.broadcast_to(part[None], (count,) + part.shape)
    return lax.all_to_all(spread, "seq", 0, 0)


def reduce_own(full):
    count = lax.axis_size("seq")
    split = full.reshape((count, full.shape[0] // count) + full.shape[1:])
    return jnp.sum(lax.all_to_all(split, "seq", 0, 0), axis=0)


def key_flags(first_pos, span_len, glob_pos, lens_wide):
    places = first_pos + jnp.arange(span_len, dtype=jnp.int32)
    begin = jnp.asarray(first_pos // BLOCK + 2 * REACH, dtype=jnp.int32)
    lens = lax.dynamic_slice_in_dim(lens_wide, begin, span_len // BLOCK)
    inside = (jnp.arange(BLOCK, dtype=jnp.int32)[None, :] < lens[:, None]).reshape(span_len)
    marked = jnp.any(glob_pos[:, None] == places[None, :], axis=0)
    return (inside, marked)


def band_kernel(mask_ref, gmask_ref, keep_ref, q_ref, do_ref, kw_ref, vw_ref, kg_ref, vg_ref,
                out_ref, dq_ref, dkw_ref, dvw_ref, dkg_ref, dvg_ref):
    scale = HEAD_DIM ** (-0.5)
    tile = pl.program_id(1)
    tile_rows = q_ref.shape[0]
    win_rows = mask_ref.shape[2]
    start = pl.multiple_of(tile * tile_rows, tile_rows)
    f32 = jnp.float32
    bf16 = jnp.bfloat16
    nt = (((1,), (1,)), ((), ()))
    tn = (((0,), (0,)), ((), ()))

    @pl.when(tile == 0)
    def _():
        dkw_ref[...] = jnp.zeros_like(dkw_ref)
        dvw_ref[...] = jnp.zeros_like(dvw_ref)
        dkg_ref[...] = jnp.zeros_like(dkg_ref)
        dvg_ref[...] = jnp.zeros_like(dvg_ref)

    band_ok = mask_ref[0] > 0.5
    glob_ok = gmask_ref[...] > 0.5
    keep = keep_ref[...] > 0.5
    for head in range(q_ref.shape[1] // HEAD_DIM):
        lanes = slice(head * HEAD_DIM, (head + 1) * HEAD_DIM)
        q = q_ref[:, lanes]
        do = do_ref[:, lanes]
        kwin = kw_ref[pl.ds(start, win_rows), lanes]
        vwin = vw_ref[pl.ds(start, win_rows), lanes]
        kg = kg_ref[:, lanes]
        vg = vg_ref[:, lanes]
        s_b = lax.dot_general(q, kwin, nt, preferred_element_type=f32) * scale
        s_b = jnp.where(band_ok, s_b, neg_large)
        s_g = lax.dot_general(q, kg, nt, preferred_element_type=f32) * scale
        s_g = jnp.where(glob_ok, s_g, neg_large)
        top = jnp.maximum(jnp.max(s_b, axis=1, keepdims=True), jnp.max(s_g, axis=1, keepdims=True))
        norm = jnp.sum(jnp.exp(s_b - top), axis=1, keepdims=True) + jnp.sum(
            jnp.exp(s_g - top), axis=1, keepdims=True
        )
        lse = top + jnp.log(norm)
        p_b = jnp.exp(s_b - lse)
        p_g = jnp.exp(s_g - lse)
        out = jnp.dot(p_b.astype(bf16), vwin, preferred_element_type=f32) + jnp.dot(
            p_g.astype(bf16), vg, preferred_element_type=f32
        )
        out_ref[:, lanes] = out
        delta = jnp.sum(
            do.astype(f32) * out.astype(bf16).astype(f32), axis=1, keepdims=True
        )
        p_b = jnp.where(keep, p_b, 0.0)
        p_g = jnp.where(keep, p_g, 0.0)
        dp_b = lax.dot_general(do, vwin, nt, preferred_element_type=f32)
        dp_g = lax.dot_general(do, vg, nt, preferred_element_type=f32)
        ds_b = (p_b * (dp_b - delta)).astype(bf16)
        ds_g = (p_g * (dp_g - delta)).astype(bf16)
        dq = jnp.dot(ds_b, kwin, preferred_element_type=f32) + jnp.dot(
            ds_g, kg, preferred_element_type=f32
        )
        dq_ref[:, lanes] = dq * scale
        dk_w = lax.dot_general(ds_b, q, tn, preferred_element_type=f32) * scale
        dv_w = lax.dot_general(p_b.astype(bf16), do, tn, preferred_element_type=f32)
        dkw_ref[pl.ds(start, win_rows), lanes] += dk_w
        dvw_ref[pl.ds(start, win_rows), lanes] += dv_w
        dkg_ref[:, lanes] += lax.dot_general(ds_g, q, tn, preferred_element_type=f32) * scale
        dvg_ref[:, lanes] += lax.dot_general(p_g.astype(bf16), do, tn, preferred_element_type=f32)


def band_call(mask, gmask, keep, queries, d_out, key_wide, value_wide, key_glob, value_glob, interpret=False):
    rows = queries.shape[0]
    wide_rows = key_wide.shape[0]
    slots = key_glob.shape[0]
    tiles, tile_rows, win_rows = mask.shape
    lanes = 2 * HEAD_DIM
    pairs = D // lanes
    f32 = jnp.float32
    row_spec = pl.BlockSpec((tile_rows, lanes), lambda p, t: (t, p))
    wide_spec = pl.BlockSpec((wide_rows, lanes), lambda p, t: (0, p))
    glob_spec = pl.BlockSpec((slots, lanes), lambda p, t: (0, p))
    return pl.pallas_call(
        band_kernel,
        grid=(pairs, tiles),
        in_specs=[
            pl.BlockSpec((1, tile_rows, win_rows), lambda p, t: (t, 0, 0)),
            pl.BlockSpec((1, slots), lambda p, t: (0, 0)),
            pl.BlockSpec((tile_rows, 1), lambda p, t: (t, 0)),
            row_spec,
            row_spec,
            wide_spec,
            wide_spec,
            glob_spec,
            glob_spec,
        ],
        out_specs=[row_spec, row_spec, wide_spec, wide_spec, glob_spec, glob_spec],
        out_shape=[
            jax.ShapeDtypeStruct((rows, D), f32),
            jax.ShapeDtypeStruct((rows, D), f32),
            jax.ShapeDtypeStruct((wide_rows, D), f32),
            jax.ShapeDtypeStruct((wide_rows, D), f32),
            jax.ShapeDtypeStruct((slots, D), f32),
            jax.ShapeDtypeStruct((slots, D), f32),
        ],
        compiler_params=pltpu.CompilerParams(dimension_semantics=("arbitrary", "arbitrary")),
        interpret=interpret,
    )(mask, gmask, keep, queries, d_out, key_wide, value_wide, key_glob, value_glob)


def local(queries, keys, values, d_out, glob_pos, block_len):
    scale = HEAD_DIM ** (-0.5)
    rows = queries.shape[0]
    reach_rows = REACH * BLOCK
    tile_rows = TILE_BLOCKS * BLOCK
    tiles = rows // tile_rows
    win_rows = tile_rows + 2 * reach_rows
    wide_rows = rows + 2 * reach_rows
    first_row = lax.axis_index("seq") * rows
    lens_wide = jnp.pad(block_len, 2 * REACH)

    places = first_row + jnp.arange(rows, dtype=jnp.int32)
    marked_rows = jnp.any(glob_pos[:, None] == places[None, :], axis=0)
    local_pos = glob_pos - first_row
    is_local = (local_pos >= 0) & (local_pos < rows)
    local_index = jnp.where(is_local, local_pos, rows)
    inside_rows, _ = key_flags(first_row, rows, glob_pos, lens_wide)

    count = lax.axis_size("seq")
    own_blocks = rows // BLOCK
    slots = own_blocks * count
    glob_block = glob_pos // BLOCK
    slot_valid = jnp.zeros((slots,), bool).at[glob_block].set(True, mode="drop")
    own_slot = lax.axis_index("seq") * own_blocks + jnp.arange(own_blocks, dtype=jnp.int32)
    own_match = glob_block[None, :] == own_slot[:, None]
    own_has = jnp.any(own_match, axis=1)
    own_pos = jnp.sum(jnp.where(own_match, glob_pos[None, :], 0), axis=1) - first_row
    own_index = jnp.where(own_has, own_pos, rows)

    stacked = jnp.stack([queries, keys, values, d_out])
    picked = jnp.take(stacked, jnp.clip(own_pos, 0, rows - 1), axis=1)
    picked = jnp.where(own_has[None, :, None], picked, jnp.zeros_like(picked))
    shared = jnp.transpose(lax.all_gather(picked, "seq"), (1, 0, 2, 3)).reshape(4, slots, D)
    qg = to_heads(shared[0])
    kg = to_heads(shared[1])
    vg = to_heads(shared[2])
    dog = to_heads(shared[3])

    pair = jnp.stack([keys, values])
    from_left, from_right = halo(pair, reach_rows)
    pair_wide = jnp.concatenate([from_left, pair, from_right], axis=1)
    k_h = to_heads(keys)
    v_h = to_heads(values)

    inside_wide, marked_wide = key_flags(first_row - reach_rows, wide_rows, glob_pos, lens_wide)
    allowed_wide = inside_wide & jnp.logical_not(marked_wide)

    allowed_t = jnp.stack(
        [lax.slice_in_dim(allowed_wide, t * tile_rows, t * tile_rows + win_rows) for t in range(tiles)]
    )
    q_block = (jnp.arange(rows, dtype=jnp.int32) // BLOCK).reshape(tiles, tile_rows)
    k_block = jnp.stack(
        [t * TILE_BLOCKS + jnp.arange(win_rows, dtype=jnp.int32) // BLOCK - REACH for t in range(tiles)]
    )
    near = jnp.abs(q_block[:, :, None] - k_block[:, None, :]) <= REACH
    band_mask = near & allowed_t[:, None, :]
    band_out, band_dq, dk_wide, dv_wide, dk_glob, dv_glob = band_call(
        band_mask.astype(jnp.float32),
        slot_valid.astype(jnp.float32)[None, :],
        jnp.logical_not(marked_rows).astype(jnp.float32)[:, None],
        queries,
        d_out,
        pair_wide[0],
        pair_wide[1],
        shared[1],
        shared[2],
    )

    g_score = mixed("hge,hre->hgr", qg, k_h) * scale
    g_score = jnp.where(inside_rows[None, None, :], g_score, neg_large)
    g_top = jnp.max(g_score, axis=-1)
    g_sum = jnp.sum(jnp.exp(g_score - g_top[..., None]), axis=-1)
    stats = gather_small(jnp.stack([g_top, g_sum]))
    all_top = stats[:, 0]
    top_glob = jnp.max(all_top, axis=0)
    sum_glob = jnp.sum(stats[:, 1] * jnp.exp(all_top - top_glob[None]), axis=0)
    lse_glob = top_glob + jnp.log(sum_glob)
    g_prob = jnp.where(slot_valid[None, :, None], jnp.exp(g_score - lse_glob[..., None]), 0.0)
    g_weight = g_prob.astype(jnp.bfloat16)
    out_own = reduce_own(from_heads(mixed("hgr,hre->hge", g_weight, v_h)))
    out_own16 = out_own.astype(jnp.bfloat16)
    delta_own = jnp.sum(
        by_head(picked[3]).astype(jnp.float32) * by_head(out_own16).astype(jnp.float32), axis=-1
    )
    delta_g = jnp.transpose(gather_small(delta_own).reshape(slots, HEADS))
    band_out16 = band_out.astype(jnp.bfloat16)
    out_full = band_out16.at[own_index].set(out_own16, mode="drop")

    grad_wide = jnp.stack([dk_wide, dv_wide])
    rims = jnp.concatenate(
        [grad_wide[:, :reach_rows], grad_wide[:, wide_rows - reach_rows :]], axis=1
    )
    back_left, back_right = halo(rims, reach_rows)
    center = grad_wide[:, reach_rows : reach_rows + rows]
    center = center.at[:, :reach_rows].add(back_left).at[:, rows - reach_rows :].add(back_right)

    g_dprob = mixed("hge,hre->hgr", dog, v_h)
    g_dscore = (g_prob * (g_dprob - delta_g[..., None])).astype(jnp.bfloat16)
    row_dq = mixed("hgr,hre->hge", g_dscore, k_h) * scale
    part_dk = mixed("hgr,hge->hre", g_dscore, qg) * scale
    part_dv = mixed("hgr,hge->hre", g_weight, dog)

    totals = reduce_own(
        jnp.concatenate([from_heads(row_dq), dk_glob, dv_glob], axis=1)
    )
    d_queries = band_dq.at[own_index].add(totals[:, :D], mode="drop")
    d_keys = (center[0] + from_heads(part_dk)).at[own_index].add(totals[:, D : 2 * D], mode="drop")
    d_values = (center[1] + from_heads(part_dv)).at[own_index].add(totals[:, 2 * D :], mode="drop")
    return (
        out_full,
        d_queries.astype(jnp.bfloat16),
        d_keys.astype(jnp.bfloat16),
        d_values.astype(jnp.bfloat16),
    )


def solution(mesh):
    rows = P(("groups", "seq"), None)
    return jax.shard_map(
        local,
        mesh=mesh,
        in_specs=(rows, rows, rows, rows, P("groups"), P("groups")),
        out_specs=(rows, rows, rows, rows),
        check_vma=False,
    )
```

```python
import jax
import jax.numpy as jnp
from jax import lax
from jax.sharding import PartitionSpec as P
from jax.experimental import pallas as pl
from jax.experimental.pallas import tpu as pltpu

D = 768
HEADS = 12
BLOCK = 64
REACH = 3
GLOBALS = 128
HEAD_DIM = 64
TILE_BLOCKS = 2

neg_large = -1e30


def mixed(form, left, right):
    return jnp.einsum(form, left, right, preferred_element_type=jnp.float32)


def to_heads(array):
    rows = array.shape[0]
    return jnp.transpose(array.reshape(rows, HEADS, HEAD_DIM), (1, 0, 2))


def from_heads(array):
    rows = array.shape[1]
    return jnp.transpose(array, (1, 0, 2)).reshape(rows, D)


def halo(cells, width):
    count = lax.axis_size("seq")
    ends = count - 1
    head = lax.slice_in_dim(cells, 0, width, axis=1)
    tail = lax.slice_in_dim(cells, cells.shape[1] - width, cells.shape[1], axis=1)
    from_left = lax.ppermute(tail, "seq", [(i, i + 1) for i in range(ends)])
    from_right = lax.ppermute(head, "seq", [(i + 1, i) for i in range(ends)])
    return from_left, from_right


def by_head(array):
    return array.reshape(array.shape[:-1] + (HEADS, HEAD_DIM))


def gather_small(part):
    count = lax.axis_size("seq")
    spread = jnp.broadcast_to(part[None], (count,) + part.shape)
    return lax.all_to_all(spread, "seq", 0, 0)


def reduce_own(full):
    count = lax.axis_size("seq")
    split = full.reshape((count, full.shape[0] // count) + full.shape[1:])
    return jnp.sum(lax.all_to_all(split, "seq", 0, 0), axis=0)


def key_flags(first_pos, span_len, glob_pos, lens_wide):
    places = first_pos + jnp.arange(span_len, dtype=jnp.int32)
    begin = jnp.asarray(first_pos // BLOCK + 2 * REACH, dtype=jnp.int32)
    lens = lax.dynamic_slice_in_dim(lens_wide, begin, span_len // BLOCK)
    inside = (jnp.arange(BLOCK, dtype=jnp.int32)[None, :] < lens[:, None]).reshape(span_len)
    marked = jnp.any(glob_pos[:, None] == places[None, :], axis=0)
    return (inside, marked)


def band_kernel(mask_ref, gmask_ref, keep_ref, q_ref, do_ref, kw_ref, vw_ref, kg_ref, vg_ref,
                out_ref, dq_ref, dkw_ref, dvw_ref, dkg_ref, dvg_ref):
    scale = HEAD_DIM ** (-0.5)
    tile = pl.program_id(1)
    tile_rows = q_ref.shape[0]
    win_rows = mask_ref.shape[2]
    start = pl.multiple_of(tile * tile_rows, tile_rows)
    f32 = jnp.float32
    bf16 = jnp.bfloat16
    nt = (((1,), (1,)), ((), ()))
    tn = (((0,), (0,)), ((), ()))

    @pl.when(tile == 0)
    def _():
        dkw_ref[...] = jnp.zeros_like(dkw_ref)
        dvw_ref[...] = jnp.zeros_like(dvw_ref)
        dkg_ref[...] = jnp.zeros_like(dkg_ref)
        dvg_ref[...] = jnp.zeros_like(dvg_ref)

    band_bias = mask_ref[0]
    glob_bias = gmask_ref[...]
    keep = keep_ref[...].astype(bf16)
    for head in range(q_ref.shape[1] // HEAD_DIM):
        lanes = slice(head * HEAD_DIM, (head + 1) * HEAD_DIM)
        q = q_ref[:, lanes] * jnp.asarray(scale, bf16)
        do = do_ref[:, lanes] * keep
        kwin = kw_ref[pl.ds(start, win_rows), lanes]
        vwin = vw_ref[pl.ds(start, win_rows), lanes]
        kg = kg_ref[:, lanes]
        vg = vg_ref[:, lanes]
        s_b = lax.dot_general(q, kwin, nt, preferred_element_type=f32) + band_bias
        s_g = lax.dot_general(q, kg, nt, preferred_element_type=f32) + glob_bias
        top = jnp.maximum(jnp.max(s_b, axis=1, keepdims=True), jnp.max(s_g, axis=1, keepdims=True))
        e_b = jnp.exp(s_b - top)
        e_g = jnp.exp(s_g - top)
        inv = 1.0 / (jnp.sum(e_b, axis=1, keepdims=True) + jnp.sum(e_g, axis=1, keepdims=True))
        p_b = e_b * inv
        p_g = e_g * inv
        w_b = p_b.astype(bf16)
        w_g = p_g.astype(bf16)
        out = jnp.dot(w_b, vwin, preferred_element_type=f32) + jnp.dot(
            w_g, vg, preferred_element_type=f32
        )
        out_ref[:, lanes] = out
        delta = jnp.sum(
            do.astype(f32) * out.astype(bf16).astype(f32), axis=1, keepdims=True
        )
        dp_b = lax.dot_general(do, vwin, nt, preferred_element_type=f32)
        dp_g = lax.dot_general(do, vg, nt, preferred_element_type=f32)
        ds_b = (p_b * (dp_b - delta)).astype(bf16)
        ds_g = (p_g * (dp_g - delta)).astype(bf16)
        dq = jnp.dot(ds_b, kwin, preferred_element_type=f32) + jnp.dot(
            ds_g, kg, preferred_element_type=f32
        )
        dq_ref[:, lanes] = dq * scale
        dkw_ref[pl.ds(start, win_rows), lanes] += lax.dot_general(ds_b, q, tn, preferred_element_type=f32)
        dvw_ref[pl.ds(start, win_rows), lanes] += lax.dot_general(w_b, do, tn, preferred_element_type=f32)
        dkg_ref[:, lanes] += lax.dot_general(ds_g, q, tn, preferred_element_type=f32)
        dvg_ref[:, lanes] += lax.dot_general(w_g, do, tn, preferred_element_type=f32)


def band_call(mask, gmask, keep, queries, d_out, key_wide, value_wide, key_glob, value_glob, interpret=False):
    rows = queries.shape[0]
    wide_rows = key_wide.shape[0]
    slots = key_glob.shape[0]
    tiles, tile_rows, win_rows = mask.shape
    lanes = 2 * HEAD_DIM
    pairs = D // lanes
    f32 = jnp.float32
    row_spec = pl.BlockSpec((tile_rows, lanes), lambda p, t: (t, p))
    wide_spec = pl.BlockSpec((wide_rows, lanes), lambda p, t: (0, p))
    glob_spec = pl.BlockSpec((slots, lanes), lambda p, t: (0, p))
    return pl.pallas_call(
        band_kernel,
        grid=(pairs, tiles),
        in_specs=[
            pl.BlockSpec((1, tile_rows, win_rows), lambda p, t: (t, 0, 0)),
            pl.BlockSpec((1, slots), lambda p, t: (0, 0)),
            pl.BlockSpec((tile_rows, 1), lambda p, t: (t, 0)),
            row_spec,
            row_spec,
            wide_spec,
            wide_spec,
            glob_spec,
            glob_spec,
        ],
        out_specs=[row_spec, row_spec, wide_spec, wide_spec, glob_spec, glob_spec],
        out_shape=[
            jax.ShapeDtypeStruct((rows, D), f32),
            jax.ShapeDtypeStruct((rows, D), f32),
            jax.ShapeDtypeStruct((wide_rows, D), f32),
            jax.ShapeDtypeStruct((wide_rows, D), f32),
            jax.ShapeDtypeStruct((slots, D), f32),
            jax.ShapeDtypeStruct((slots, D), f32),
        ],
        compiler_params=pltpu.CompilerParams(dimension_semantics=("arbitrary", "arbitrary")),
        interpret=interpret,
    )(mask, gmask, keep, queries, d_out, key_wide, value_wide, key_glob, value_glob)


def local(queries, keys, values, d_out, glob_pos, block_len):
    scale = HEAD_DIM ** (-0.5)
    rows = queries.shape[0]
    reach_rows = REACH * BLOCK
    tile_rows = TILE_BLOCKS * BLOCK
    tiles = rows // tile_rows
    win_rows = tile_rows + 2 * reach_rows
    wide_rows = rows + 2 * reach_rows
    first_row = lax.axis_index("seq") * rows
    lens_wide = jnp.pad(block_len, 2 * REACH)

    places = first_row + jnp.arange(rows, dtype=jnp.int32)
    marked_rows = jnp.any(glob_pos[:, None] == places[None, :], axis=0)
    local_pos = glob_pos - first_row
    is_local = (local_pos >= 0) & (local_pos < rows)
    local_index = jnp.where(is_local, local_pos, rows)
    inside_rows, _ = key_flags(first_row, rows, glob_pos, lens_wide)

    count = lax.axis_size("seq")
    own_blocks = rows // BLOCK
    slots = own_blocks * count
    glob_block = glob_pos // BLOCK
    slot_valid = jnp.zeros((slots,), bool).at[glob_block].set(True, mode="drop")
    own_slot = lax.axis_index("seq") * own_blocks + jnp.arange(own_blocks, dtype=jnp.int32)
    own_match = glob_block[None, :] == own_slot[:, None]
    own_has = jnp.any(own_match, axis=1)
    own_pos = jnp.sum(jnp.where(own_match, glob_pos[None, :], 0), axis=1) - first_row
    own_index = jnp.where(own_has, own_pos, rows)

    stacked = jnp.stack([queries, keys, values, d_out])
    picked = jnp.take(stacked, jnp.clip(own_pos, 0, rows - 1), axis=1)
    picked = jnp.where(own_has[None, :, None], picked, jnp.zeros_like(picked))
    shared = jnp.transpose(lax.all_gather(picked, "seq"), (1, 0, 2, 3)).reshape(4, slots, D)
    qg = to_heads(shared[0])
    kg = to_heads(shared[1])
    vg = to_heads(shared[2])
    dog = to_heads(shared[3])

    pair = jnp.stack([keys, values])
    from_left, from_right = halo(pair, reach_rows)
    pair_wide = jnp.concatenate([from_left, pair, from_right], axis=1)
    k_h = to_heads(keys)
    v_h = to_heads(values)

    inside_wide, marked_wide = key_flags(first_row - reach_rows, wide_rows, glob_pos, lens_wide)
    allowed_wide = inside_wide & jnp.logical_not(marked_wide)

    allowed_t = jnp.stack(
        [lax.slice_in_dim(allowed_wide, t * tile_rows, t * tile_rows + win_rows) for t in range(tiles)]
    )
    q_block = (jnp.arange(rows, dtype=jnp.int32) // BLOCK).reshape(tiles, tile_rows)
    k_block = jnp.stack(
        [t * TILE_BLOCKS + jnp.arange(win_rows, dtype=jnp.int32) // BLOCK - REACH for t in range(tiles)]
    )
    near = jnp.abs(q_block[:, :, None] - k_block[:, None, :]) <= REACH
    band_mask = near & allowed_t[:, None, :]
    band_out, band_dq, dk_wide, dv_wide, dk_glob, dv_glob = band_call(
        jnp.where(band_mask, 0.0, neg_large).astype(jnp.float32),
        jnp.where(slot_valid, 0.0, neg_large).astype(jnp.float32)[None, :],
        jnp.logical_not(marked_rows).astype(jnp.float32)[:, None],
        queries,
        d_out,
        pair_wide[0],
        pair_wide[1],
        shared[1],
        shared[2],
    )

    g_score = mixed("hge,hre->hgr", qg, k_h) * scale
    g_score = jnp.where(inside_rows[None, None, :], g_score, neg_large)
    g_top = jnp.max(g_score, axis=-1)
    g_sum = jnp.sum(jnp.exp(g_score - g_top[..., None]), axis=-1)
    stats = gather_small(jnp.stack([g_top, g_sum]))
    all_top = stats[:, 0]
    top_glob = jnp.max(all_top, axis=0)
    sum_glob = jnp.sum(stats[:, 1] * jnp.exp(all_top - top_glob[None]), axis=0)
    lse_glob = top_glob + jnp.log(sum_glob)
    g_prob = jnp.where(slot_valid[None, :, None], jnp.exp(g_score - lse_glob[..., None]), 0.0)
    g_weight = g_prob.astype(jnp.bfloat16)
    out_own = reduce_own(from_heads(mixed("hgr,hre->hge", g_weight, v_h)))
    out_own16 = out_own.astype(jnp.bfloat16)
    delta_own = jnp.sum(
        by_head(picked[3]).astype(jnp.float32) * by_head(out_own16).astype(jnp.float32), axis=-1
    )
    delta_g = jnp.transpose(gather_small(delta_own).reshape(slots, HEADS))
    band_out16 = band_out.astype(jnp.bfloat16)
    out_full = band_out16.at[own_index].set(out_own16, mode="drop")

    grad_wide = jnp.stack([dk_wide, dv_wide])
    rims = jnp.concatenate(
        [grad_wide[:, :reach_rows], grad_wide[:, wide_rows - reach_rows :]], axis=1
    )
    back_left, back_right = halo(rims, reach_rows)
    center = grad_wide[:, reach_rows : reach_rows + rows]
    center = center.at[:, :reach_rows].add(back_left).at[:, rows - reach_rows :].add(back_right)

    g_dprob = mixed("hge,hre->hgr", dog, v_h)
    g_dscore = (g_prob * (g_dprob - delta_g[..., None])).astype(jnp.bfloat16)
    row_dq = mixed("hgr,hre->hge", g_dscore, k_h) * scale
    part_dk = mixed("hgr,hge->hre", g_dscore, qg) * scale
    part_dv = mixed("hgr,hge->hre", g_weight, dog)

    totals = reduce_own(
        jnp.concatenate([from_heads(row_dq), dk_glob, dv_glob], axis=1)
    )
    d_queries = band_dq.at[own_index].add(totals[:, :D], mode="drop")
    d_keys = (center[0] + from_heads(part_dk)).at[own_index].add(totals[:, D : 2 * D], mode="drop")
    d_values = (center[1] + from_heads(part_dv)).at[own_index].add(totals[:, 2 * D :], mode="drop")
    return (
        out_full,
        d_queries.astype(jnp.bfloat16),
        d_keys.astype(jnp.bfloat16),
        d_values.astype(jnp.bfloat16),
    )


def solution(mesh):
    rows = P(("groups", "seq"), None)
    return jax.shard_map(
        local,
        mesh=mesh,
        in_specs=(rows, rows, rows, rows, P("groups"), P("groups")),
        out_specs=(rows, rows, rows, rows),
        check_vma=False,
    )
```

```python
import jax
import jax.numpy as jnp
from jax import lax
from jax.sharding import PartitionSpec as P
from jax.experimental import pallas as pl
from jax.experimental.pallas import tpu as pltpu

D = 768
HEADS = 12
BLOCK = 64
REACH = 3
GLOBALS = 128
HEAD_DIM = 64
TILE_BLOCKS = 2

neg_large = -1e30


def mixed(form, left, right):
    return jnp.einsum(form, left, right, preferred_element_type=jnp.float32)


def to_heads(array):
    rows = array.shape[0]
    return jnp.transpose(array.reshape(rows, HEADS, HEAD_DIM), (1, 0, 2))


def from_heads(array):
    rows = array.shape[1]
    return jnp.transpose(array, (1, 0, 2)).reshape(rows, D)


def halo(cells, width):
    count = lax.axis_size("seq")
    ends = count - 1
    head = lax.slice_in_dim(cells, 0, width, axis=1)
    tail = lax.slice_in_dim(cells, cells.shape[1] - width, cells.shape[1], axis=1)
    from_left = lax.ppermute(tail, "seq", [(i, i + 1) for i in range(ends)])
    from_right = lax.ppermute(head, "seq", [(i + 1, i) for i in range(ends)])
    return from_left, from_right


def by_head(array):
    return array.reshape(array.shape[:-1] + (HEADS, HEAD_DIM))


def gather_small(part):
    count = lax.axis_size("seq")
    spread = jnp.broadcast_to(part[None], (count,) + part.shape)
    return lax.all_to_all(spread, "seq", 0, 0)


def reduce_own(full):
    count = lax.axis_size("seq")
    split = full.reshape((count, full.shape[0] // count) + full.shape[1:])
    return jnp.sum(lax.all_to_all(split, "seq", 0, 0), axis=0)


def key_flags(first_pos, span_len, glob_pos, lens_wide):
    places = first_pos + jnp.arange(span_len, dtype=jnp.int32)
    begin = jnp.asarray(first_pos // BLOCK + 2 * REACH, dtype=jnp.int32)
    lens = lax.dynamic_slice_in_dim(lens_wide, begin, span_len // BLOCK)
    inside = (jnp.arange(BLOCK, dtype=jnp.int32)[None, :] < lens[:, None]).reshape(span_len)
    marked = jnp.any(glob_pos[:, None] == places[None, :], axis=0)
    return (inside, marked)


def band_kernel(mask_ref, gmask_ref, keep_ref, q_ref, do_ref, kw_ref, vw_ref, kg_ref, vg_ref,
                out_ref, dq_ref, dkw_ref, dvw_ref, dkg_ref, dvg_ref):
    scale = HEAD_DIM ** (-0.5)
    tile = pl.program_id(1)
    tile_rows = q_ref.shape[0]
    win_rows = mask_ref.shape[2]
    start = pl.multiple_of(tile * tile_rows, tile_rows)
    f32 = jnp.float32
    bf16 = jnp.bfloat16
    nt = (((1,), (1,)), ((), ()))
    tn = (((0,), (0,)), ((), ()))

    @pl.when(tile == 0)
    def _():
        dkw_ref[...] = jnp.zeros_like(dkw_ref)
        dvw_ref[...] = jnp.zeros_like(dvw_ref)
        dkg_ref[...] = jnp.zeros_like(dkg_ref)
        dvg_ref[...] = jnp.zeros_like(dvg_ref)

    band_bias = mask_ref[0]
    glob_bias = gmask_ref[...]
    keep = keep_ref[...].astype(bf16)
    for head in range(q_ref.shape[1] // HEAD_DIM):
        lanes = slice(head * HEAD_DIM, (head + 1) * HEAD_DIM)
        q = q_ref[:, lanes] * jnp.asarray(scale, bf16)
        do = do_ref[:, lanes] * keep
        kwin = kw_ref[pl.ds(start, win_rows), lanes]
        vwin = vw_ref[pl.ds(start, win_rows), lanes]
        kg = kg_ref[:, lanes]
        vg = vg_ref[:, lanes]
        s_b = lax.dot_general(q, kwin, nt, preferred_element_type=f32) + band_bias
        s_g = lax.dot_general(q, kg, nt, preferred_element_type=f32) + glob_bias
        top = jnp.maximum(jnp.max(s_b, axis=1, keepdims=True), jnp.max(s_g, axis=1, keepdims=True))
        e_b = jnp.exp(s_b - top)
        e_g = jnp.exp(s_g - top)
        inv = 1.0 / (jnp.sum(e_b, axis=1, keepdims=True) + jnp.sum(e_g, axis=1, keepdims=True))
        p_b = e_b * inv
        p_g = e_g * inv
        w_b = p_b.astype(bf16)
        w_g = p_g.astype(bf16)
        out = jnp.dot(w_b, vwin, preferred_element_type=f32) + jnp.dot(
            w_g, vg, preferred_element_type=f32
        )
        out_ref[:, lanes] = out
        delta = jnp.sum(
            do.astype(f32) * out.astype(bf16).astype(f32), axis=1, keepdims=True
        )
        dp_b = lax.dot_general(do, vwin, nt, preferred_element_type=f32)
        dp_g = lax.dot_general(do, vg, nt, preferred_element_type=f32)
        ds_b = (p_b * (dp_b - delta)).astype(bf16)
        ds_g = (p_g * (dp_g - delta)).astype(bf16)
        dq = jnp.dot(ds_b, kwin, preferred_element_type=f32) + jnp.dot(
            ds_g, kg, preferred_element_type=f32
        )
        dq_ref[:, lanes] = dq * scale
        dkw_ref[pl.ds(start, win_rows), lanes] += lax.dot_general(ds_b, q, tn, preferred_element_type=f32)
        dvw_ref[pl.ds(start, win_rows), lanes] += lax.dot_general(w_b, do, tn, preferred_element_type=f32)
        dkg_ref[:, lanes] += lax.dot_general(ds_g, q, tn, preferred_element_type=f32)
        dvg_ref[:, lanes] += lax.dot_general(w_g, do, tn, preferred_element_type=f32)


def band_call(mask, gmask, keep, queries, d_out, key_wide, value_wide, key_glob, value_glob, interpret=False):
    rows = queries.shape[0]
    wide_rows = key_wide.shape[0]
    slots = key_glob.shape[0]
    tiles, tile_rows, win_rows = mask.shape
    lanes = 2 * HEAD_DIM
    pairs = D // lanes
    f32 = jnp.float32
    row_spec = pl.BlockSpec((tile_rows, lanes), lambda p, t: (t, p))
    wide_spec = pl.BlockSpec((wide_rows, lanes), lambda p, t: (0, p))
    glob_spec = pl.BlockSpec((slots, lanes), lambda p, t: (0, p))
    return pl.pallas_call(
        band_kernel,
        grid=(pairs, tiles),
        in_specs=[
            pl.BlockSpec((1, tile_rows, win_rows), lambda p, t: (t, 0, 0)),
            pl.BlockSpec((1, slots), lambda p, t: (0, 0)),
            pl.BlockSpec((tile_rows, 1), lambda p, t: (t, 0)),
            row_spec,
            row_spec,
            wide_spec,
            wide_spec,
            glob_spec,
            glob_spec,
        ],
        out_specs=[row_spec, row_spec, wide_spec, wide_spec, glob_spec, glob_spec],
        out_shape=[
            jax.ShapeDtypeStruct((rows, D), f32),
            jax.ShapeDtypeStruct((rows, D), f32),
            jax.ShapeDtypeStruct((wide_rows, D), f32),
            jax.ShapeDtypeStruct((wide_rows, D), f32),
            jax.ShapeDtypeStruct((slots, D), f32),
            jax.ShapeDtypeStruct((slots, D), f32),
        ],
        compiler_params=pltpu.CompilerParams(dimension_semantics=("arbitrary", "arbitrary")),
        interpret=interpret,
    )(mask, gmask, keep, queries, d_out, key_wide, value_wide, key_glob, value_glob)


def local(queries, keys, values, d_out, glob_pos, block_len):
    scale = HEAD_DIM ** (-0.5)
    rows = queries.shape[0]
    reach_rows = REACH * BLOCK
    tile_rows = TILE_BLOCKS * BLOCK
    tiles = rows // tile_rows
    win_rows = tile_rows + 2 * reach_rows
    wide_rows = rows + 2 * reach_rows
    first_row = lax.axis_index("seq") * rows
    lens_wide = jnp.pad(block_len, 2 * REACH)

    places = first_row + jnp.arange(rows, dtype=jnp.int32)
    marked_rows = jnp.any(glob_pos[:, None] == places[None, :], axis=0)
    local_pos = glob_pos - first_row
    is_local = (local_pos >= 0) & (local_pos < rows)
    local_index = jnp.where(is_local, local_pos, rows)
    inside_rows, _ = key_flags(first_row, rows, glob_pos, lens_wide)

    count = lax.axis_size("seq")
    own_blocks = rows // BLOCK
    slots = own_blocks * count
    glob_block = glob_pos // BLOCK
    slot_valid = jnp.zeros((slots,), bool).at[glob_block].set(True, mode="drop")
    own_slot = lax.axis_index("seq") * own_blocks + jnp.arange(own_blocks, dtype=jnp.int32)
    own_match = glob_block[None, :] == own_slot[:, None]
    own_has = jnp.any(own_match, axis=1)
    own_pos = jnp.sum(jnp.where(own_match, glob_pos[None, :], 0), axis=1) - first_row
    own_offset = own_pos - BLOCK * jnp.arange(own_blocks, dtype=jnp.int32)
    own_row = own_has[:, None] & (jnp.arange(BLOCK, dtype=jnp.int32)[None, :] == own_offset[:, None])

    def place(base, extra):
        shaped = base.reshape(own_blocks, BLOCK, D)
        return jnp.where(own_row[:, :, None], shaped + extra[:, None, :], shaped).reshape(rows, D)

    stacked = jnp.stack([queries, keys, values, d_out])
    picked = jnp.take(stacked, jnp.clip(own_pos, 0, rows - 1), axis=1)
    picked = jnp.where(own_has[None, :, None], picked, jnp.zeros_like(picked))
    shared = jnp.transpose(lax.all_gather(picked, "seq"), (1, 0, 2, 3)).reshape(4, slots, D)
    qg = to_heads(shared[0])
    kg = to_heads(shared[1])
    vg = to_heads(shared[2])
    dog = to_heads(shared[3])

    pair = jnp.stack([keys, values])
    from_left, from_right = halo(pair, reach_rows)
    pair_wide = jnp.concatenate([from_left, pair, from_right], axis=1)
    k_h = to_heads(keys)
    v_h = to_heads(values)

    inside_wide, marked_wide = key_flags(first_row - reach_rows, wide_rows, glob_pos, lens_wide)
    allowed_wide = inside_wide & jnp.logical_not(marked_wide)

    allowed_t = jnp.stack(
        [lax.slice_in_dim(allowed_wide, t * tile_rows, t * tile_rows + win_rows) for t in range(tiles)]
    )
    q_block = (jnp.arange(rows, dtype=jnp.int32) // BLOCK).reshape(tiles, tile_rows)
    k_block = jnp.stack(
        [t * TILE_BLOCKS + jnp.arange(win_rows, dtype=jnp.int32) // BLOCK - REACH for t in range(tiles)]
    )
    near = jnp.abs(q_block[:, :, None] - k_block[:, None, :]) <= REACH
    band_mask = near & allowed_t[:, None, :]
    band_out, band_dq, dk_wide, dv_wide, dk_glob, dv_glob = band_call(
        jnp.where(band_mask, 0.0, neg_large).astype(jnp.float32),
        jnp.where(slot_valid, 0.0, neg_large).astype(jnp.float32)[None, :],
        jnp.logical_not(marked_rows).astype(jnp.float32)[:, None],
        queries,
        d_out,
        pair_wide[0],
        pair_wide[1],
        shared[1],
        shared[2],
    )

    g_score = mixed("hge,hre->hgr", qg, k_h) * scale
    g_score = jnp.where(inside_rows[None, None, :], g_score, neg_large)
    g_top = jnp.max(g_score, axis=-1)
    g_sum = jnp.sum(jnp.exp(g_score - g_top[..., None]), axis=-1)
    stats = gather_small(jnp.stack([g_top, g_sum]))
    all_top = stats[:, 0]
    top_glob = jnp.max(all_top, axis=0)
    sum_glob = jnp.sum(stats[:, 1] * jnp.exp(all_top - top_glob[None]), axis=0)
    lse_glob = top_glob + jnp.log(sum_glob)
    g_prob = jnp.where(slot_valid[None, :, None], jnp.exp(g_score - lse_glob[..., None]), 0.0)
    g_weight = g_prob.astype(jnp.bfloat16)
    out_own = reduce_own(from_heads(mixed("hgr,hre->hge", g_weight, v_h)))
    out_own16 = out_own.astype(jnp.bfloat16)
    delta_own = jnp.sum(
        by_head(picked[3]).astype(jnp.float32) * by_head(out_own16).astype(jnp.float32), axis=-1
    )
    delta_g = jnp.transpose(gather_small(delta_own).reshape(slots, HEADS))
    band_out16 = band_out.astype(jnp.bfloat16)
    out_full = jnp.where(
        own_row[:, :, None], out_own16[:, None, :], band_out16.reshape(own_blocks, BLOCK, D)
    ).reshape(rows, D)

    grad_wide = jnp.stack([dk_wide, dv_wide])
    rims = jnp.concatenate(
        [grad_wide[:, :reach_rows], grad_wide[:, wide_rows - reach_rows :]], axis=1
    )
    back_left, back_right = halo(rims, reach_rows)
    center = grad_wide[:, reach_rows : reach_rows + rows]
    center = center.at[:, :reach_rows].add(back_left).at[:, rows - reach_rows :].add(back_right)

    g_dprob = mixed("hge,hre->hgr", dog, v_h)
    g_dscore = (g_prob * (g_dprob - delta_g[..., None])).astype(jnp.bfloat16)
    row_dq = mixed("hgr,hre->hge", g_dscore, k_h) * scale
    part_dk = mixed("hgr,hge->hre", g_dscore, qg) * scale
    part_dv = mixed("hgr,hge->hre", g_weight, dog)

    totals = reduce_own(
        jnp.concatenate([from_heads(row_dq), dk_glob, dv_glob], axis=1)
    )
    d_queries = place(band_dq, totals[:, :D])
    d_keys = place(center[0] + from_heads(part_dk), totals[:, D : 2 * D])
    d_values = place(center[1] + from_heads(part_dv), totals[:, 2 * D :])
    return (
        out_full,
        d_queries.astype(jnp.bfloat16),
        d_keys.astype(jnp.bfloat16),
        d_values.astype(jnp.bfloat16),
    )


def solution(mesh):
    rows = P(("groups", "seq"), None)
    return jax.shard_map(
        local,
        mesh=mesh,
        in_specs=(rows, rows, rows, rows, P("groups"), P("groups")),
        out_specs=(rows, rows, rows, rows),
        check_vma=False,
    )
```

```python
import jax
import jax.numpy as jnp
from jax import lax
from jax.sharding import PartitionSpec as P
from jax.experimental import pallas as pl
from jax.experimental.pallas import tpu as pltpu

D = 768
HEADS = 12
BLOCK = 64
REACH = 3
GLOBALS = 128
HEAD_DIM = 64
TILE_BLOCKS = 2

neg_large = -1e30


def mixed(form, left, right):
    return jnp.einsum(form, left, right, preferred_element_type=jnp.float32)


def to_heads(array):
    rows = array.shape[0]
    return jnp.transpose(array.reshape(rows, HEADS, HEAD_DIM), (1, 0, 2))


def from_heads(array):
    rows = array.shape[1]
    return jnp.transpose(array, (1, 0, 2)).reshape(rows, D)


def halo(cells, width):
    count = lax.axis_size("seq")
    ends = count - 1
    head = lax.slice_in_dim(cells, 0, width, axis=1)
    tail = lax.slice_in_dim(cells, cells.shape[1] - width, cells.shape[1], axis=1)
    from_left = lax.ppermute(tail, "seq", [(i, i + 1) for i in range(ends)])
    from_right = lax.ppermute(head, "seq", [(i + 1, i) for i in range(ends)])
    return from_left, from_right


def by_head(array):
    return array.reshape(array.shape[:-1] + (HEADS, HEAD_DIM))


def gather_small(part):
    count = lax.axis_size("seq")
    spread = jnp.broadcast_to(part[None], (count,) + part.shape)
    return lax.all_to_all(spread, "seq", 0, 0)


def reduce_own(full):
    count = lax.axis_size("seq")
    split = full.reshape((count, full.shape[0] // count) + full.shape[1:])
    return jnp.sum(lax.all_to_all(split, "seq", 0, 0), axis=0)


def key_flags(first_pos, span_len, glob_pos, lens_wide):
    places = first_pos + jnp.arange(span_len, dtype=jnp.int32)
    begin = jnp.asarray(first_pos // BLOCK + 2 * REACH, dtype=jnp.int32)
    lens = lax.dynamic_slice_in_dim(lens_wide, begin, span_len // BLOCK)
    inside = (jnp.arange(BLOCK, dtype=jnp.int32)[None, :] < lens[:, None]).reshape(span_len)
    marked = jnp.any(glob_pos[:, None] == places[None, :], axis=0)
    return (inside, marked)


def band_kernel(mask_ref, gmask_ref, keep_ref, q_ref, do_ref, kw_ref, vw_ref, kg_ref, vg_ref,
                out_ref, dq_ref, dkw_ref, dvw_ref, dkg_ref, dvg_ref):
    scale = HEAD_DIM ** (-0.5)
    tile = pl.program_id(1)
    tile_rows = q_ref.shape[0]
    win_rows = mask_ref.shape[2]
    start = pl.multiple_of(tile * tile_rows, tile_rows)
    f32 = jnp.float32
    bf16 = jnp.bfloat16
    nt = (((1,), (1,)), ((), ()))
    tn = (((0,), (0,)), ((), ()))

    @pl.when(tile == 0)
    def _():
        dkw_ref[...] = jnp.zeros_like(dkw_ref)
        dvw_ref[...] = jnp.zeros_like(dvw_ref)
        dkg_ref[...] = jnp.zeros_like(dkg_ref)
        dvg_ref[...] = jnp.zeros_like(dvg_ref)

    band_bias = mask_ref[0]
    glob_bias = gmask_ref[...]
    keep = keep_ref[...].astype(bf16)
    for head in range(q_ref.shape[1] // HEAD_DIM):
        lanes = slice(head * HEAD_DIM, (head + 1) * HEAD_DIM)
        q = q_ref[:, lanes] * jnp.asarray(scale, bf16)
        do = do_ref[:, lanes] * keep
        kwin = kw_ref[pl.ds(start, win_rows), lanes]
        vwin = vw_ref[pl.ds(start, win_rows), lanes]
        kg = kg_ref[:, lanes]
        vg = vg_ref[:, lanes]
        s_b = lax.dot_general(q, kwin, nt, preferred_element_type=f32) + band_bias
        s_g = lax.dot_general(q, kg, nt, preferred_element_type=f32) + glob_bias
        top = jnp.maximum(jnp.max(s_b, axis=1, keepdims=True), jnp.max(s_g, axis=1, keepdims=True))
        e_b = jnp.exp(s_b - top)
        e_g = jnp.exp(s_g - top)
        inv = 1.0 / (jnp.sum(e_b, axis=1, keepdims=True) + jnp.sum(e_g, axis=1, keepdims=True))
        p_b = e_b * inv
        p_g = e_g * inv
        w_b = p_b.astype(bf16)
        w_g = p_g.astype(bf16)
        out = jnp.dot(w_b, vwin, preferred_element_type=f32) + jnp.dot(
            w_g, vg, preferred_element_type=f32
        )
        out_ref[:, lanes] = out
        delta = jnp.sum(
            do.astype(f32) * out.astype(bf16).astype(f32), axis=1, keepdims=True
        )
        dp_b = lax.dot_general(do, vwin, nt, preferred_element_type=f32)
        dp_g = lax.dot_general(do, vg, nt, preferred_element_type=f32)
        ds_b = (p_b * (dp_b - delta)).astype(bf16)
        ds_g = (p_g * (dp_g - delta)).astype(bf16)
        dq = jnp.dot(ds_b, kwin, preferred_element_type=f32) + jnp.dot(
            ds_g, kg, preferred_element_type=f32
        )
        dq_ref[:, lanes] = dq * scale
        dkw_ref[pl.ds(start, win_rows), lanes] += lax.dot_general(ds_b, q, tn, preferred_element_type=f32)
        dvw_ref[pl.ds(start, win_rows), lanes] += lax.dot_general(w_b, do, tn, preferred_element_type=f32)
        dkg_ref[:, lanes] += lax.dot_general(ds_g, q, tn, preferred_element_type=f32)
        dvg_ref[:, lanes] += lax.dot_general(w_g, do, tn, preferred_element_type=f32)


def band_call(mask, gmask, keep, queries, d_out, key_wide, value_wide, key_glob, value_glob, interpret=False):
    rows = queries.shape[0]
    wide_rows = key_wide.shape[0]
    slots = key_glob.shape[0]
    tiles, tile_rows, win_rows = mask.shape
    lanes = 2 * HEAD_DIM
    pairs = D // lanes
    f32 = jnp.float32
    row_spec = pl.BlockSpec((tile_rows, lanes), lambda p, t: (t, p))
    wide_spec = pl.BlockSpec((wide_rows, lanes), lambda p, t: (0, p))
    glob_spec = pl.BlockSpec((slots, lanes), lambda p, t: (0, p))
    return pl.pallas_call(
        band_kernel,
        grid=(pairs, tiles),
        in_specs=[
            pl.BlockSpec((1, tile_rows, win_rows), lambda p, t: (t, 0, 0)),
            pl.BlockSpec((1, slots), lambda p, t: (0, 0)),
            pl.BlockSpec((tile_rows, 1), lambda p, t: (t, 0)),
            row_spec,
            row_spec,
            wide_spec,
            wide_spec,
            glob_spec,
            glob_spec,
        ],
        out_specs=[row_spec, row_spec, wide_spec, wide_spec, glob_spec, glob_spec],
        out_shape=[
            jax.ShapeDtypeStruct((rows, D), f32),
            jax.ShapeDtypeStruct((rows, D), f32),
            jax.ShapeDtypeStruct((wide_rows, D), f32),
            jax.ShapeDtypeStruct((wide_rows, D), f32),
            jax.ShapeDtypeStruct((slots, D), f32),
            jax.ShapeDtypeStruct((slots, D), f32),
        ],
        compiler_params=pltpu.CompilerParams(dimension_semantics=("arbitrary", "arbitrary")),
        interpret=interpret,
    )(mask, gmask, keep, queries, d_out, key_wide, value_wide, key_glob, value_glob)


def local(queries, keys, values, d_out, glob_pos, block_len):
    scale = HEAD_DIM ** (-0.5)
    rows = queries.shape[0]
    reach_rows = REACH * BLOCK
    tile_rows = TILE_BLOCKS * BLOCK
    tiles = rows // tile_rows
    win_rows = tile_rows + 2 * reach_rows
    wide_rows = rows + 2 * reach_rows
    first_row = lax.axis_index("seq") * rows
    lens_wide = jnp.pad(block_len, 2 * REACH)

    places = first_row + jnp.arange(rows, dtype=jnp.int32)
    marked_rows = jnp.any(glob_pos[:, None] == places[None, :], axis=0)
    local_pos = glob_pos - first_row
    is_local = (local_pos >= 0) & (local_pos < rows)
    local_index = jnp.where(is_local, local_pos, rows)
    inside_rows, _ = key_flags(first_row, rows, glob_pos, lens_wide)

    count = lax.axis_size("seq")
    own_blocks = rows // BLOCK
    slots = own_blocks * count
    glob_block = glob_pos // BLOCK
    slot_valid = jnp.zeros((slots,), bool).at[glob_block].set(True, mode="drop")
    own_slot = lax.axis_index("seq") * own_blocks + jnp.arange(own_blocks, dtype=jnp.int32)
    own_match = glob_block[None, :] == own_slot[:, None]
    own_has = jnp.any(own_match, axis=1)
    own_pos = jnp.sum(jnp.where(own_match, glob_pos[None, :], 0), axis=1) - first_row
    own_offset = own_pos - BLOCK * jnp.arange(own_blocks, dtype=jnp.int32)
    own_row = own_has[:, None] & (jnp.arange(BLOCK, dtype=jnp.int32)[None, :] == own_offset[:, None])

    def place(base, extra):
        shaped = base.reshape(own_blocks, BLOCK, D)
        return jnp.where(own_row[:, :, None], shaped + extra[:, None, :], shaped).reshape(rows, D)

    own_pick = (
        own_has[:, None] & (jnp.arange(rows, dtype=jnp.int32)[None, :] == own_pos[:, None])
    ).astype(jnp.bfloat16)
    picked = jnp.stack(
        [
            jnp.dot(own_pick, source, preferred_element_type=jnp.float32).astype(jnp.bfloat16)
            for source in (queries, keys, values, d_out)
        ]
    )
    shared = jnp.transpose(lax.all_gather(picked, "seq"), (1, 0, 2, 3)).reshape(4, slots, D)
    qg = to_heads(shared[0])
    kg = to_heads(shared[1])
    vg = to_heads(shared[2])
    dog = to_heads(shared[3])

    pair = jnp.stack([keys, values])
    from_left, from_right = halo(pair, reach_rows)
    pair_wide = jnp.concatenate([from_left, pair, from_right], axis=1)
    k_h = to_heads(keys)
    v_h = to_heads(values)

    inside_wide, marked_wide = key_flags(first_row - reach_rows, wide_rows, glob_pos, lens_wide)
    allowed_wide = inside_wide & jnp.logical_not(marked_wide)

    allowed_t = jnp.stack(
        [lax.slice_in_dim(allowed_wide, t * tile_rows, t * tile_rows + win_rows) for t in range(tiles)]
    )
    q_block = (jnp.arange(rows, dtype=jnp.int32) // BLOCK).reshape(tiles, tile_rows)
    k_block = jnp.stack(
        [t * TILE_BLOCKS + jnp.arange(win_rows, dtype=jnp.int32) // BLOCK - REACH for t in range(tiles)]
    )
    near = jnp.abs(q_block[:, :, None] - k_block[:, None, :]) <= REACH
    band_mask = near & allowed_t[:, None, :]
    band_out, band_dq, dk_wide, dv_wide, dk_glob, dv_glob = band_call(
        jnp.where(band_mask, 0.0, neg_large).astype(jnp.float32),
        jnp.where(slot_valid, 0.0, neg_large).astype(jnp.float32)[None, :],
        jnp.logical_not(marked_rows).astype(jnp.float32)[:, None],
        queries,
        d_out,
        pair_wide[0],
        pair_wide[1],
        shared[1],
        shared[2],
    )

    g_score = mixed("hge,hre->hgr", qg, k_h) * scale
    g_score = jnp.where(inside_rows[None, None, :], g_score, neg_large)
    g_top = jnp.max(g_score, axis=-1)
    g_exp = jnp.exp(g_score - g_top[..., None])
    g_sum = jnp.sum(g_exp, axis=-1)
    g_acc = mixed("hgr,hre->hge", g_exp.astype(jnp.bfloat16), v_h)
    packed = jnp.concatenate([g_acc, g_top[..., None], g_sum[..., None]], axis=-1)
    packed = jnp.transpose(packed, (1, 0, 2)).reshape(count, own_blocks, HEADS, HEAD_DIM + 2)
    parts = lax.all_to_all(packed, "seq", 0, 0)
    part_top = parts[..., HEAD_DIM]
    own_top = jnp.max(part_top, axis=0)
    rescale = jnp.exp(part_top - own_top[None])
    own_sum = jnp.sum(parts[..., HEAD_DIM + 1] * rescale, axis=0)
    own_acc = jnp.sum(parts[..., :HEAD_DIM] * rescale[..., None], axis=0)
    out_own16 = (own_acc / own_sum[..., None]).reshape(own_blocks, D).astype(jnp.bfloat16)
    own_lse = own_top + jnp.log(own_sum)
    delta_own = jnp.sum(
        by_head(picked[3]).astype(jnp.float32) * by_head(out_own16).astype(jnp.float32), axis=-1
    )
    glob_stats = gather_small(jnp.stack([own_lse, delta_own], axis=-1)).reshape(slots, HEADS, 2)
    lse_glob = jnp.transpose(glob_stats[..., 0])
    delta_g = jnp.transpose(glob_stats[..., 1])
    g_prob = jnp.where(slot_valid[None, :, None], jnp.exp(g_score - lse_glob[..., None]), 0.0)
    g_weight = g_prob.astype(jnp.bfloat16)
    band_out16 = band_out.astype(jnp.bfloat16)
    out_full = jnp.where(
        own_row[:, :, None], out_own16[:, None, :], band_out16.reshape(own_blocks, BLOCK, D)
    ).reshape(rows, D)

    grad_wide = jnp.stack([dk_wide, dv_wide])
    rims = jnp.concatenate(
        [grad_wide[:, :reach_rows], grad_wide[:, wide_rows - reach_rows :]], axis=1
    )
    back_left, back_right = halo(rims, reach_rows)
    center = grad_wide[:, reach_rows : reach_rows + rows]
    center = center.at[:, :reach_rows].add(back_left).at[:, rows - reach_rows :].add(back_right)

    g_dprob = mixed("hge,hre->hgr", dog, v_h)
    g_dscore = (g_prob * (g_dprob - delta_g[..., None])).astype(jnp.bfloat16)
    row_dq = mixed("hgr,hre->hge", g_dscore, k_h) * scale
    part_dk = mixed("hgr,hge->hre", g_dscore, qg) * scale
    part_dv = mixed("hgr,hge->hre", g_weight, dog)

    totals = reduce_own(
        jnp.concatenate([from_heads(row_dq), dk_glob, dv_glob], axis=1)
    )
    d_queries = place(band_dq, totals[:, :D])
    d_keys = place(center[0] + from_heads(part_dk), totals[:, D : 2 * D])
    d_values = place(center[1] + from_heads(part_dv), totals[:, 2 * D :])
    return (
        out_full,
        d_queries.astype(jnp.bfloat16),
        d_keys.astype(jnp.bfloat16),
        d_values.astype(jnp.bfloat16),
    )


def solution(mesh):
    rows = P(("groups", "seq"), None)
    return jax.shard_map(
        local,
        mesh=mesh,
        in_specs=(rows, rows, rows, rows, P("groups"), P("groups")),
        out_specs=(rows, rows, rows, rows),
        check_vma=False,
    )
```

```python
import jax
import jax.numpy as jnp
from jax import lax
from jax.sharding import PartitionSpec as P
from jax.experimental import pallas as pl
from jax.experimental.pallas import tpu as pltpu

D = 768
HEADS = 12
BLOCK = 64
REACH = 3
GLOBALS = 128
HEAD_DIM = 64
TILE_BLOCKS = 2

neg_large = -1e30


def mixed(form, left, right):
    return jnp.einsum(form, left, right, preferred_element_type=jnp.float32)


def to_heads(array):
    rows = array.shape[0]
    return jnp.transpose(array.reshape(rows, HEADS, HEAD_DIM), (1, 0, 2))


def from_heads(array):
    rows = array.shape[1]
    return jnp.transpose(array, (1, 0, 2)).reshape(rows, D)


def halo(cells, width):
    count = lax.axis_size("seq")
    ends = count - 1
    head = lax.slice_in_dim(cells, 0, width, axis=1)
    tail = lax.slice_in_dim(cells, cells.shape[1] - width, cells.shape[1], axis=1)
    from_left = lax.ppermute(tail, "seq", [(i, i + 1) for i in range(ends)])
    from_right = lax.ppermute(head, "seq", [(i + 1, i) for i in range(ends)])
    return from_left, from_right


def by_head(array):
    return array.reshape(array.shape[:-1] + (HEADS, HEAD_DIM))


def gather_small(part):
    count = lax.axis_size("seq")
    spread = jnp.broadcast_to(part[None], (count,) + part.shape)
    return lax.all_to_all(spread, "seq", 0, 0)


def reduce_own(full):
    count = lax.axis_size("seq")
    split = full.reshape((count, full.shape[0] // count) + full.shape[1:])
    return jnp.sum(lax.all_to_all(split, "seq", 0, 0), axis=0)


def key_flags(first_pos, span_len, glob_pos, lens_wide):
    places = first_pos + jnp.arange(span_len, dtype=jnp.int32)
    begin = jnp.asarray(first_pos // BLOCK + 2 * REACH, dtype=jnp.int32)
    lens = lax.dynamic_slice_in_dim(lens_wide, begin, span_len // BLOCK)
    inside = (jnp.arange(BLOCK, dtype=jnp.int32)[None, :] < lens[:, None]).reshape(span_len)
    marked = jnp.any(glob_pos[:, None] == places[None, :], axis=0)
    return (inside, marked)


def band_kernel(mask_ref, gmask_ref, keep_ref, q_ref, do_ref, kw_ref, vw_ref, kg_ref, vg_ref,
                out_ref, dq_ref, dkw_ref, dvw_ref, dkg_ref, dvg_ref):
    scale = HEAD_DIM ** (-0.5)
    tile = pl.program_id(1)
    tile_rows = q_ref.shape[0]
    win_rows = mask_ref.shape[2]
    start = pl.multiple_of(tile * tile_rows, tile_rows)
    f32 = jnp.float32
    bf16 = jnp.bfloat16
    nt = (((1,), (1,)), ((), ()))
    tn = (((0,), (0,)), ((), ()))

    @pl.when(tile == 0)
    def _():
        dkw_ref[...] = jnp.zeros_like(dkw_ref)
        dvw_ref[...] = jnp.zeros_like(dvw_ref)
        dkg_ref[...] = jnp.zeros_like(dkg_ref)
        dvg_ref[...] = jnp.zeros_like(dvg_ref)

    band_bias = mask_ref[0]
    glob_bias = gmask_ref[...]
    keep = keep_ref[...].astype(bf16)
    for head in range(q_ref.shape[1] // HEAD_DIM):
        lanes = slice(head * HEAD_DIM, (head + 1) * HEAD_DIM)
        q = q_ref[:, lanes] * jnp.asarray(scale, bf16)
        do = do_ref[:, lanes] * keep
        kwin = kw_ref[pl.ds(start, win_rows), lanes]
        vwin = vw_ref[pl.ds(start, win_rows), lanes]
        kg = kg_ref[:, lanes]
        vg = vg_ref[:, lanes]
        s_b = lax.dot_general(q, kwin, nt, preferred_element_type=f32) + band_bias
        s_g = lax.dot_general(q, kg, nt, preferred_element_type=f32) + glob_bias
        top = jnp.maximum(jnp.max(s_b, axis=1, keepdims=True), jnp.max(s_g, axis=1, keepdims=True))
        e_b = jnp.exp(s_b - top)
        e_g = jnp.exp(s_g - top)
        inv = 1.0 / (jnp.sum(e_b, axis=1, keepdims=True) + jnp.sum(e_g, axis=1, keepdims=True))
        p_b = e_b * inv
        p_g = e_g * inv
        w_b = p_b.astype(bf16)
        w_g = p_g.astype(bf16)
        out = jnp.dot(w_b, vwin, preferred_element_type=f32) + jnp.dot(
            w_g, vg, preferred_element_type=f32
        )
        out_ref[:, lanes] = out
        delta = jnp.sum(
            do.astype(f32) * out.astype(bf16).astype(f32), axis=1, keepdims=True
        )
        dp_b = lax.dot_general(do, vwin, nt, preferred_element_type=f32)
        dp_g = lax.dot_general(do, vg, nt, preferred_element_type=f32)
        ds_b = (p_b * (dp_b - delta)).astype(bf16)
        ds_g = (p_g * (dp_g - delta)).astype(bf16)
        dq = jnp.dot(ds_b, kwin, preferred_element_type=f32) + jnp.dot(
            ds_g, kg, preferred_element_type=f32
        )
        dq_ref[:, lanes] = dq * scale
        dkw_ref[pl.ds(start, win_rows), lanes] += lax.dot_general(ds_b, q, tn, preferred_element_type=f32)
        dvw_ref[pl.ds(start, win_rows), lanes] += lax.dot_general(w_b, do, tn, preferred_element_type=f32)
        dkg_ref[:, lanes] += lax.dot_general(ds_g, q, tn, preferred_element_type=f32)
        dvg_ref[:, lanes] += lax.dot_general(w_g, do, tn, preferred_element_type=f32)


def band_call(mask, gmask, keep, queries, d_out, key_wide, value_wide, key_glob, value_glob, interpret=False):
    rows = queries.shape[0]
    wide_rows = key_wide.shape[0]
    slots = key_glob.shape[0]
    tiles, tile_rows, win_rows = mask.shape
    lanes = 2 * HEAD_DIM
    pairs = D // lanes
    f32 = jnp.float32
    row_spec = pl.BlockSpec((tile_rows, lanes), lambda p, t: (t, p))
    wide_spec = pl.BlockSpec((wide_rows, lanes), lambda p, t: (0, p))
    glob_spec = pl.BlockSpec((slots, lanes), lambda p, t: (0, p))
    return pl.pallas_call(
        band_kernel,
        grid=(pairs, tiles),
        in_specs=[
            pl.BlockSpec((1, tile_rows, win_rows), lambda p, t: (t, 0, 0)),
            pl.BlockSpec((1, slots), lambda p, t: (0, 0)),
            pl.BlockSpec((tile_rows, 1), lambda p, t: (t, 0)),
            row_spec,
            row_spec,
            wide_spec,
            wide_spec,
            glob_spec,
            glob_spec,
        ],
        out_specs=[row_spec, row_spec, wide_spec, wide_spec, glob_spec, glob_spec],
        out_shape=[
            jax.ShapeDtypeStruct((rows, D), f32),
            jax.ShapeDtypeStruct((rows, D), f32),
            jax.ShapeDtypeStruct((wide_rows, D), f32),
            jax.ShapeDtypeStruct((wide_rows, D), f32),
            jax.ShapeDtypeStruct((slots, D), f32),
            jax.ShapeDtypeStruct((slots, D), f32),
        ],
        compiler_params=pltpu.CompilerParams(dimension_semantics=("arbitrary", "arbitrary")),
        interpret=interpret,
    )(mask, gmask, keep, queries, d_out, key_wide, value_wide, key_glob, value_glob)


def local(queries, keys, values, d_out, glob_pos, block_len):
    scale = HEAD_DIM ** (-0.5)
    rows = queries.shape[0]
    reach_rows = REACH * BLOCK
    tile_rows = TILE_BLOCKS * BLOCK
    tiles = rows // tile_rows
    win_rows = tile_rows + 2 * reach_rows
    wide_rows = rows + 2 * reach_rows
    first_row = lax.axis_index("seq") * rows
    lens_wide = jnp.pad(block_len, 2 * REACH)

    places = first_row + jnp.arange(rows, dtype=jnp.int32)
    marked_rows = jnp.any(glob_pos[:, None] == places[None, :], axis=0)
    local_pos = glob_pos - first_row
    is_local = (local_pos >= 0) & (local_pos < rows)
    local_index = jnp.where(is_local, local_pos, rows)
    inside_rows, _ = key_flags(first_row, rows, glob_pos, lens_wide)

    count = lax.axis_size("seq")
    own_blocks = rows // BLOCK
    slots = own_blocks * count
    glob_block = glob_pos // BLOCK
    slot_valid = jnp.zeros((slots,), bool).at[glob_block].set(True, mode="drop")
    own_slot = lax.axis_index("seq") * own_blocks + jnp.arange(own_blocks, dtype=jnp.int32)
    own_match = glob_block[None, :] == own_slot[:, None]
    own_has = jnp.any(own_match, axis=1)
    own_pos = jnp.sum(jnp.where(own_match, glob_pos[None, :], 0), axis=1) - first_row
    own_offset = own_pos - BLOCK * jnp.arange(own_blocks, dtype=jnp.int32)
    own_row = own_has[:, None] & (jnp.arange(BLOCK, dtype=jnp.int32)[None, :] == own_offset[:, None])

    def place(base, extra):
        shaped = base.reshape(own_blocks, BLOCK, D)
        return jnp.where(own_row[:, :, None], shaped + extra[:, None, :], shaped).reshape(rows, D)

    own_pick = (
        own_has[:, None] & (jnp.arange(rows, dtype=jnp.int32)[None, :] == own_pos[:, None])
    ).astype(jnp.bfloat16)
    picked = jnp.stack(
        [
            jnp.dot(own_pick, source, preferred_element_type=jnp.float32).astype(jnp.bfloat16)
            for source in (queries, keys, values, d_out)
        ]
    )
    shared = jnp.transpose(gather_small(picked), (1, 0, 2, 3)).reshape(4, slots, D)
    qg = to_heads(shared[0])
    kg = to_heads(shared[1])
    vg = to_heads(shared[2])
    dog = to_heads(shared[3])

    pair = jnp.stack([keys, values])
    from_left, from_right = halo(pair, reach_rows)
    pair_wide = jnp.concatenate([from_left, pair, from_right], axis=1)
    k_h = to_heads(keys)
    v_h = to_heads(values)

    inside_wide, marked_wide = key_flags(first_row - reach_rows, wide_rows, glob_pos, lens_wide)
    allowed_wide = inside_wide & jnp.logical_not(marked_wide)

    allowed_t = jnp.stack(
        [lax.slice_in_dim(allowed_wide, t * tile_rows, t * tile_rows + win_rows) for t in range(tiles)]
    )
    q_block = (jnp.arange(rows, dtype=jnp.int32) // BLOCK).reshape(tiles, tile_rows)
    k_block = jnp.stack(
        [t * TILE_BLOCKS + jnp.arange(win_rows, dtype=jnp.int32) // BLOCK - REACH for t in range(tiles)]
    )
    near = jnp.abs(q_block[:, :, None] - k_block[:, None, :]) <= REACH
    band_mask = near & allowed_t[:, None, :]
    band_out, band_dq, dk_wide, dv_wide, dk_glob, dv_glob = band_call(
        jnp.where(band_mask, 0.0, neg_large).astype(jnp.float32),
        jnp.where(slot_valid, 0.0, neg_large).astype(jnp.float32)[None, :],
        jnp.logical_not(marked_rows).astype(jnp.float32)[:, None],
        queries,
        d_out,
        pair_wide[0],
        pair_wide[1],
        shared[1],
        shared[2],
    )

    g_score = mixed("hge,hre->hgr", qg, k_h) * scale
    g_score = jnp.where(inside_rows[None, None, :], g_score, neg_large)
    g_top = jnp.max(g_score, axis=-1)
    g_sum = jnp.sum(jnp.exp(g_score - g_top[..., None]), axis=-1)
    stats = gather_small(jnp.stack([g_top, g_sum]))
    all_top = stats[:, 0]
    top_glob = jnp.max(all_top, axis=0)
    sum_glob = jnp.sum(stats[:, 1] * jnp.exp(all_top - top_glob[None]), axis=0)
    lse_glob = top_glob + jnp.log(sum_glob)
    g_prob = jnp.where(slot_valid[None, :, None], jnp.exp(g_score - lse_glob[..., None]), 0.0)
    g_weight = g_prob.astype(jnp.bfloat16)
    out_own = reduce_own(from_heads(mixed("hgr,hre->hge", g_weight, v_h)))
    out_own16 = out_own.astype(jnp.bfloat16)
    delta_own = jnp.sum(
        by_head(picked[3]).astype(jnp.float32) * by_head(out_own16).astype(jnp.float32), axis=-1
    )
    delta_g = jnp.transpose(gather_small(delta_own).reshape(slots, HEADS))
    band_out16 = band_out.astype(jnp.bfloat16)
    out_full = jnp.where(
        own_row[:, :, None], out_own16[:, None, :], band_out16.reshape(own_blocks, BLOCK, D)
    ).reshape(rows, D)

    grad_wide = jnp.stack([dk_wide, dv_wide])
    rims = jnp.concatenate(
        [grad_wide[:, :reach_rows], grad_wide[:, wide_rows - reach_rows :]], axis=1
    )
    back_left, back_right = halo(rims, reach_rows)
    center = grad_wide[:, reach_rows : reach_rows + rows]
    center = center.at[:, :reach_rows].add(back_left).at[:, rows - reach_rows :].add(back_right)

    g_dprob = mixed("hge,hre->hgr", dog, v_h)
    g_dscore = (g_prob * (g_dprob - delta_g[..., None])).astype(jnp.bfloat16)
    row_dq = mixed("hgr,hre->hge", g_dscore, k_h) * scale
    part_dk = mixed("hgr,hge->hre", g_dscore, qg) * scale
    part_dv = mixed("hgr,hge->hre", g_weight, dog)

    totals = reduce_own(
        jnp.concatenate([from_heads(row_dq), dk_glob, dv_glob], axis=1)
    )
    d_queries = place(band_dq, totals[:, :D])
    d_keys = place(center[0] + from_heads(part_dk), totals[:, D : 2 * D])
    d_values = place(center[1] + from_heads(part_dv), totals[:, 2 * D :])
    return (
        out_full,
        d_queries.astype(jnp.bfloat16),
        d_keys.astype(jnp.bfloat16),
        d_values.astype(jnp.bfloat16),
    )


def solution(mesh):
    rows = P(("groups", "seq"), None)
    return jax.shard_map(
        local,
        mesh=mesh,
        in_specs=(rows, rows, rows, rows, P("groups"), P("groups")),
        out_specs=(rows, rows, rows, rows),
        check_vma=False,
    )
```

```python
import jax
import jax.numpy as jnp
from jax import lax
from jax.sharding import PartitionSpec as P
from jax.experimental import pallas as pl
from jax.experimental.pallas import tpu as pltpu

D = 768
HEADS = 12
BLOCK = 64
REACH = 3
GLOBALS = 128
HEAD_DIM = 64
TILE_BLOCKS = 2

neg_large = -1e30


def mixed(form, left, right):
    return jnp.einsum(form, left, right, preferred_element_type=jnp.float32)


def to_heads(array):
    rows = array.shape[0]
    return jnp.transpose(array.reshape(rows, HEADS, HEAD_DIM), (1, 0, 2))


def from_heads(array):
    rows = array.shape[1]
    return jnp.transpose(array, (1, 0, 2)).reshape(rows, D)


def halo(cells, width):
    count = lax.axis_size("seq")
    ends = count - 1
    head = lax.slice_in_dim(cells, 0, width, axis=1)
    tail = lax.slice_in_dim(cells, cells.shape[1] - width, cells.shape[1], axis=1)
    from_left = lax.ppermute(tail, "seq", [(i, i + 1) for i in range(ends)])
    from_right = lax.ppermute(head, "seq", [(i + 1, i) for i in range(ends)])
    return from_left, from_right


def by_head(array):
    return array.reshape(array.shape[:-1] + (HEADS, HEAD_DIM))


def gather_small(part):
    count = lax.axis_size("seq")
    spread = jnp.broadcast_to(part[None], (count,) + part.shape)
    return lax.all_to_all(spread, "seq", 0, 0)


def reduce_own(full):
    count = lax.axis_size("seq")
    split = full.reshape((count, full.shape[0] // count) + full.shape[1:])
    return jnp.sum(lax.all_to_all(split, "seq", 0, 0), axis=0)


def key_flags(first_pos, span_len, glob_pos, lens_wide):
    places = first_pos + jnp.arange(span_len, dtype=jnp.int32)
    begin = jnp.asarray(first_pos // BLOCK + 2 * REACH, dtype=jnp.int32)
    lens = lax.dynamic_slice_in_dim(lens_wide, begin, span_len // BLOCK)
    inside = (jnp.arange(BLOCK, dtype=jnp.int32)[None, :] < lens[:, None]).reshape(span_len)
    marked = jnp.any(glob_pos[:, None] == places[None, :], axis=0)
    return (inside, marked)


def band_kernel(mask_ref, gmask_ref, keep_ref, q_ref, do_ref, kw_ref, vw_ref, kg_ref, vg_ref,
                out_ref, dq_ref, dkw_ref, dvw_ref, dkg_ref, dvg_ref):
    scale = HEAD_DIM ** (-0.5)
    tile = pl.program_id(1)
    tile_rows = q_ref.shape[0]
    win_rows = mask_ref.shape[2]
    start = pl.multiple_of(tile * tile_rows, tile_rows)
    f32 = jnp.float32
    bf16 = jnp.bfloat16
    nt = (((1,), (1,)), ((), ()))
    tn = (((0,), (0,)), ((), ()))

    @pl.when(tile == 0)
    def _():
        dkw_ref[...] = jnp.zeros_like(dkw_ref)
        dvw_ref[...] = jnp.zeros_like(dvw_ref)
        dkg_ref[...] = jnp.zeros_like(dkg_ref)
        dvg_ref[...] = jnp.zeros_like(dvg_ref)

    band_bias = mask_ref[0]
    glob_bias = gmask_ref[...]
    keep = keep_ref[...].astype(bf16)
    for head in range(q_ref.shape[1] // HEAD_DIM):
        lanes = slice(head * HEAD_DIM, (head + 1) * HEAD_DIM)
        q = q_ref[:, lanes] * jnp.asarray(scale, bf16)
        do = do_ref[:, lanes] * keep
        kwin = kw_ref[pl.ds(start, win_rows), lanes]
        vwin = vw_ref[pl.ds(start, win_rows), lanes]
        kg = kg_ref[:, lanes]
        vg = vg_ref[:, lanes]
        s_b = lax.dot_general(q, kwin, nt, preferred_element_type=f32) + band_bias
        s_g = lax.dot_general(q, kg, nt, preferred_element_type=f32) + glob_bias
        top = jnp.maximum(jnp.max(s_b, axis=1, keepdims=True), jnp.max(s_g, axis=1, keepdims=True))
        e_b = jnp.exp(s_b - top)
        e_g = jnp.exp(s_g - top)
        inv = 1.0 / (jnp.sum(e_b, axis=1, keepdims=True) + jnp.sum(e_g, axis=1, keepdims=True))
        p_b = e_b * inv
        p_g = e_g * inv
        w_b = p_b.astype(bf16)
        w_g = p_g.astype(bf16)
        out = jnp.dot(w_b, vwin, preferred_element_type=f32) + jnp.dot(
            w_g, vg, preferred_element_type=f32
        )
        out_ref[:, lanes] = out
        delta = jnp.sum(
            do.astype(f32) * out.astype(bf16).astype(f32), axis=1, keepdims=True
        )
        dp_b = lax.dot_general(do, vwin, nt, preferred_element_type=f32)
        dp_g = lax.dot_general(do, vg, nt, preferred_element_type=f32)
        ds_b = (p_b * (dp_b - delta)).astype(bf16)
        ds_g = (p_g * (dp_g - delta)).astype(bf16)
        dq = jnp.dot(ds_b, kwin, preferred_element_type=f32) + jnp.dot(
            ds_g, kg, preferred_element_type=f32
        )
        dq_ref[:, lanes] = dq * scale
        dkw_ref[pl.ds(start, win_rows), lanes] += lax.dot_general(ds_b, q, tn, preferred_element_type=f32)
        dvw_ref[pl.ds(start, win_rows), lanes] += lax.dot_general(w_b, do, tn, preferred_element_type=f32)
        dkg_ref[:, lanes] += lax.dot_general(ds_g, q, tn, preferred_element_type=f32)
        dvg_ref[:, lanes] += lax.dot_general(w_g, do, tn, preferred_element_type=f32)


def band_call(mask, gmask, keep, queries, d_out, key_wide, value_wide, key_glob, value_glob, interpret=False):
    rows = queries.shape[0]
    wide_rows = key_wide.shape[0]
    slots = key_glob.shape[0]
    tiles, tile_rows, win_rows = mask.shape
    lanes = 2 * HEAD_DIM
    pairs = D // lanes
    f32 = jnp.float32
    row_spec = pl.BlockSpec((tile_rows, lanes), lambda p, t: (t, p))
    wide_spec = pl.BlockSpec((wide_rows, lanes), lambda p, t: (0, p))
    glob_spec = pl.BlockSpec((slots, lanes), lambda p, t: (0, p))
    return pl.pallas_call(
        band_kernel,
        grid=(pairs, tiles),
        in_specs=[
            pl.BlockSpec((1, tile_rows, win_rows), lambda p, t: (t, 0, 0)),
            pl.BlockSpec((1, slots), lambda p, t: (0, 0)),
            pl.BlockSpec((tile_rows, 1), lambda p, t: (t, 0)),
            row_spec,
            row_spec,
            wide_spec,
            wide_spec,
            glob_spec,
            glob_spec,
        ],
        out_specs=[row_spec, row_spec, wide_spec, wide_spec, glob_spec, glob_spec],
        out_shape=[
            jax.ShapeDtypeStruct((rows, D), f32),
            jax.ShapeDtypeStruct((rows, D), f32),
            jax.ShapeDtypeStruct((wide_rows, D), f32),
            jax.ShapeDtypeStruct((wide_rows, D), f32),
            jax.ShapeDtypeStruct((slots, D), f32),
            jax.ShapeDtypeStruct((slots, D), f32),
        ],
        compiler_params=pltpu.CompilerParams(dimension_semantics=("arbitrary", "arbitrary")),
        interpret=interpret,
    )(mask, gmask, keep, queries, d_out, key_wide, value_wide, key_glob, value_glob)


def band_kernel_t(mask_ref, gmask_ref, keep_ref, keep_row_ref, q_ref, qt_ref, do_ref, dot_ref,
                  kw_ref, kt_ref, vw_ref, vt_ref, kg_ref, kgt_ref, vg_ref, vgt_ref,
                  out_ref, dq_ref, dkw_ref, dvw_ref, dkg_ref, dvg_ref):
    scale = HEAD_DIM ** (-0.5)
    tile = pl.program_id(1)
    tile_rows = q_ref.shape[0]
    win_rows = mask_ref.shape[1]
    start = pl.multiple_of(tile * tile_rows, tile_rows)
    f32 = jnp.float32
    bf16 = jnp.bfloat16

    @pl.when(tile == 0)
    def _():
        dkw_ref[...] = jnp.zeros_like(dkw_ref)
        dvw_ref[...] = jnp.zeros_like(dvw_ref)
        dkg_ref[...] = jnp.zeros_like(dkg_ref)
        dvg_ref[...] = jnp.zeros_like(dvg_ref)

    band_bias = mask_ref[0]
    glob_bias = gmask_ref[...]
    keep = keep_ref[...].astype(bf16)
    keep_row = keep_row_ref[...].astype(bf16)
    shrink = jnp.asarray(scale, bf16)
    for head in range(q_ref.shape[1] // HEAD_DIM):
        lanes = slice(head * HEAD_DIM, (head + 1) * HEAD_DIM)
        q = q_ref[:, lanes] * shrink
        qt = qt_ref[lanes, :] * shrink
        do = do_ref[:, lanes] * keep
        dot = dot_ref[lanes, :] * keep_row
        kwin = kw_ref[pl.ds(start, win_rows), lanes]
        ktwin = kt_ref[lanes, pl.ds(start, win_rows)]
        vwin = vw_ref[pl.ds(start, win_rows), lanes]
        vtwin = vt_ref[lanes, pl.ds(start, win_rows)]
        kg = kg_ref[:, lanes]
        kgt = kgt_ref[lanes, :]
        vg = vg_ref[:, lanes]
        vgt = vgt_ref[lanes, :]
        s_b = jnp.dot(kwin, qt, preferred_element_type=f32) + band_bias
        s_g = jnp.dot(kg, qt, preferred_element_type=f32) + glob_bias
        top = jnp.maximum(jnp.max(s_b, axis=0, keepdims=True), jnp.max(s_g, axis=0, keepdims=True))
        e_b = jnp.exp(s_b - top)
        e_g = jnp.exp(s_g - top)
        inv = 1.0 / (jnp.sum(e_b, axis=0, keepdims=True) + jnp.sum(e_g, axis=0, keepdims=True))
        p_b = e_b * inv
        p_g = e_g * inv
        w_b = p_b.astype(bf16)
        w_g = p_g.astype(bf16)
        out = jnp.dot(vtwin, w_b, preferred_element_type=f32) + jnp.dot(
            vgt, w_g, preferred_element_type=f32
        )
        out_ref[lanes, :] = out
        delta = jnp.sum(
            dot.astype(f32) * out.astype(bf16).astype(f32), axis=0, keepdims=True
        )
        dp_b = jnp.dot(vwin, dot, preferred_element_type=f32)
        dp_g = jnp.dot(vg, dot, preferred_element_type=f32)
        ds_b = (p_b * (dp_b - delta)).astype(bf16)
        ds_g = (p_g * (dp_g - delta)).astype(bf16)
        dq = jnp.dot(ktwin, ds_b, preferred_element_type=f32) + jnp.dot(
            kgt, ds_g, preferred_element_type=f32
        )
        dq_ref[lanes, :] = dq * scale
        dkw_ref[pl.ds(start, win_rows), lanes] += jnp.dot(ds_b, q, preferred_element_type=f32)
        dvw_ref[pl.ds(start, win_rows), lanes] += jnp.dot(w_b, do, preferred_element_type=f32)
        dkg_ref[:, lanes] += jnp.dot(ds_g, q, preferred_element_type=f32)
        dvg_ref[:, lanes] += jnp.dot(w_g, do, preferred_element_type=f32)


def band_call_t(mask, gmask, keep, queries, d_out, key_wide, value_wide, key_glob, value_glob, interpret=False):
    rows = queries.shape[0]
    wide_rows = key_wide.shape[0]
    slots = key_glob.shape[0]
    tiles, tile_rows, win_rows = mask.shape
    lanes = 2 * HEAD_DIM
    pairs = D // lanes
    f32 = jnp.float32
    row_spec = pl.BlockSpec((tile_rows, lanes), lambda p, t: (t, p))
    col_spec = pl.BlockSpec((lanes, tile_rows), lambda p, t: (p, t))
    wide_spec = pl.BlockSpec((wide_rows, lanes), lambda p, t: (0, p))
    wide_t_spec = pl.BlockSpec((lanes, wide_rows), lambda p, t: (p, 0))
    glob_spec = pl.BlockSpec((slots, lanes), lambda p, t: (0, p))
    glob_t_spec = pl.BlockSpec((lanes, slots), lambda p, t: (p, 0))
    out_t, dq_t, dkw, dvw, dkg, dvg = pl.pallas_call(
        band_kernel_t,
        grid=(pairs, tiles),
        in_specs=[
            pl.BlockSpec((1, win_rows, tile_rows), lambda p, t: (t, 0, 0)),
            pl.BlockSpec((slots, 1), lambda p, t: (0, 0)),
            pl.BlockSpec((tile_rows, 1), lambda p, t: (t, 0)),
            pl.BlockSpec((1, tile_rows), lambda p, t: (0, t)),
            row_spec,
            col_spec,
            row_spec,
            col_spec,
            wide_spec,
            wide_t_spec,
            wide_spec,
            wide_t_spec,
            glob_spec,
            glob_t_spec,
            glob_spec,
            glob_t_spec,
        ],
        out_specs=[col_spec, col_spec, wide_spec, wide_spec, glob_spec, glob_spec],
        out_shape=[
            jax.ShapeDtypeStruct((D, rows), f32),
            jax.ShapeDtypeStruct((D, rows), f32),
            jax.ShapeDtypeStruct((wide_rows, D), f32),
            jax.ShapeDtypeStruct((wide_rows, D), f32),
            jax.ShapeDtypeStruct((slots, D), f32),
            jax.ShapeDtypeStruct((slots, D), f32),
        ],
        compiler_params=pltpu.CompilerParams(dimension_semantics=("arbitrary", "arbitrary")),
        interpret=interpret,
    )(
        jnp.transpose(mask, (0, 2, 1)),
        jnp.transpose(gmask),
        keep,
        jnp.transpose(keep),
        queries,
        jnp.transpose(queries),
        d_out,
        jnp.transpose(d_out),
        key_wide,
        jnp.transpose(key_wide),
        value_wide,
        jnp.transpose(value_wide),
        key_glob,
        jnp.transpose(key_glob),
        value_glob,
        jnp.transpose(value_glob),
    )
    return jnp.transpose(out_t), jnp.transpose(dq_t), dkw, dvw, dkg, dvg


def local(queries, keys, values, d_out, glob_pos, block_len):
    scale = HEAD_DIM ** (-0.5)
    rows = queries.shape[0]
    reach_rows = REACH * BLOCK
    tile_rows = TILE_BLOCKS * BLOCK
    tiles = rows // tile_rows
    win_rows = tile_rows + 2 * reach_rows
    wide_rows = rows + 2 * reach_rows
    first_row = lax.axis_index("seq") * rows
    lens_wide = jnp.pad(block_len, 2 * REACH)

    places = first_row + jnp.arange(rows, dtype=jnp.int32)
    marked_rows = jnp.any(glob_pos[:, None] == places[None, :], axis=0)
    local_pos = glob_pos - first_row
    is_local = (local_pos >= 0) & (local_pos < rows)
    local_index = jnp.where(is_local, local_pos, rows)
    inside_rows, _ = key_flags(first_row, rows, glob_pos, lens_wide)

    count = lax.axis_size("seq")
    own_blocks = rows // BLOCK
    slots = own_blocks * count
    glob_block = glob_pos // BLOCK
    slot_valid = jnp.zeros((slots,), bool).at[glob_block].set(True, mode="drop")
    own_slot = lax.axis_index("seq") * own_blocks + jnp.arange(own_blocks, dtype=jnp.int32)
    own_match = glob_block[None, :] == own_slot[:, None]
    own_has = jnp.any(own_match, axis=1)
    own_pos = jnp.sum(jnp.where(own_match, glob_pos[None, :], 0), axis=1) - first_row
    own_offset = own_pos - BLOCK * jnp.arange(own_blocks, dtype=jnp.int32)
    own_row = own_has[:, None] & (jnp.arange(BLOCK, dtype=jnp.int32)[None, :] == own_offset[:, None])

    def place(base, extra):
        shaped = base.reshape(own_blocks, BLOCK, D)
        return jnp.where(own_row[:, :, None], shaped + extra[:, None, :], shaped).reshape(rows, D)

    own_pick = (
        own_has[:, None] & (jnp.arange(rows, dtype=jnp.int32)[None, :] == own_pos[:, None])
    ).astype(jnp.bfloat16)
    picked = jnp.stack(
        [
            jnp.dot(own_pick, source, preferred_element_type=jnp.float32).astype(jnp.bfloat16)
            for source in (queries, keys, values, d_out)
        ]
    )
    shared = jnp.transpose(gather_small(picked), (1, 0, 2, 3)).reshape(4, slots, D)
    qg = to_heads(shared[0])
    kg = to_heads(shared[1])
    vg = to_heads(shared[2])
    dog = to_heads(shared[3])

    pair = jnp.stack([keys, values])
    from_left, from_right = halo(pair, reach_rows)
    pair_wide = jnp.concatenate([from_left, pair, from_right], axis=1)
    k_h = to_heads(keys)
    v_h = to_heads(values)

    inside_wide, marked_wide = key_flags(first_row - reach_rows, wide_rows, glob_pos, lens_wide)
    allowed_wide = inside_wide & jnp.logical_not(marked_wide)

    allowed_t = jnp.stack(
        [lax.slice_in_dim(allowed_wide, t * tile_rows, t * tile_rows + win_rows) for t in range(tiles)]
    )
    q_block = (jnp.arange(rows, dtype=jnp.int32) // BLOCK).reshape(tiles, tile_rows)
    k_block = jnp.stack(
        [t * TILE_BLOCKS + jnp.arange(win_rows, dtype=jnp.int32) // BLOCK - REACH for t in range(tiles)]
    )
    near = jnp.abs(q_block[:, :, None] - k_block[:, None, :]) <= REACH
    band_mask = near & allowed_t[:, None, :]
    band_out, band_dq, dk_wide, dv_wide, dk_glob, dv_glob = band_call_t(
        jnp.where(band_mask, 0.0, neg_large).astype(jnp.float32),
        jnp.where(slot_valid, 0.0, neg_large).astype(jnp.float32)[None, :],
        jnp.logical_not(marked_rows).astype(jnp.float32)[:, None],
        queries,
        d_out,
        pair_wide[0],
        pair_wide[1],
        shared[1],
        shared[2],
    )

    g_score = mixed("hge,hre->hgr", qg, k_h) * scale
    g_score = jnp.where(inside_rows[None, None, :], g_score, neg_large)
    g_top = jnp.max(g_score, axis=-1)
    g_sum = jnp.sum(jnp.exp(g_score - g_top[..., None]), axis=-1)
    stats = gather_small(jnp.stack([g_top, g_sum]))
    all_top = stats[:, 0]
    top_glob = jnp.max(all_top, axis=0)
    sum_glob = jnp.sum(stats[:, 1] * jnp.exp(all_top - top_glob[None]), axis=0)
    lse_glob = top_glob + jnp.log(sum_glob)
    g_prob = jnp.where(slot_valid[None, :, None], jnp.exp(g_score - lse_glob[..., None]), 0.0)
    g_weight = g_prob.astype(jnp.bfloat16)
    out_own = reduce_own(from_heads(mixed("hgr,hre->hge", g_weight, v_h)))
    out_own16 = out_own.astype(jnp.bfloat16)
    delta_own = jnp.sum(
        by_head(picked[3]).astype(jnp.float32) * by_head(out_own16).astype(jnp.float32), axis=-1
    )
    delta_g = jnp.transpose(gather_small(delta_own).reshape(slots, HEADS))
    band_out16 = band_out.astype(jnp.bfloat16)
    out_full = jnp.where(
        own_row[:, :, None], out_own16[:, None, :], band_out16.reshape(own_blocks, BLOCK, D)
    ).reshape(rows, D)

    grad_wide = jnp.stack([dk_wide, dv_wide])
    rims = jnp.concatenate(
        [grad_wide[:, :reach_rows], grad_wide[:, wide_rows - reach_rows :]], axis=1
    )
    back_left, back_right = halo(rims, reach_rows)
    center = grad_wide[:, reach_rows : reach_rows + rows]
    center = center.at[:, :reach_rows].add(back_left).at[:, rows - reach_rows :].add(back_right)

    g_dprob = mixed("hge,hre->hgr", dog, v_h)
    g_dscore = (g_prob * (g_dprob - delta_g[..., None])).astype(jnp.bfloat16)
    row_dq = mixed("hgr,hre->hge", g_dscore, k_h) * scale
    part_dk = mixed("hgr,hge->hre", g_dscore, qg) * scale
    part_dv = mixed("hgr,hge->hre", g_weight, dog)

    totals = reduce_own(
        jnp.concatenate([from_heads(row_dq), dk_glob, dv_glob], axis=1)
    )
    d_queries = place(band_dq, totals[:, :D])
    d_keys = place(center[0] + from_heads(part_dk), totals[:, D : 2 * D])
    d_values = place(center[1] + from_heads(part_dv), totals[:, 2 * D :])
    return (
        out_full,
        d_queries.astype(jnp.bfloat16),
        d_keys.astype(jnp.bfloat16),
        d_values.astype(jnp.bfloat16),
    )


def solution(mesh):
    rows = P(("groups", "seq"), None)
    return jax.shard_map(
        local,
        mesh=mesh,
        in_specs=(rows, rows, rows, rows, P("groups"), P("groups")),
        out_specs=(rows, rows, rows, rows),
        check_vma=False,
    )
```

```python
import jax
import jax.numpy as jnp
from jax import lax
from jax.sharding import PartitionSpec as P
from jax.experimental import pallas as pl
from jax.experimental.pallas import tpu as pltpu

D = 768
HEADS = 12
BLOCK = 64
REACH = 3
GLOBALS = 128
HEAD_DIM = 64
TILE_BLOCKS = 2

neg_large = -1e30


def mixed(form, left, right):
    return jnp.einsum(form, left, right, preferred_element_type=jnp.float32)


def to_heads(array):
    rows = array.shape[0]
    return jnp.transpose(array.reshape(rows, HEADS, HEAD_DIM), (1, 0, 2))


def from_heads(array):
    rows = array.shape[1]
    return jnp.transpose(array, (1, 0, 2)).reshape(rows, D)


def halo(cells, width):
    count = lax.axis_size("seq")
    ends = count - 1
    head = lax.slice_in_dim(cells, 0, width, axis=1)
    tail = lax.slice_in_dim(cells, cells.shape[1] - width, cells.shape[1], axis=1)
    from_left = lax.ppermute(tail, "seq", [(i, i + 1) for i in range(ends)])
    from_right = lax.ppermute(head, "seq", [(i + 1, i) for i in range(ends)])
    return from_left, from_right


def by_head(array):
    return array.reshape(array.shape[:-1] + (HEADS, HEAD_DIM))


def gather_small(part):
    count = lax.axis_size("seq")
    spread = jnp.broadcast_to(part[None], (count,) + part.shape)
    return lax.all_to_all(spread, "seq", 0, 0)


def reduce_own(full):
    count = lax.axis_size("seq")
    split = full.reshape((count, full.shape[0] // count) + full.shape[1:])
    return jnp.sum(lax.all_to_all(split, "seq", 0, 0), axis=0)


def key_flags(first_pos, span_len, glob_pos, lens_wide):
    places = first_pos + jnp.arange(span_len, dtype=jnp.int32)
    begin = jnp.asarray(first_pos // BLOCK + 2 * REACH, dtype=jnp.int32)
    lens = lax.dynamic_slice_in_dim(lens_wide, begin, span_len // BLOCK)
    inside = (jnp.arange(BLOCK, dtype=jnp.int32)[None, :] < lens[:, None]).reshape(span_len)
    marked = jnp.any(glob_pos[:, None] == places[None, :], axis=0)
    return (inside, marked)


def band_kernel(mask_ref, gmask_ref, keep_ref, q_ref, do_ref, kw_ref, vw_ref, kg_ref, vg_ref,
                out_ref, dq_ref, dkw_ref, dvw_ref, dkg_ref, dvg_ref):
    scale = HEAD_DIM ** (-0.5)
    tile = pl.program_id(1)
    tile_rows = q_ref.shape[0]
    win_rows = mask_ref.shape[2]
    start = pl.multiple_of(tile * tile_rows, tile_rows)
    f32 = jnp.float32
    bf16 = jnp.bfloat16
    nt = (((1,), (1,)), ((), ()))
    tn = (((0,), (0,)), ((), ()))

    @pl.when(tile == 0)
    def _():
        dkw_ref[...] = jnp.zeros_like(dkw_ref)
        dvw_ref[...] = jnp.zeros_like(dvw_ref)
        dkg_ref[...] = jnp.zeros_like(dkg_ref)
        dvg_ref[...] = jnp.zeros_like(dvg_ref)

    band_bias = mask_ref[0]
    glob_bias = gmask_ref[...]
    keep = keep_ref[...].astype(bf16)
    for head in range(q_ref.shape[1] // HEAD_DIM):
        lanes = slice(head * HEAD_DIM, (head + 1) * HEAD_DIM)
        q = q_ref[:, lanes] * jnp.asarray(scale, bf16)
        do = do_ref[:, lanes] * keep
        kwin = kw_ref[pl.ds(start, win_rows), lanes]
        vwin = vw_ref[pl.ds(start, win_rows), lanes]
        kg = kg_ref[:, lanes]
        vg = vg_ref[:, lanes]
        s_b = lax.dot_general(q, kwin, nt, preferred_element_type=f32) + band_bias
        s_g = lax.dot_general(q, kg, nt, preferred_element_type=f32) + glob_bias
        top = jnp.maximum(jnp.max(s_b, axis=1, keepdims=True), jnp.max(s_g, axis=1, keepdims=True))
        e_b = jnp.exp(s_b - top)
        e_g = jnp.exp(s_g - top)
        inv = 1.0 / (jnp.sum(e_b, axis=1, keepdims=True) + jnp.sum(e_g, axis=1, keepdims=True))
        p_b = e_b * inv
        p_g = e_g * inv
        w_b = p_b.astype(bf16)
        w_g = p_g.astype(bf16)
        out = jnp.dot(w_b, vwin, preferred_element_type=f32) + jnp.dot(
            w_g, vg, preferred_element_type=f32
        )
        out_ref[:, lanes] = out
        delta = jnp.sum(
            do.astype(f32) * out.astype(bf16).astype(f32), axis=1, keepdims=True
        )
        dp_b = lax.dot_general(do, vwin, nt, preferred_element_type=f32)
        dp_g = lax.dot_general(do, vg, nt, preferred_element_type=f32)
        ds_b = (p_b * (dp_b - delta)).astype(bf16)
        ds_g = (p_g * (dp_g - delta)).astype(bf16)
        dq = jnp.dot(ds_b, kwin, preferred_element_type=f32) + jnp.dot(
            ds_g, kg, preferred_element_type=f32
        )
        dq_ref[:, lanes] = dq * scale
        dkw_ref[pl.ds(start, win_rows), lanes] += lax.dot_general(ds_b, q, tn, preferred_element_type=f32)
        dvw_ref[pl.ds(start, win_rows), lanes] += lax.dot_general(w_b, do, tn, preferred_element_type=f32)
        dkg_ref[:, lanes] += lax.dot_general(ds_g, q, tn, preferred_element_type=f32)
        dvg_ref[:, lanes] += lax.dot_general(w_g, do, tn, preferred_element_type=f32)


def band_call(mask, gmask, keep, queries, d_out, key_wide, value_wide, key_glob, value_glob, interpret=False):
    rows = queries.shape[0]
    wide_rows = key_wide.shape[0]
    slots = key_glob.shape[0]
    tiles, tile_rows, win_rows = mask.shape
    lanes = 2 * HEAD_DIM
    pairs = D // lanes
    f32 = jnp.float32
    row_spec = pl.BlockSpec((tile_rows, lanes), lambda p, t: (t, p))
    wide_spec = pl.BlockSpec((wide_rows, lanes), lambda p, t: (0, p))
    glob_spec = pl.BlockSpec((slots, lanes), lambda p, t: (0, p))
    return pl.pallas_call(
        band_kernel,
        grid=(pairs, tiles),
        in_specs=[
            pl.BlockSpec((1, tile_rows, win_rows), lambda p, t: (t, 0, 0)),
            pl.BlockSpec((1, slots), lambda p, t: (0, 0)),
            pl.BlockSpec((tile_rows, 1), lambda p, t: (t, 0)),
            row_spec,
            row_spec,
            wide_spec,
            wide_spec,
            glob_spec,
            glob_spec,
        ],
        out_specs=[row_spec, row_spec, wide_spec, wide_spec, glob_spec, glob_spec],
        out_shape=[
            jax.ShapeDtypeStruct((rows, D), f32),
            jax.ShapeDtypeStruct((rows, D), f32),
            jax.ShapeDtypeStruct((wide_rows, D), f32),
            jax.ShapeDtypeStruct((wide_rows, D), f32),
            jax.ShapeDtypeStruct((slots, D), f32),
            jax.ShapeDtypeStruct((slots, D), f32),
        ],
        compiler_params=pltpu.CompilerParams(dimension_semantics=("arbitrary", "arbitrary")),
        interpret=interpret,
    )(mask, gmask, keep, queries, d_out, key_wide, value_wide, key_glob, value_glob)


def band_kernel_t(mask_ref, gmask_ref, keep_ref, q_ref, do_ref,
                  kw_ref, kt_ref, vw_ref, vt_ref, kg_ref, kgt_ref, vg_ref, vgt_ref,
                  out_ref, dq_ref, dkw_ref, dvw_ref, dkg_ref, dvg_ref):
    scale = HEAD_DIM ** (-0.5)
    tile = pl.program_id(1)
    tile_rows = q_ref.shape[0]
    win_rows = mask_ref.shape[1]
    start = pl.multiple_of(tile * tile_rows, tile_rows)
    f32 = jnp.float32
    bf16 = jnp.bfloat16

    @pl.when(tile == 0)
    def _():
        dkw_ref[...] = jnp.zeros_like(dkw_ref)
        dvw_ref[...] = jnp.zeros_like(dvw_ref)
        dkg_ref[...] = jnp.zeros_like(dkg_ref)
        dvg_ref[...] = jnp.zeros_like(dvg_ref)

    band_bias = mask_ref[0]
    glob_bias = gmask_ref[...]
    keep = keep_ref[...]
    for head in range(q_ref.shape[1] // HEAD_DIM):
        lanes = slice(head * HEAD_DIM, (head + 1) * HEAD_DIM)
        q_wide = q_ref[:, lanes].astype(f32) * scale
        do_wide = do_ref[:, lanes].astype(f32) * keep
        q = q_wide.astype(bf16)
        qt = jnp.transpose(q_wide).astype(bf16)
        do = do_wide.astype(bf16)
        dot = jnp.transpose(do_wide).astype(bf16)
        kwin = kw_ref[pl.ds(start, win_rows), lanes]
        ktwin = kt_ref[lanes, pl.ds(start, win_rows)]
        vwin = vw_ref[pl.ds(start, win_rows), lanes]
        vtwin = vt_ref[lanes, pl.ds(start, win_rows)]
        kg = kg_ref[:, lanes]
        kgt = kgt_ref[lanes, :]
        vg = vg_ref[:, lanes]
        vgt = vgt_ref[lanes, :]
        s_b = jnp.dot(kwin, qt, preferred_element_type=f32) + band_bias
        s_g = jnp.dot(kg, qt, preferred_element_type=f32) + glob_bias
        top = jnp.maximum(jnp.max(s_b, axis=0, keepdims=True), jnp.max(s_g, axis=0, keepdims=True))
        e_b = jnp.exp(s_b - top)
        e_g = jnp.exp(s_g - top)
        inv = 1.0 / (jnp.sum(e_b, axis=0, keepdims=True) + jnp.sum(e_g, axis=0, keepdims=True))
        p_b = e_b * inv
        p_g = e_g * inv
        w_b = p_b.astype(bf16)
        w_g = p_g.astype(bf16)
        out = jnp.dot(vtwin, w_b, preferred_element_type=f32) + jnp.dot(
            vgt, w_g, preferred_element_type=f32
        )
        out_ref[:, lanes] = jnp.transpose(out)
        delta = jnp.sum(
            dot.astype(f32) * out.astype(bf16).astype(f32), axis=0, keepdims=True
        )
        dp_b = jnp.dot(vwin, dot, preferred_element_type=f32)
        dp_g = jnp.dot(vg, dot, preferred_element_type=f32)
        ds_b = (p_b * (dp_b - delta)).astype(bf16)
        ds_g = (p_g * (dp_g - delta)).astype(bf16)
        dq = jnp.dot(ktwin, ds_b, preferred_element_type=f32) + jnp.dot(
            kgt, ds_g, preferred_element_type=f32
        )
        dq_ref[:, lanes] = jnp.transpose(dq) * scale
        dkw_ref[pl.ds(start, win_rows), lanes] += jnp.dot(ds_b, q, preferred_element_type=f32)
        dvw_ref[pl.ds(start, win_rows), lanes] += jnp.dot(w_b, do, preferred_element_type=f32)
        dkg_ref[:, lanes] += jnp.dot(ds_g, q, preferred_element_type=f32)
        dvg_ref[:, lanes] += jnp.dot(w_g, do, preferred_element_type=f32)


def band_call_t(mask, gmask, keep, queries, d_out, key_wide, value_wide, key_glob, value_glob, interpret=False):
    rows = queries.shape[0]
    wide_rows = key_wide.shape[0]
    slots = key_glob.shape[0]
    tiles, tile_rows, win_rows = mask.shape
    lanes = 2 * HEAD_DIM
    pairs = D // lanes
    f32 = jnp.float32
    row_spec = pl.BlockSpec((tile_rows, lanes), lambda p, t: (t, p))
    col_spec = pl.BlockSpec((lanes, tile_rows), lambda p, t: (p, t))
    wide_spec = pl.BlockSpec((wide_rows, lanes), lambda p, t: (0, p))
    wide_t_spec = pl.BlockSpec((lanes, wide_rows), lambda p, t: (p, 0))
    glob_spec = pl.BlockSpec((slots, lanes), lambda p, t: (0, p))
    glob_t_spec = pl.BlockSpec((lanes, slots), lambda p, t: (p, 0))
    out_t, dq_t, dkw, dvw, dkg, dvg = pl.pallas_call(
        band_kernel_t,
        grid=(pairs, tiles),
        in_specs=[
            pl.BlockSpec((1, win_rows, tile_rows), lambda p, t: (t, 0, 0)),
            pl.BlockSpec((slots, 1), lambda p, t: (0, 0)),
            pl.BlockSpec((tile_rows, 1), lambda p, t: (t, 0)),
            row_spec,
            row_spec,
            wide_spec,
            wide_t_spec,
            wide_spec,
            wide_t_spec,
            glob_spec,
            glob_t_spec,
            glob_spec,
            glob_t_spec,
        ],
        out_specs=[row_spec, row_spec, wide_spec, wide_spec, glob_spec, glob_spec],
        out_shape=[
            jax.ShapeDtypeStruct((rows, D), f32),
            jax.ShapeDtypeStruct((rows, D), f32),
            jax.ShapeDtypeStruct((wide_rows, D), f32),
            jax.ShapeDtypeStruct((wide_rows, D), f32),
            jax.ShapeDtypeStruct((slots, D), f32),
            jax.ShapeDtypeStruct((slots, D), f32),
        ],
        compiler_params=pltpu.CompilerParams(dimension_semantics=("arbitrary", "arbitrary")),
        interpret=interpret,
    )(
        jnp.transpose(mask, (0, 2, 1)),
        jnp.transpose(gmask),
        keep,
        queries,
        d_out,
        key_wide,
        jnp.transpose(key_wide),
        value_wide,
        jnp.transpose(value_wide),
        key_glob,
        jnp.transpose(key_glob),
        value_glob,
        jnp.transpose(value_glob),
    )
    return out_t, dq_t, dkw, dvw, dkg, dvg


def local(queries, keys, values, d_out, glob_pos, block_len):
    scale = HEAD_DIM ** (-0.5)
    rows = queries.shape[0]
    reach_rows = REACH * BLOCK
    tile_rows = TILE_BLOCKS * BLOCK
    tiles = rows // tile_rows
    win_rows = tile_rows + 2 * reach_rows
    wide_rows = rows + 2 * reach_rows
    first_row = lax.axis_index("seq") * rows
    lens_wide = jnp.pad(block_len, 2 * REACH)

    places = first_row + jnp.arange(rows, dtype=jnp.int32)
    marked_rows = jnp.any(glob_pos[:, None] == places[None, :], axis=0)
    local_pos = glob_pos - first_row
    is_local = (local_pos >= 0) & (local_pos < rows)
    local_index = jnp.where(is_local, local_pos, rows)
    inside_rows, _ = key_flags(first_row, rows, glob_pos, lens_wide)

    count = lax.axis_size("seq")
    own_blocks = rows // BLOCK
    slots = own_blocks * count
    glob_block = glob_pos // BLOCK
    slot_valid = jnp.zeros((slots,), bool).at[glob_block].set(True, mode="drop")
    own_slot = lax.axis_index("seq") * own_blocks + jnp.arange(own_blocks, dtype=jnp.int32)
    own_match = glob_block[None, :] == own_slot[:, None]
    own_has = jnp.any(own_match, axis=1)
    own_pos = jnp.sum(jnp.where(own_match, glob_pos[None, :], 0), axis=1) - first_row
    own_offset = own_pos - BLOCK * jnp.arange(own_blocks, dtype=jnp.int32)
    own_row = own_has[:, None] & (jnp.arange(BLOCK, dtype=jnp.int32)[None, :] == own_offset[:, None])

    def place(base, extra):
        shaped = base.reshape(own_blocks, BLOCK, D)
        return jnp.where(own_row[:, :, None], shaped + extra[:, None, :], shaped).reshape(rows, D)

    own_pick = (
        own_has[:, None] & (jnp.arange(rows, dtype=jnp.int32)[None, :] == own_pos[:, None])
    ).astype(jnp.bfloat16)
    picked = jnp.stack(
        [
            jnp.dot(own_pick, source, preferred_element_type=jnp.float32).astype(jnp.bfloat16)
            for source in (queries, keys, values, d_out)
        ]
    )
    shared = jnp.transpose(gather_small(picked), (1, 0, 2, 3)).reshape(4, slots, D)
    qg = to_heads(shared[0])
    kg = to_heads(shared[1])
    vg = to_heads(shared[2])
    dog = to_heads(shared[3])

    pair = jnp.stack([keys, values])
    from_left, from_right = halo(pair, reach_rows)
    pair_wide = jnp.concatenate([from_left, pair, from_right], axis=1)
    k_h = to_heads(keys)
    v_h = to_heads(values)

    inside_wide, marked_wide = key_flags(first_row - reach_rows, wide_rows, glob_pos, lens_wide)
    allowed_wide = inside_wide & jnp.logical_not(marked_wide)

    allowed_t = jnp.stack(
        [lax.slice_in_dim(allowed_wide, t * tile_rows, t * tile_rows + win_rows) for t in range(tiles)]
    )
    q_block = (jnp.arange(rows, dtype=jnp.int32) // BLOCK).reshape(tiles, tile_rows)
    k_block = jnp.stack(
        [t * TILE_BLOCKS + jnp.arange(win_rows, dtype=jnp.int32) // BLOCK - REACH for t in range(tiles)]
    )
    near = jnp.abs(q_block[:, :, None] - k_block[:, None, :]) <= REACH
    band_mask = near & allowed_t[:, None, :]
    band_out, band_dq, dk_wide, dv_wide, dk_glob, dv_glob = band_call_t(
        jnp.where(band_mask, 0.0, neg_large).astype(jnp.float32),
        jnp.where(slot_valid, 0.0, neg_large).astype(jnp.float32)[None, :],
        jnp.logical_not(marked_rows).astype(jnp.float32)[:, None],
        queries,
        d_out,
        pair_wide[0],
        pair_wide[1],
        shared[1],
        shared[2],
    )

    g_score = mixed("hge,hre->hgr", qg, k_h) * scale
    g_score = jnp.where(inside_rows[None, None, :], g_score, neg_large)
    g_top = jnp.max(g_score, axis=-1)
    g_sum = jnp.sum(jnp.exp(g_score - g_top[..., None]), axis=-1)
    stats = gather_small(jnp.stack([g_top, g_sum]))
    all_top = stats[:, 0]
    top_glob = jnp.max(all_top, axis=0)
    sum_glob = jnp.sum(stats[:, 1] * jnp.exp(all_top - top_glob[None]), axis=0)
    lse_glob = top_glob + jnp.log(sum_glob)
    g_prob = jnp.where(slot_valid[None, :, None], jnp.exp(g_score - lse_glob[..., None]), 0.0)
    g_weight = g_prob.astype(jnp.bfloat16)
    out_own = reduce_own(from_heads(mixed("hgr,hre->hge", g_weight, v_h)))
    out_own16 = out_own.astype(jnp.bfloat16)
    delta_own = jnp.sum(
        by_head(picked[3]).astype(jnp.float32) * by_head(out_own16).astype(jnp.float32), axis=-1
    )
    delta_g = jnp.transpose(gather_small(delta_own).reshape(slots, HEADS))
    band_out16 = band_out.astype(jnp.bfloat16)
    out_full = jnp.where(
        own_row[:, :, None], out_own16[:, None, :], band_out16.reshape(own_blocks, BLOCK, D)
    ).reshape(rows, D)

    grad_wide = jnp.stack([dk_wide, dv_wide])
    rims = jnp.concatenate(
        [grad_wide[:, :reach_rows], grad_wide[:, wide_rows - reach_rows :]], axis=1
    )
    back_left, back_right = halo(rims, reach_rows)
    center = grad_wide[:, reach_rows : reach_rows + rows]
    center = center.at[:, :reach_rows].add(back_left).at[:, rows - reach_rows :].add(back_right)

    g_dprob = mixed("hge,hre->hgr", dog, v_h)
    g_dscore = (g_prob * (g_dprob - delta_g[..., None])).astype(jnp.bfloat16)
    row_dq = mixed("hgr,hre->hge", g_dscore, k_h) * scale
    part_dk = mixed("hgr,hge->hre", g_dscore, qg) * scale
    part_dv = mixed("hgr,hge->hre", g_weight, dog)

    totals = reduce_own(
        jnp.concatenate([from_heads(row_dq), dk_glob, dv_glob], axis=1)
    )
    d_queries = place(band_dq, totals[:, :D])
    d_keys = place(center[0] + from_heads(part_dk), totals[:, D : 2 * D])
    d_values = place(center[1] + from_heads(part_dv), totals[:, 2 * D :])
    return (
        out_full,
        d_queries.astype(jnp.bfloat16),
        d_keys.astype(jnp.bfloat16),
        d_values.astype(jnp.bfloat16),
    )


def solution(mesh):
    rows = P(("groups", "seq"), None)
    return jax.shard_map(
        local,
        mesh=mesh,
        in_specs=(rows, rows, rows, rows, P("groups"), P("groups")),
        out_specs=(rows, rows, rows, rows),
        check_vma=False,
    )
```

```python
import jax
import jax.numpy as jnp
from jax import lax
from jax.sharding import PartitionSpec as P
from jax.experimental import pallas as pl
from jax.experimental.pallas import tpu as pltpu

D = 768
HEADS = 12
BLOCK = 64
REACH = 3
GLOBALS = 128
HEAD_DIM = 64
TILE_BLOCKS = 2

neg_large = -1e30


def mixed(form, left, right):
    return jnp.einsum(form, left, right, preferred_element_type=jnp.float32)


def to_heads(array):
    rows = array.shape[0]
    return jnp.transpose(array.reshape(rows, HEADS, HEAD_DIM), (1, 0, 2))


def from_heads(array):
    rows = array.shape[1]
    return jnp.transpose(array, (1, 0, 2)).reshape(rows, D)


def halo(cells, width):
    count = lax.axis_size("seq")
    ends = count - 1
    head = lax.slice_in_dim(cells, 0, width, axis=1)
    tail = lax.slice_in_dim(cells, cells.shape[1] - width, cells.shape[1], axis=1)
    from_left = lax.ppermute(tail, "seq", [(i, i + 1) for i in range(ends)])
    from_right = lax.ppermute(head, "seq", [(i + 1, i) for i in range(ends)])
    return from_left, from_right


def by_head(array):
    return array.reshape(array.shape[:-1] + (HEADS, HEAD_DIM))


def gather_small(part):
    count = lax.axis_size("seq")
    spread = jnp.broadcast_to(part[None], (count,) + part.shape)
    return lax.all_to_all(spread, "seq", 0, 0)


def reduce_own(full):
    count = lax.axis_size("seq")
    split = full.reshape((count, full.shape[0] // count) + full.shape[1:])
    return jnp.sum(lax.all_to_all(split, "seq", 0, 0), axis=0)


def key_flags(first_pos, span_len, glob_pos, lens_wide):
    places = first_pos + jnp.arange(span_len, dtype=jnp.int32)
    begin = jnp.asarray(first_pos // BLOCK + 2 * REACH, dtype=jnp.int32)
    lens = lax.dynamic_slice_in_dim(lens_wide, begin, span_len // BLOCK)
    inside = (jnp.arange(BLOCK, dtype=jnp.int32)[None, :] < lens[:, None]).reshape(span_len)
    marked = jnp.any(glob_pos[:, None] == places[None, :], axis=0)
    return (inside, marked)


def band_kernel(mask_ref, gmask_ref, keep_ref, q_ref, do_ref, kw_ref, vw_ref, kg_ref, vg_ref,
                out_ref, dq_ref, dkw_ref, dvw_ref, dkg_ref, dvg_ref):
    scale = HEAD_DIM ** (-0.5)
    tile = pl.program_id(1)
    tile_rows = q_ref.shape[0]
    win_rows = mask_ref.shape[2]
    start = pl.multiple_of(tile * tile_rows, tile_rows)
    f32 = jnp.float32
    bf16 = jnp.bfloat16
    nt = (((1,), (1,)), ((), ()))
    tn = (((0,), (0,)), ((), ()))

    @pl.when(tile == 0)
    def _():
        dkw_ref[...] = jnp.zeros_like(dkw_ref)
        dvw_ref[...] = jnp.zeros_like(dvw_ref)
        dkg_ref[...] = jnp.zeros_like(dkg_ref)
        dvg_ref[...] = jnp.zeros_like(dvg_ref)

    band_bias = mask_ref[0]
    glob_bias = gmask_ref[...]
    keep = keep_ref[...].astype(bf16)
    for head in range(q_ref.shape[1] // HEAD_DIM):
        lanes = slice(head * HEAD_DIM, (head + 1) * HEAD_DIM)
        q = q_ref[:, lanes] * jnp.asarray(scale, bf16)
        do = do_ref[:, lanes] * keep
        kwin = kw_ref[pl.ds(start, win_rows), lanes]
        vwin = vw_ref[pl.ds(start, win_rows), lanes]
        kg = kg_ref[:, lanes]
        vg = vg_ref[:, lanes]
        s_b = lax.dot_general(q, kwin, nt, preferred_element_type=f32) + band_bias
        s_g = lax.dot_general(q, kg, nt, preferred_element_type=f32) + glob_bias
        top = jnp.maximum(jnp.max(s_b, axis=1, keepdims=True), jnp.max(s_g, axis=1, keepdims=True))
        e_b = jnp.exp(s_b - top)
        e_g = jnp.exp(s_g - top)
        inv = 1.0 / (jnp.sum(e_b, axis=1, keepdims=True) + jnp.sum(e_g, axis=1, keepdims=True))
        p_b = e_b * inv
        p_g = e_g * inv
        w_b = p_b.astype(bf16)
        w_g = p_g.astype(bf16)
        out = jnp.dot(w_b, vwin, preferred_element_type=f32) + jnp.dot(
            w_g, vg, preferred_element_type=f32
        )
        out_ref[:, lanes] = out
        delta = jnp.sum(
            do.astype(f32) * out.astype(bf16).astype(f32), axis=1, keepdims=True
        )
        dp_b = lax.dot_general(do, vwin, nt, preferred_element_type=f32)
        dp_g = lax.dot_general(do, vg, nt, preferred_element_type=f32)
        ds_b = (p_b * (dp_b - delta)).astype(bf16)
        ds_g = (p_g * (dp_g - delta)).astype(bf16)
        dq = jnp.dot(ds_b, kwin, preferred_element_type=f32) + jnp.dot(
            ds_g, kg, preferred_element_type=f32
        )
        dq_ref[:, lanes] = dq * scale
        dkw_ref[pl.ds(start, win_rows), lanes] += lax.dot_general(ds_b, q, tn, preferred_element_type=f32)
        dvw_ref[pl.ds(start, win_rows), lanes] += lax.dot_general(w_b, do, tn, preferred_element_type=f32)
        dkg_ref[:, lanes] += lax.dot_general(ds_g, q, tn, preferred_element_type=f32)
        dvg_ref[:, lanes] += lax.dot_general(w_g, do, tn, preferred_element_type=f32)


def band_call(mask, gmask, keep, queries, d_out, key_wide, value_wide, key_glob, value_glob, interpret=False):
    rows = queries.shape[0]
    wide_rows = key_wide.shape[0]
    slots = key_glob.shape[0]
    tiles, tile_rows, win_rows = mask.shape
    lanes = 2 * HEAD_DIM
    pairs = D // lanes
    f32 = jnp.float32
    row_spec = pl.BlockSpec((tile_rows, lanes), lambda p, t: (t, p))
    wide_spec = pl.BlockSpec((wide_rows, lanes), lambda p, t: (0, p))
    glob_spec = pl.BlockSpec((slots, lanes), lambda p, t: (0, p))
    return pl.pallas_call(
        band_kernel,
        grid=(pairs, tiles),
        in_specs=[
            pl.BlockSpec((1, tile_rows, win_rows), lambda p, t: (t, 0, 0)),
            pl.BlockSpec((1, slots), lambda p, t: (0, 0)),
            pl.BlockSpec((tile_rows, 1), lambda p, t: (t, 0)),
            row_spec,
            row_spec,
            wide_spec,
            wide_spec,
            glob_spec,
            glob_spec,
        ],
        out_specs=[row_spec, row_spec, wide_spec, wide_spec, glob_spec, glob_spec],
        out_shape=[
            jax.ShapeDtypeStruct((rows, D), f32),
            jax.ShapeDtypeStruct((rows, D), f32),
            jax.ShapeDtypeStruct((wide_rows, D), f32),
            jax.ShapeDtypeStruct((wide_rows, D), f32),
            jax.ShapeDtypeStruct((slots, D), f32),
            jax.ShapeDtypeStruct((slots, D), f32),
        ],
        compiler_params=pltpu.CompilerParams(dimension_semantics=("arbitrary", "arbitrary")),
        interpret=interpret,
    )(mask, gmask, keep, queries, d_out, key_wide, value_wide, key_glob, value_glob)


def band_kernel_t(mask_ref, gmask_ref, keep_ref, q_ref, do_ref,
                  kw_ref, kt_ref, vw_ref, vt_ref, kg_ref, kgt_ref, vg_ref, vgt_ref,
                  out_ref, dq_ref, dkw_ref, dvw_ref, dkg_ref, dvg_ref):
    scale = HEAD_DIM ** (-0.5)
    tile = pl.program_id(1)
    tile_rows = q_ref.shape[0]
    win_rows = mask_ref.shape[1]
    start = pl.multiple_of(tile * tile_rows, tile_rows)
    f32 = jnp.float32
    bf16 = jnp.bfloat16

    @pl.when(tile == 0)
    def _():
        dkw_ref[...] = jnp.zeros_like(dkw_ref)
        dvw_ref[...] = jnp.zeros_like(dvw_ref)
        dkg_ref[...] = jnp.zeros_like(dkg_ref)
        dvg_ref[...] = jnp.zeros_like(dvg_ref)

    band_bias = mask_ref[0]
    glob_bias = gmask_ref[...]
    keep = keep_ref[...]
    for head in range(q_ref.shape[1] // HEAD_DIM):
        lanes = slice(head * HEAD_DIM, (head + 1) * HEAD_DIM)
        q_wide = q_ref[:, lanes].astype(f32) * scale
        do_wide = do_ref[:, lanes].astype(f32) * keep
        q = q_wide.astype(bf16)
        qt = jnp.transpose(q_wide).astype(bf16)
        do = do_wide.astype(bf16)
        dot = jnp.transpose(do_wide).astype(bf16)
        kwin = kw_ref[pl.ds(start, win_rows), lanes]
        ktwin = kt_ref[lanes, pl.ds(start, win_rows)]
        vwin = vw_ref[pl.ds(start, win_rows), lanes]
        vtwin = vt_ref[lanes, pl.ds(start, win_rows)]
        kg = kg_ref[:, lanes]
        kgt = kgt_ref[lanes, :]
        vg = vg_ref[:, lanes]
        vgt = vgt_ref[lanes, :]
        s_b = jnp.dot(kwin, qt, preferred_element_type=f32) + band_bias
        s_g = jnp.dot(kg, qt, preferred_element_type=f32) + glob_bias
        top = jnp.maximum(jnp.max(s_b, axis=0, keepdims=True), jnp.max(s_g, axis=0, keepdims=True))
        e_b = jnp.exp(s_b - top)
        e_g = jnp.exp(s_g - top)
        inv = 1.0 / (jnp.sum(e_b, axis=0, keepdims=True) + jnp.sum(e_g, axis=0, keepdims=True))
        p_b = e_b * inv
        p_g = e_g * inv
        w_b = p_b.astype(bf16)
        w_g = p_g.astype(bf16)
        out = jnp.dot(vtwin, w_b, preferred_element_type=f32) + jnp.dot(
            vgt, w_g, preferred_element_type=f32
        )
        out_ref[:, lanes] = jnp.transpose(out)
        delta = jnp.sum(
            dot.astype(f32) * out.astype(bf16).astype(f32), axis=0, keepdims=True
        )
        dp_b = jnp.dot(vwin, dot, preferred_element_type=f32)
        dp_g = jnp.dot(vg, dot, preferred_element_type=f32)
        ds_b = (p_b * (dp_b - delta)).astype(bf16)
        ds_g = (p_g * (dp_g - delta)).astype(bf16)
        dq = jnp.dot(ktwin, ds_b, preferred_element_type=f32) + jnp.dot(
            kgt, ds_g, preferred_element_type=f32
        )
        dq_ref[:, lanes] = jnp.transpose(dq) * scale
        dkw_ref[pl.ds(start, win_rows), lanes] += jnp.dot(ds_b, q, preferred_element_type=f32)
        dvw_ref[pl.ds(start, win_rows), lanes] += jnp.dot(w_b, do, preferred_element_type=f32)
        dkg_ref[:, lanes] += jnp.dot(ds_g, q, preferred_element_type=f32)
        dvg_ref[:, lanes] += jnp.dot(w_g, do, preferred_element_type=f32)


def band_call_t(mask, gmask, keep, queries, d_out, key_wide, value_wide, key_glob, value_glob, interpret=False):
    rows = queries.shape[0]
    wide_rows = key_wide.shape[0]
    slots = key_glob.shape[0]
    tiles, tile_rows, win_rows = mask.shape
    lanes = 2 * HEAD_DIM
    pairs = D // lanes
    f32 = jnp.float32
    row_spec = pl.BlockSpec((tile_rows, lanes), lambda p, t: (t, p))
    col_spec = pl.BlockSpec((lanes, tile_rows), lambda p, t: (p, t))
    wide_spec = pl.BlockSpec((wide_rows, lanes), lambda p, t: (0, p))
    wide_t_spec = pl.BlockSpec((lanes, wide_rows), lambda p, t: (p, 0))
    glob_spec = pl.BlockSpec((slots, lanes), lambda p, t: (0, p))
    glob_t_spec = pl.BlockSpec((lanes, slots), lambda p, t: (p, 0))
    out_t, dq_t, dkw, dvw, dkg, dvg = pl.pallas_call(
        band_kernel_t,
        grid=(pairs, tiles),
        in_specs=[
            pl.BlockSpec((1, win_rows, tile_rows), lambda p, t: (t, 0, 0)),
            pl.BlockSpec((slots, 1), lambda p, t: (0, 0)),
            pl.BlockSpec((tile_rows, 1), lambda p, t: (t, 0)),
            row_spec,
            row_spec,
            wide_spec,
            wide_t_spec,
            wide_spec,
            wide_t_spec,
            glob_spec,
            glob_t_spec,
            glob_spec,
            glob_t_spec,
        ],
        out_specs=[row_spec, row_spec, wide_spec, wide_spec, glob_spec, glob_spec],
        out_shape=[
            jax.ShapeDtypeStruct((rows, D), f32),
            jax.ShapeDtypeStruct((rows, D), f32),
            jax.ShapeDtypeStruct((wide_rows, D), f32),
            jax.ShapeDtypeStruct((wide_rows, D), f32),
            jax.ShapeDtypeStruct((slots, D), f32),
            jax.ShapeDtypeStruct((slots, D), f32),
        ],
        compiler_params=pltpu.CompilerParams(dimension_semantics=("arbitrary", "arbitrary")),
        interpret=interpret,
    )(
        jnp.transpose(mask, (0, 2, 1)),
        jnp.transpose(gmask),
        keep,
        queries,
        d_out,
        key_wide,
        jnp.transpose(key_wide),
        value_wide,
        jnp.transpose(value_wide),
        key_glob,
        jnp.transpose(key_glob),
        value_glob,
        jnp.transpose(value_glob),
    )
    return out_t, dq_t, dkw, dvw, dkg, dvg


def local(queries, keys, values, d_out, glob_pos, block_len):
    scale = HEAD_DIM ** (-0.5)
    rows = queries.shape[0]
    reach_rows = REACH * BLOCK
    tile_rows = TILE_BLOCKS * BLOCK
    tiles = rows // tile_rows
    win_rows = tile_rows + 2 * reach_rows
    wide_rows = rows + 2 * reach_rows
    first_row = lax.axis_index("seq") * rows
    lens_wide = jnp.pad(block_len, 2 * REACH)

    places = first_row + jnp.arange(rows, dtype=jnp.int32)
    marked_rows = jnp.any(glob_pos[:, None] == places[None, :], axis=0)
    local_pos = glob_pos - first_row
    is_local = (local_pos >= 0) & (local_pos < rows)
    local_index = jnp.where(is_local, local_pos, rows)
    inside_rows, _ = key_flags(first_row, rows, glob_pos, lens_wide)

    count = lax.axis_size("seq")
    own_blocks = rows // BLOCK
    slots = own_blocks * count
    glob_block = glob_pos // BLOCK
    slot_valid = jnp.zeros((slots,), bool).at[glob_block].set(True, mode="drop")
    own_slot = lax.axis_index("seq") * own_blocks + jnp.arange(own_blocks, dtype=jnp.int32)
    own_match = glob_block[None, :] == own_slot[:, None]
    own_has = jnp.any(own_match, axis=1)
    own_pos = jnp.sum(jnp.where(own_match, glob_pos[None, :], 0), axis=1) - first_row
    own_offset = own_pos - BLOCK * jnp.arange(own_blocks, dtype=jnp.int32)
    own_row = own_has[:, None] & (jnp.arange(BLOCK, dtype=jnp.int32)[None, :] == own_offset[:, None])

    def place(base, extra):
        shaped = base.reshape(own_blocks, BLOCK, D)
        return jnp.where(own_row[:, :, None], shaped + extra[:, None, :], shaped).reshape(rows, D)

    own_pick = (
        own_has[:, None] & (jnp.arange(rows, dtype=jnp.int32)[None, :] == own_pos[:, None])
    ).astype(jnp.bfloat16)
    picked = jnp.stack(
        [
            jnp.dot(own_pick, source, preferred_element_type=jnp.float32).astype(jnp.bfloat16)
            for source in (queries, keys, values, d_out)
        ]
    )
    shared = jnp.transpose(gather_small(picked), (1, 0, 2, 3)).reshape(4, slots, D)
    qg = to_heads(shared[0])
    kg = to_heads(shared[1])
    vg = to_heads(shared[2])
    dog = to_heads(shared[3])

    pair = jnp.stack([keys, values])
    from_left, from_right = halo(pair, reach_rows)
    pair_wide = jnp.concatenate([from_left, pair, from_right], axis=1)
    k_h = to_heads(keys)
    v_h = to_heads(values)

    inside_wide, marked_wide = key_flags(first_row - reach_rows, wide_rows, glob_pos, lens_wide)
    allowed_wide = inside_wide & jnp.logical_not(marked_wide)

    allowed_t = jnp.stack(
        [lax.slice_in_dim(allowed_wide, t * tile_rows, t * tile_rows + win_rows) for t in range(tiles)]
    )
    q_block = (jnp.arange(rows, dtype=jnp.int32) // BLOCK).reshape(tiles, tile_rows)
    k_block = jnp.stack(
        [t * TILE_BLOCKS + jnp.arange(win_rows, dtype=jnp.int32) // BLOCK - REACH for t in range(tiles)]
    )
    near = jnp.abs(q_block[:, :, None] - k_block[:, None, :]) <= REACH
    band_mask = near & allowed_t[:, None, :]
    band_out, band_dq, dk_wide, dv_wide, dk_glob, dv_glob = band_call_t(
        jnp.where(band_mask, 0.0, neg_large).astype(jnp.float32),
        jnp.where(slot_valid, 0.0, neg_large).astype(jnp.float32)[None, :],
        jnp.logical_not(marked_rows).astype(jnp.float32)[:, None],
        queries,
        d_out,
        pair_wide[0],
        pair_wide[1],
        shared[1],
        shared[2],
    )

    g_score = mixed("hge,hre->hgr", qg, k_h) * scale
    g_score = jnp.where(inside_rows[None, None, :], g_score, neg_large)
    g_top = jnp.max(g_score, axis=-1)
    g_exp = jnp.exp(g_score - g_top[..., None])
    g_sum = jnp.sum(g_exp, axis=-1)
    g_acc = from_heads(mixed("hgr,hre->hge", g_exp.astype(jnp.bfloat16), v_h))
    payload = jnp.concatenate([g_acc, jnp.transpose(g_top), jnp.transpose(g_sum)], axis=1)
    parts = lax.all_to_all(payload.reshape(count, own_blocks, D + 2 * HEADS), "seq", 0, 0)
    part_top = parts[:, :, D : D + HEADS]
    own_top = jnp.max(part_top, axis=0)
    rescale = jnp.exp(part_top - own_top[None])
    own_sum = jnp.sum(parts[:, :, D + HEADS :] * rescale, axis=0)
    own_acc = jnp.sum(by_head(parts[:, :, :D]) * rescale[..., None], axis=0)
    out_own16 = (own_acc / own_sum[..., None]).reshape(own_blocks, D).astype(jnp.bfloat16)
    own_lse = own_top + jnp.log(own_sum)
    delta_own = jnp.sum(
        by_head(picked[3]).astype(jnp.float32) * by_head(out_own16).astype(jnp.float32), axis=-1
    )
    glob_stats = gather_small(jnp.stack([own_lse, delta_own], axis=-1)).reshape(slots, HEADS, 2)
    lse_glob = jnp.transpose(glob_stats[..., 0])
    delta_g = jnp.transpose(glob_stats[..., 1])
    g_prob = jnp.where(slot_valid[None, :, None], jnp.exp(g_score - lse_glob[..., None]), 0.0)
    g_weight = g_prob.astype(jnp.bfloat16)
    band_out16 = band_out.astype(jnp.bfloat16)
    out_full = jnp.where(
        own_row[:, :, None], out_own16[:, None, :], band_out16.reshape(own_blocks, BLOCK, D)
    ).reshape(rows, D)

    grad_wide = jnp.stack([dk_wide, dv_wide])
    rims = jnp.concatenate(
        [grad_wide[:, :reach_rows], grad_wide[:, wide_rows - reach_rows :]], axis=1
    )
    back_left, back_right = halo(rims, reach_rows)
    center = grad_wide[:, reach_rows : reach_rows + rows]
    center = center.at[:, :reach_rows].add(back_left).at[:, rows - reach_rows :].add(back_right)

    g_dprob = mixed("hge,hre->hgr", dog, v_h)
    g_dscore = (g_prob * (g_dprob - delta_g[..., None])).astype(jnp.bfloat16)
    row_dq = mixed("hgr,hre->hge", g_dscore, k_h) * scale
    part_dk = mixed("hgr,hge->hre", g_dscore, qg) * scale
    part_dv = mixed("hgr,hge->hre", g_weight, dog)

    totals = reduce_own(
        jnp.concatenate([from_heads(row_dq), dk_glob, dv_glob], axis=1)
    )
    d_queries = place(band_dq, totals[:, :D])
    d_keys = place(center[0] + from_heads(part_dk), totals[:, D : 2 * D])
    d_values = place(center[1] + from_heads(part_dv), totals[:, 2 * D :])
    return (
        out_full,
        d_queries.astype(jnp.bfloat16),
        d_keys.astype(jnp.bfloat16),
        d_values.astype(jnp.bfloat16),
    )


def solution(mesh):
    rows = P(("groups", "seq"), None)
    return jax.shard_map(
        local,
        mesh=mesh,
        in_specs=(rows, rows, rows, rows, P("groups"), P("groups")),
        out_specs=(rows, rows, rows, rows),
        check_vma=False,
    )
```

```python
import jax
import jax.numpy as jnp
from jax import lax
from jax.sharding import PartitionSpec as P
from jax.experimental import pallas as pl
from jax.experimental.pallas import tpu as pltpu

D = 768
HEADS = 12
BLOCK = 64
REACH = 3
GLOBALS = 128
HEAD_DIM = 64
TILE_BLOCKS = 2

neg_large = -1e30


def mixed(form, left, right):
    return jnp.einsum(form, left, right, preferred_element_type=jnp.float32)


def to_heads(array):
    rows = array.shape[0]
    return jnp.transpose(array.reshape(rows, HEADS, HEAD_DIM), (1, 0, 2))


def from_heads(array):
    rows = array.shape[1]
    return jnp.transpose(array, (1, 0, 2)).reshape(rows, D)


def halo(cells, width):
    count = lax.axis_size("seq")
    ends = count - 1
    head = lax.slice_in_dim(cells, 0, width, axis=1)
    tail = lax.slice_in_dim(cells, cells.shape[1] - width, cells.shape[1], axis=1)
    from_left = lax.ppermute(tail, "seq", [(i, i + 1) for i in range(ends)])
    from_right = lax.ppermute(head, "seq", [(i + 1, i) for i in range(ends)])
    return from_left, from_right


def by_head(array):
    return array.reshape(array.shape[:-1] + (HEADS, HEAD_DIM))


def gather_small(part):
    count = lax.axis_size("seq")
    spread = jnp.broadcast_to(part[None], (count,) + part.shape)
    return lax.all_to_all(spread, "seq", 0, 0)


def reduce_own(full):
    count = lax.axis_size("seq")
    split = full.reshape((count, full.shape[0] // count) + full.shape[1:])
    return jnp.sum(lax.all_to_all(split, "seq", 0, 0), axis=0)


def key_flags(first_pos, span_len, glob_pos, lens_wide):
    places = first_pos + jnp.arange(span_len, dtype=jnp.int32)
    begin = jnp.asarray(first_pos // BLOCK + 2 * REACH, dtype=jnp.int32)
    lens = lax.dynamic_slice_in_dim(lens_wide, begin, span_len // BLOCK)
    inside = (jnp.arange(BLOCK, dtype=jnp.int32)[None, :] < lens[:, None]).reshape(span_len)
    marked = jnp.any(glob_pos[:, None] == places[None, :], axis=0)
    return (inside, marked)


def band_kernel(mask_ref, gmask_ref, keep_ref, q_ref, do_ref, kw_ref, vw_ref, kg_ref, vg_ref,
                out_ref, dq_ref, dkw_ref, dvw_ref, dkg_ref, dvg_ref):
    scale = HEAD_DIM ** (-0.5)
    tile = pl.program_id(1)
    tile_rows = q_ref.shape[0]
    win_rows = mask_ref.shape[2]
    start = pl.multiple_of(tile * tile_rows, tile_rows)
    f32 = jnp.float32
    bf16 = jnp.bfloat16
    nt = (((1,), (1,)), ((), ()))
    tn = (((0,), (0,)), ((), ()))

    @pl.when(tile == 0)
    def _():
        dkw_ref[...] = jnp.zeros_like(dkw_ref)
        dvw_ref[...] = jnp.zeros_like(dvw_ref)
        dkg_ref[...] = jnp.zeros_like(dkg_ref)
        dvg_ref[...] = jnp.zeros_like(dvg_ref)

    band_bias = mask_ref[0]
    glob_bias = gmask_ref[...]
    keep = keep_ref[...].astype(bf16)
    for head in range(q_ref.shape[1] // HEAD_DIM):
        lanes = slice(head * HEAD_DIM, (head + 1) * HEAD_DIM)
        q = q_ref[:, lanes] * jnp.asarray(scale, bf16)
        do = do_ref[:, lanes] * keep
        kwin = kw_ref[pl.ds(start, win_rows), lanes]
        vwin = vw_ref[pl.ds(start, win_rows), lanes]
        kg = kg_ref[:, lanes]
        vg = vg_ref[:, lanes]
        s_b = lax.dot_general(q, kwin, nt, preferred_element_type=f32) + band_bias
        s_g = lax.dot_general(q, kg, nt, preferred_element_type=f32) + glob_bias
        top = jnp.maximum(jnp.max(s_b, axis=1, keepdims=True), jnp.max(s_g, axis=1, keepdims=True))
        e_b = jnp.exp(s_b - top)
        e_g = jnp.exp(s_g - top)
        inv = 1.0 / (jnp.sum(e_b, axis=1, keepdims=True) + jnp.sum(e_g, axis=1, keepdims=True))
        p_b = e_b * inv
        p_g = e_g * inv
        w_b = p_b.astype(bf16)
        w_g = p_g.astype(bf16)
        out = jnp.dot(w_b, vwin, preferred_element_type=f32) + jnp.dot(
            w_g, vg, preferred_element_type=f32
        )
        out_ref[:, lanes] = out
        delta = jnp.sum(
            do.astype(f32) * out.astype(bf16).astype(f32), axis=1, keepdims=True
        )
        dp_b = lax.dot_general(do, vwin, nt, preferred_element_type=f32)
        dp_g = lax.dot_general(do, vg, nt, preferred_element_type=f32)
        ds_b = (p_b * (dp_b - delta)).astype(bf16)
        ds_g = (p_g * (dp_g - delta)).astype(bf16)
        dq = jnp.dot(ds_b, kwin, preferred_element_type=f32) + jnp.dot(
            ds_g, kg, preferred_element_type=f32
        )
        dq_ref[:, lanes] = dq * scale
        dkw_ref[pl.ds(start, win_rows), lanes] += lax.dot_general(ds_b, q, tn, preferred_element_type=f32)
        dvw_ref[pl.ds(start, win_rows), lanes] += lax.dot_general(w_b, do, tn, preferred_element_type=f32)
        dkg_ref[:, lanes] += lax.dot_general(ds_g, q, tn, preferred_element_type=f32)
        dvg_ref[:, lanes] += lax.dot_general(w_g, do, tn, preferred_element_type=f32)


def band_call(mask, gmask, keep, queries, d_out, key_wide, value_wide, key_glob, value_glob, interpret=False):
    rows = queries.shape[0]
    wide_rows = key_wide.shape[0]
    slots = key_glob.shape[0]
    tiles, tile_rows, win_rows = mask.shape
    lanes = 2 * HEAD_DIM
    pairs = D // lanes
    f32 = jnp.float32
    row_spec = pl.BlockSpec((tile_rows, lanes), lambda p, t: (t, p))
    wide_spec = pl.BlockSpec((wide_rows, lanes), lambda p, t: (0, p))
    glob_spec = pl.BlockSpec((slots, lanes), lambda p, t: (0, p))
    return pl.pallas_call(
        band_kernel,
        grid=(pairs, tiles),
        in_specs=[
            pl.BlockSpec((1, tile_rows, win_rows), lambda p, t: (t, 0, 0)),
            pl.BlockSpec((1, slots), lambda p, t: (0, 0)),
            pl.BlockSpec((tile_rows, 1), lambda p, t: (t, 0)),
            row_spec,
            row_spec,
            wide_spec,
            wide_spec,
            glob_spec,
            glob_spec,
        ],
        out_specs=[row_spec, row_spec, wide_spec, wide_spec, glob_spec, glob_spec],
        out_shape=[
            jax.ShapeDtypeStruct((rows, D), f32),
            jax.ShapeDtypeStruct((rows, D), f32),
            jax.ShapeDtypeStruct((wide_rows, D), f32),
            jax.ShapeDtypeStruct((wide_rows, D), f32),
            jax.ShapeDtypeStruct((slots, D), f32),
            jax.ShapeDtypeStruct((slots, D), f32),
        ],
        compiler_params=pltpu.CompilerParams(dimension_semantics=("arbitrary", "arbitrary")),
        interpret=interpret,
    )(mask, gmask, keep, queries, d_out, key_wide, value_wide, key_glob, value_glob)


def band_kernel_t(mask_ref, gmask_ref, keep_ref, keep_row_ref, q_ref, qt_ref, do_ref, dot_ref,
                  kw_ref, kt_ref, vw_ref, vt_ref, kg_ref, kgt_ref, vg_ref, vgt_ref,
                  out_ref, dq_ref, dkw_ref, dvw_ref, dkg_ref, dvg_ref):
    scale = HEAD_DIM ** (-0.5)
    tile = pl.program_id(1)
    tile_rows = q_ref.shape[0]
    win_rows = mask_ref.shape[1]
    start = pl.multiple_of(tile * tile_rows, tile_rows)
    f32 = jnp.float32
    bf16 = jnp.bfloat16

    @pl.when(tile == 0)
    def _():
        dkw_ref[...] = jnp.zeros_like(dkw_ref)
        dvw_ref[...] = jnp.zeros_like(dvw_ref)
        dkg_ref[...] = jnp.zeros_like(dkg_ref)
        dvg_ref[...] = jnp.zeros_like(dvg_ref)

    band_bias = mask_ref[0]
    glob_bias = gmask_ref[...]
    keep = keep_ref[...].astype(bf16)
    keep_row = keep_row_ref[...].astype(bf16)
    shrink = jnp.asarray(scale, bf16)
    for head in range(q_ref.shape[1] // HEAD_DIM):
        lanes = slice(head * HEAD_DIM, (head + 1) * HEAD_DIM)
        q = q_ref[:, lanes] * shrink
        qt = qt_ref[lanes, :] * shrink
        do = do_ref[:, lanes] * keep
        dot = dot_ref[lanes, :] * keep_row
        kwin = kw_ref[pl.ds(start, win_rows), lanes]
        ktwin = kt_ref[lanes, pl.ds(start, win_rows)]
        vwin = vw_ref[pl.ds(start, win_rows), lanes]
        vtwin = vt_ref[lanes, pl.ds(start, win_rows)]
        kg = kg_ref[:, lanes]
        kgt = kgt_ref[lanes, :]
        vg = vg_ref[:, lanes]
        vgt = vgt_ref[lanes, :]
        s_b = jnp.dot(kwin, qt, preferred_element_type=f32) + band_bias
        s_g = jnp.dot(kg, qt, preferred_element_type=f32) + glob_bias
        top = jnp.maximum(jnp.max(s_b, axis=0, keepdims=True), jnp.max(s_g, axis=0, keepdims=True))
        e_b = jnp.exp(s_b - top)
        e_g = jnp.exp(s_g - top)
        inv = 1.0 / (jnp.sum(e_b, axis=0, keepdims=True) + jnp.sum(e_g, axis=0, keepdims=True))
        p_b = e_b * inv
        p_g = e_g * inv
        w_b = p_b.astype(bf16)
        w_g = p_g.astype(bf16)
        out = jnp.dot(vtwin, w_b, preferred_element_type=f32) + jnp.dot(
            vgt, w_g, preferred_element_type=f32
        )
        out_ref[lanes, :] = out
        delta = jnp.sum(
            dot.astype(f32) * out.astype(bf16).astype(f32), axis=0, keepdims=True
        )
        dp_b = jnp.dot(vwin, dot, preferred_element_type=f32)
        dp_g = jnp.dot(vg, dot, preferred_element_type=f32)
        ds_b = (p_b * (dp_b - delta)).astype(bf16)
        ds_g = (p_g * (dp_g - delta)).astype(bf16)
        dq = jnp.dot(ktwin, ds_b, preferred_element_type=f32) + jnp.dot(
            kgt, ds_g, preferred_element_type=f32
        )
        dq_ref[lanes, :] = dq * scale
        dkw_ref[pl.ds(start, win_rows), lanes] += jnp.dot(ds_b, q, preferred_element_type=f32)
        dvw_ref[pl.ds(start, win_rows), lanes] += jnp.dot(w_b, do, preferred_element_type=f32)
        dkg_ref[:, lanes] += jnp.dot(ds_g, q, preferred_element_type=f32)
        dvg_ref[:, lanes] += jnp.dot(w_g, do, preferred_element_type=f32)


def band_call_t(mask, gmask, keep, queries, d_out, key_wide, value_wide, key_glob, value_glob, key_wide_t=None, value_wide_t=None, interpret=False):
    rows = queries.shape[0]
    wide_rows = key_wide.shape[0]
    slots = key_glob.shape[0]
    tiles, tile_rows, win_rows = mask.shape
    lanes = 2 * HEAD_DIM
    pairs = D // lanes
    f32 = jnp.float32
    row_spec = pl.BlockSpec((tile_rows, lanes), lambda p, t: (t, p))
    col_spec = pl.BlockSpec((lanes, tile_rows), lambda p, t: (p, t))
    wide_spec = pl.BlockSpec((wide_rows, lanes), lambda p, t: (0, p))
    wide_t_spec = pl.BlockSpec((lanes, wide_rows), lambda p, t: (p, 0))
    glob_spec = pl.BlockSpec((slots, lanes), lambda p, t: (0, p))
    glob_t_spec = pl.BlockSpec((lanes, slots), lambda p, t: (p, 0))
    out_t, dq_t, dkw, dvw, dkg, dvg = pl.pallas_call(
        band_kernel_t,
        grid=(pairs, tiles),
        in_specs=[
            pl.BlockSpec((1, win_rows, tile_rows), lambda p, t: (t, 0, 0)),
            pl.BlockSpec((slots, 1), lambda p, t: (0, 0)),
            pl.BlockSpec((tile_rows, 1), lambda p, t: (t, 0)),
            pl.BlockSpec((1, tile_rows), lambda p, t: (0, t)),
            row_spec,
            col_spec,
            row_spec,
            col_spec,
            wide_spec,
            wide_t_spec,
            wide_spec,
            wide_t_spec,
            glob_spec,
            glob_t_spec,
            glob_spec,
            glob_t_spec,
        ],
        out_specs=[col_spec, col_spec, wide_spec, wide_spec, glob_spec, glob_spec],
        out_shape=[
            jax.ShapeDtypeStruct((D, rows), f32),
            jax.ShapeDtypeStruct((D, rows), f32),
            jax.ShapeDtypeStruct((wide_rows, D), f32),
            jax.ShapeDtypeStruct((wide_rows, D), f32),
            jax.ShapeDtypeStruct((slots, D), f32),
            jax.ShapeDtypeStruct((slots, D), f32),
        ],
        compiler_params=pltpu.CompilerParams(dimension_semantics=("arbitrary", "arbitrary")),
        interpret=interpret,
    )(
        jnp.transpose(mask, (0, 2, 1)),
        jnp.transpose(gmask),
        keep,
        jnp.transpose(keep),
        queries,
        jnp.transpose(queries),
        d_out,
        jnp.transpose(d_out),
        key_wide,
        jnp.transpose(key_wide) if key_wide_t is None else key_wide_t,
        value_wide,
        jnp.transpose(value_wide) if value_wide_t is None else value_wide_t,
        key_glob,
        jnp.transpose(key_glob),
        value_glob,
        jnp.transpose(value_glob),
    )
    return jnp.transpose(out_t), jnp.transpose(dq_t), dkw, dvw, dkg, dvg


def local(queries, keys, values, d_out, glob_pos, block_len):
    scale = HEAD_DIM ** (-0.5)
    rows = queries.shape[0]
    reach_rows = REACH * BLOCK
    tile_rows = TILE_BLOCKS * BLOCK
    tiles = rows // tile_rows
    win_rows = tile_rows + 2 * reach_rows
    wide_rows = rows + 2 * reach_rows
    first_row = lax.axis_index("seq") * rows
    lens_wide = jnp.pad(block_len, 2 * REACH)

    places = first_row + jnp.arange(rows, dtype=jnp.int32)
    marked_rows = jnp.any(glob_pos[:, None] == places[None, :], axis=0)
    local_pos = glob_pos - first_row
    is_local = (local_pos >= 0) & (local_pos < rows)
    local_index = jnp.where(is_local, local_pos, rows)
    inside_rows, _ = key_flags(first_row, rows, glob_pos, lens_wide)

    count = lax.axis_size("seq")
    own_blocks = rows // BLOCK
    slots = own_blocks * count
    glob_block = glob_pos // BLOCK
    slot_valid = jnp.zeros((slots,), bool).at[glob_block].set(True, mode="drop")
    own_slot = lax.axis_index("seq") * own_blocks + jnp.arange(own_blocks, dtype=jnp.int32)
    own_match = glob_block[None, :] == own_slot[:, None]
    own_has = jnp.any(own_match, axis=1)
    own_pos = jnp.sum(jnp.where(own_match, glob_pos[None, :], 0), axis=1) - first_row
    own_offset = own_pos - BLOCK * jnp.arange(own_blocks, dtype=jnp.int32)
    own_row = own_has[:, None] & (jnp.arange(BLOCK, dtype=jnp.int32)[None, :] == own_offset[:, None])

    def place(base, extra):
        shaped = base.reshape(own_blocks, BLOCK, D)
        return jnp.where(own_row[:, :, None], shaped + extra[:, None, :], shaped).reshape(rows, D)

    own_pick = (
        own_has[:, None] & (jnp.arange(rows, dtype=jnp.int32)[None, :] == own_pos[:, None])
    ).astype(jnp.bfloat16)
    picked = jnp.stack(
        [
            jnp.dot(own_pick, source, preferred_element_type=jnp.float32).astype(jnp.bfloat16)
            for source in (queries, keys, values, d_out)
        ]
    )
    shared = jnp.transpose(gather_small(picked), (1, 0, 2, 3)).reshape(4, slots, D)
    qg = to_heads(shared[0])
    kg = to_heads(shared[1])
    vg = to_heads(shared[2])
    dog = to_heads(shared[3])

    pair = jnp.stack([keys, values])
    from_left, from_right = halo(pair, reach_rows)
    pair_wide = jnp.concatenate([from_left, pair, from_right], axis=1)
    k_h = to_heads(keys)
    v_h = to_heads(values)

    inside_wide, marked_wide = key_flags(first_row - reach_rows, wide_rows, glob_pos, lens_wide)
    allowed_wide = inside_wide & jnp.logical_not(marked_wide)

    allowed_t = jnp.stack(
        [lax.slice_in_dim(allowed_wide, t * tile_rows, t * tile_rows + win_rows) for t in range(tiles)]
    )
    q_block = (jnp.arange(rows, dtype=jnp.int32) // BLOCK).reshape(tiles, tile_rows)
    k_block = jnp.stack(
        [t * TILE_BLOCKS + jnp.arange(win_rows, dtype=jnp.int32) // BLOCK - REACH for t in range(tiles)]
    )
    near = jnp.abs(q_block[:, :, None] - k_block[:, None, :]) <= REACH
    band_mask = near & allowed_t[:, None, :]
    band_out, band_dq, dk_wide, dv_wide, dk_glob, dv_glob = band_call_t(
        jnp.where(band_mask, 0.0, neg_large).astype(jnp.float32),
        jnp.where(slot_valid, 0.0, neg_large).astype(jnp.float32)[None, :],
        jnp.logical_not(marked_rows).astype(jnp.float32)[:, None],
        queries,
        d_out,
        pair_wide[0],
        pair_wide[1],
        shared[1],
        shared[2],
        jnp.concatenate([jnp.transpose(from_left[0]), jnp.transpose(keys), jnp.transpose(from_right[0])], axis=1),
        jnp.concatenate([jnp.transpose(from_left[1]), jnp.transpose(values), jnp.transpose(from_right[1])], axis=1),
    )

    g_score = mixed("hge,hre->hgr", qg, k_h) * scale
    g_score = jnp.where(inside_rows[None, None, :], g_score, neg_large)
    g_top = jnp.max(g_score, axis=-1)
    g_sum = jnp.sum(jnp.exp(g_score - g_top[..., None]), axis=-1)
    stats = gather_small(jnp.stack([g_top, g_sum]))
    all_top = stats[:, 0]
    top_glob = jnp.max(all_top, axis=0)
    sum_glob = jnp.sum(stats[:, 1] * jnp.exp(all_top - top_glob[None]), axis=0)
    lse_glob = top_glob + jnp.log(sum_glob)
    g_prob = jnp.where(slot_valid[None, :, None], jnp.exp(g_score - lse_glob[..., None]), 0.0)
    g_weight = g_prob.astype(jnp.bfloat16)
    out_own = reduce_own(from_heads(mixed("hgr,hre->hge", g_weight, v_h)))
    out_own16 = out_own.astype(jnp.bfloat16)
    delta_own = jnp.sum(
        by_head(picked[3]).astype(jnp.float32) * by_head(out_own16).astype(jnp.float32), axis=-1
    )
    delta_g = jnp.transpose(gather_small(delta_own).reshape(slots, HEADS))
    band_out16 = band_out.astype(jnp.bfloat16)
    out_full = jnp.where(
        own_row[:, :, None], out_own16[:, None, :], band_out16.reshape(own_blocks, BLOCK, D)
    ).reshape(rows, D)

    grad_wide = jnp.stack([dk_wide, dv_wide])
    rims = jnp.concatenate(
        [grad_wide[:, :reach_rows], grad_wide[:, wide_rows - reach_rows :]], axis=1
    )
    back_left, back_right = halo(rims, reach_rows)
    center = grad_wide[:, reach_rows : reach_rows + rows]
    center = center.at[:, :reach_rows].add(back_left).at[:, rows - reach_rows :].add(back_right)

    g_dprob = mixed("hge,hre->hgr", dog, v_h)
    g_dscore = (g_prob * (g_dprob - delta_g[..., None])).astype(jnp.bfloat16)
    row_dq = mixed("hgr,hre->hge", g_dscore, k_h) * scale
    part_dk = mixed("hgr,hge->hre", g_dscore, qg) * scale
    part_dv = mixed("hgr,hge->hre", g_weight, dog)

    totals = reduce_own(
        jnp.concatenate([from_heads(row_dq), dk_glob, dv_glob], axis=1)
    )
    d_queries = place(band_dq, totals[:, :D])
    d_keys = place(center[0] + from_heads(part_dk), totals[:, D : 2 * D])
    d_values = place(center[1] + from_heads(part_dv), totals[:, 2 * D :])
    return (
        out_full,
        d_queries.astype(jnp.bfloat16),
        d_keys.astype(jnp.bfloat16),
        d_values.astype(jnp.bfloat16),
    )


def solution(mesh):
    rows = P(("groups", "seq"), None)
    return jax.shard_map(
        local,
        mesh=mesh,
        in_specs=(rows, rows, rows, rows, P("groups"), P("groups")),
        out_specs=(rows, rows, rows, rows),
        check_vma=False,
    )
```

```python
import jax
import jax.numpy as jnp
from jax import lax
from jax.sharding import PartitionSpec as P
from jax.experimental import pallas as pl
from jax.experimental.pallas import tpu as pltpu

D = 768
HEADS = 12
BLOCK = 64
REACH = 3
GLOBALS = 128
HEAD_DIM = 64
TILE_BLOCKS = 2

neg_large = -1e30


def mixed(form, left, right):
    return jnp.einsum(form, left, right, preferred_element_type=jnp.float32)


def to_heads(array):
    rows = array.shape[0]
    return jnp.transpose(array.reshape(rows, HEADS, HEAD_DIM), (1, 0, 2))


def from_heads(array):
    rows = array.shape[1]
    return jnp.transpose(array, (1, 0, 2)).reshape(rows, D)


def halo(cells, width):
    count = lax.axis_size("seq")
    ends = count - 1
    head = lax.slice_in_dim(cells, 0, width, axis=1)
    tail = lax.slice_in_dim(cells, cells.shape[1] - width, cells.shape[1], axis=1)
    from_left = lax.ppermute(tail, "seq", [(i, i + 1) for i in range(ends)])
    from_right = lax.ppermute(head, "seq", [(i + 1, i) for i in range(ends)])
    return from_left, from_right


def by_head(array):
    return array.reshape(array.shape[:-1] + (HEADS, HEAD_DIM))


def gather_small(part):
    count = lax.axis_size("seq")
    spread = jnp.broadcast_to(part[None], (count,) + part.shape)
    return lax.all_to_all(spread, "seq", 0, 0)


def reduce_own(full):
    count = lax.axis_size("seq")
    split = full.reshape((count, full.shape[0] // count) + full.shape[1:])
    return jnp.sum(lax.all_to_all(split, "seq", 0, 0), axis=0)


def key_flags(first_pos, span_len, glob_pos, lens_wide):
    places = first_pos + jnp.arange(span_len, dtype=jnp.int32)
    begin = jnp.asarray(first_pos // BLOCK + 2 * REACH, dtype=jnp.int32)
    lens = lax.dynamic_slice_in_dim(lens_wide, begin, span_len // BLOCK)
    inside = (jnp.arange(BLOCK, dtype=jnp.int32)[None, :] < lens[:, None]).reshape(span_len)
    marked = jnp.any(glob_pos[:, None] == places[None, :], axis=0)
    return (inside, marked)


def band_kernel(mask_ref, gmask_ref, keep_ref, q_ref, do_ref, kw_ref, vw_ref, kg_ref, vg_ref,
                out_ref, dq_ref, dkw_ref, dvw_ref, dkg_ref, dvg_ref):
    scale = HEAD_DIM ** (-0.5)
    tile = pl.program_id(1)
    tile_rows = q_ref.shape[0]
    win_rows = mask_ref.shape[2]
    start = pl.multiple_of(tile * tile_rows, tile_rows)
    f32 = jnp.float32
    bf16 = jnp.bfloat16
    nt = (((1,), (1,)), ((), ()))
    tn = (((0,), (0,)), ((), ()))

    @pl.when(tile == 0)
    def _():
        dkw_ref[...] = jnp.zeros_like(dkw_ref)
        dvw_ref[...] = jnp.zeros_like(dvw_ref)
        dkg_ref[...] = jnp.zeros_like(dkg_ref)
        dvg_ref[...] = jnp.zeros_like(dvg_ref)

    band_bias = mask_ref[0]
    glob_bias = gmask_ref[...]
    keep = keep_ref[...].astype(bf16)
    for head in range(q_ref.shape[1] // HEAD_DIM):
        lanes = slice(head * HEAD_DIM, (head + 1) * HEAD_DIM)
        q = q_ref[:, lanes] * jnp.asarray(scale, bf16)
        do = do_ref[:, lanes] * keep
        kwin = kw_ref[pl.ds(start, win_rows), lanes]
        vwin = vw_ref[pl.ds(start, win_rows), lanes]
        kg = kg_ref[:, lanes]
        vg = vg_ref[:, lanes]
        s_b = lax.dot_general(q, kwin, nt, preferred_element_type=f32) + band_bias
        s_g = lax.dot_general(q, kg, nt, preferred_element_type=f32) + glob_bias
        top = jnp.maximum(jnp.max(s_b, axis=1, keepdims=True), jnp.max(s_g, axis=1, keepdims=True))
        e_b = jnp.exp(s_b - top)
        e_g = jnp.exp(s_g - top)
        inv = 1.0 / (jnp.sum(e_b, axis=1, keepdims=True) + jnp.sum(e_g, axis=1, keepdims=True))
        p_b = e_b * inv
        p_g = e_g * inv
        w_b = p_b.astype(bf16)
        w_g = p_g.astype(bf16)
        out = jnp.dot(w_b, vwin, preferred_element_type=f32) + jnp.dot(
            w_g, vg, preferred_element_type=f32
        )
        out_ref[:, lanes] = out
        delta = jnp.sum(
            do.astype(f32) * out.astype(bf16).astype(f32), axis=1, keepdims=True
        )
        dp_b = lax.dot_general(do, vwin, nt, preferred_element_type=f32)
        dp_g = lax.dot_general(do, vg, nt, preferred_element_type=f32)
        ds_b = (p_b * (dp_b - delta)).astype(bf16)
        ds_g = (p_g * (dp_g - delta)).astype(bf16)
        dq = jnp.dot(ds_b, kwin, preferred_element_type=f32) + jnp.dot(
            ds_g, kg, preferred_element_type=f32
        )
        dq_ref[:, lanes] = dq * scale
        dkw_ref[pl.ds(start, win_rows), lanes] += lax.dot_general(ds_b, q, tn, preferred_element_type=f32)
        dvw_ref[pl.ds(start, win_rows), lanes] += lax.dot_general(w_b, do, tn, preferred_element_type=f32)
        dkg_ref[:, lanes] += lax.dot_general(ds_g, q, tn, preferred_element_type=f32)
        dvg_ref[:, lanes] += lax.dot_general(w_g, do, tn, preferred_element_type=f32)


def band_call(mask, gmask, keep, queries, d_out, key_wide, value_wide, key_glob, value_glob, interpret=False):
    rows = queries.shape[0]
    wide_rows = key_wide.shape[0]
    slots = key_glob.shape[0]
    tiles, tile_rows, win_rows = mask.shape
    lanes = 2 * HEAD_DIM
    pairs = D // lanes
    f32 = jnp.float32
    row_spec = pl.BlockSpec((tile_rows, lanes), lambda p, t: (t, p))
    wide_spec = pl.BlockSpec((wide_rows, lanes), lambda p, t: (0, p))
    glob_spec = pl.BlockSpec((slots, lanes), lambda p, t: (0, p))
    return pl.pallas_call(
        band_kernel,
        grid=(pairs, tiles),
        in_specs=[
            pl.BlockSpec((1, tile_rows, win_rows), lambda p, t: (t, 0, 0)),
            pl.BlockSpec((1, slots), lambda p, t: (0, 0)),
            pl.BlockSpec((tile_rows, 1), lambda p, t: (t, 0)),
            row_spec,
            row_spec,
            wide_spec,
            wide_spec,
            glob_spec,
            glob_spec,
        ],
        out_specs=[row_spec, row_spec, wide_spec, wide_spec, glob_spec, glob_spec],
        out_shape=[
            jax.ShapeDtypeStruct((rows, D), f32),
            jax.ShapeDtypeStruct((rows, D), f32),
            jax.ShapeDtypeStruct((wide_rows, D), f32),
            jax.ShapeDtypeStruct((wide_rows, D), f32),
            jax.ShapeDtypeStruct((slots, D), f32),
            jax.ShapeDtypeStruct((slots, D), f32),
        ],
        compiler_params=pltpu.CompilerParams(dimension_semantics=("arbitrary", "arbitrary")),
        interpret=interpret,
    )(mask, gmask, keep, queries, d_out, key_wide, value_wide, key_glob, value_glob)


def band_kernel_t(mask_ref, gmask_ref, keep_ref, keep_row_ref, q_ref, qt_ref, do_ref, dot_ref,
                  kw_ref, kt_ref, vw_ref, vt_ref, kg_ref, kgt_ref, vg_ref, vgt_ref,
                  out_ref, dq_ref, dkw_ref, dvw_ref, dkg_ref, dvg_ref):
    scale = HEAD_DIM ** (-0.5)
    tile = pl.program_id(1)
    tile_rows = q_ref.shape[0]
    win_rows = mask_ref.shape[1]
    start = pl.multiple_of(tile * tile_rows, tile_rows)
    f32 = jnp.float32
    bf16 = jnp.bfloat16

    @pl.when(tile == 0)
    def _():
        dkw_ref[...] = jnp.zeros_like(dkw_ref)
        dvw_ref[...] = jnp.zeros_like(dvw_ref)
        dkg_ref[...] = jnp.zeros_like(dkg_ref)
        dvg_ref[...] = jnp.zeros_like(dvg_ref)

    band_bias = mask_ref[0]
    glob_bias = gmask_ref[...]
    keep = keep_ref[...].astype(bf16)
    keep_row = keep_row_ref[...].astype(bf16)
    shrink = jnp.asarray(scale, bf16)
    for head in range(q_ref.shape[1] // HEAD_DIM):
        lanes = slice(head * HEAD_DIM, (head + 1) * HEAD_DIM)
        q = q_ref[:, lanes] * shrink
        qt = qt_ref[lanes, :] * shrink
        do = do_ref[:, lanes] * keep
        dot = dot_ref[lanes, :] * keep_row
        kwin = kw_ref[pl.ds(start, win_rows), lanes]
        ktwin = kt_ref[lanes, pl.ds(start, win_rows)]
        vwin = vw_ref[pl.ds(start, win_rows), lanes]
        vtwin = vt_ref[lanes, pl.ds(start, win_rows)]
        kg = kg_ref[:, lanes]
        kgt = kgt_ref[lanes, :]
        vg = vg_ref[:, lanes]
        vgt = vgt_ref[lanes, :]
        s_b = jnp.dot(kwin, qt, preferred_element_type=f32) + band_bias
        s_g = jnp.dot(kg, qt, preferred_element_type=f32) + glob_bias
        top = jnp.maximum(jnp.max(s_b, axis=0, keepdims=True), jnp.max(s_g, axis=0, keepdims=True))
        e_b = jnp.exp(s_b - top)
        e_g = jnp.exp(s_g - top)
        inv = 1.0 / (jnp.sum(e_b, axis=0, keepdims=True) + jnp.sum(e_g, axis=0, keepdims=True))
        p_b = e_b * inv
        p_g = e_g * inv
        w_b = p_b.astype(bf16)
        w_g = p_g.astype(bf16)
        out = jnp.dot(vtwin, w_b, preferred_element_type=f32) + jnp.dot(
            vgt, w_g, preferred_element_type=f32
        )
        out_ref[lanes, :] = out
        delta = jnp.sum(
            dot.astype(f32) * out.astype(bf16).astype(f32), axis=0, keepdims=True
        )
        dp_b = jnp.dot(vwin, dot, preferred_element_type=f32)
        dp_g = jnp.dot(vg, dot, preferred_element_type=f32)
        ds_b = (p_b * (dp_b - delta)).astype(bf16)
        ds_g = (p_g * (dp_g - delta)).astype(bf16)
        dq = jnp.dot(ktwin, ds_b, preferred_element_type=f32) + jnp.dot(
            kgt, ds_g, preferred_element_type=f32
        )
        dq_ref[lanes, :] = dq * scale
        dkw_ref[pl.ds(start, win_rows), lanes] += jnp.dot(ds_b, q, preferred_element_type=f32)
        dvw_ref[pl.ds(start, win_rows), lanes] += jnp.dot(w_b, do, preferred_element_type=f32)
        dkg_ref[:, lanes] += jnp.dot(ds_g, q, preferred_element_type=f32)
        dvg_ref[:, lanes] += jnp.dot(w_g, do, preferred_element_type=f32)


def band_call_t(mask, gmask, keep, queries, d_out, key_wide, value_wide, key_glob, value_glob, interpret=False):
    rows = queries.shape[0]
    wide_rows = key_wide.shape[0]
    slots = key_glob.shape[0]
    tiles, tile_rows, win_rows = mask.shape
    lanes = 2 * HEAD_DIM
    pairs = D // lanes
    f32 = jnp.float32
    row_spec = pl.BlockSpec((tile_rows, lanes), lambda p, t: (t, p))
    col_spec = pl.BlockSpec((lanes, tile_rows), lambda p, t: (p, t))
    wide_spec = pl.BlockSpec((wide_rows, lanes), lambda p, t: (0, p))
    wide_t_spec = pl.BlockSpec((lanes, wide_rows), lambda p, t: (p, 0))
    glob_spec = pl.BlockSpec((slots, lanes), lambda p, t: (0, p))
    glob_t_spec = pl.BlockSpec((lanes, slots), lambda p, t: (p, 0))
    out_t, dq_t, dkw, dvw, dkg, dvg = pl.pallas_call(
        band_kernel_t,
        grid=(pairs, tiles),
        in_specs=[
            pl.BlockSpec((1, win_rows, tile_rows), lambda p, t: (t, 0, 0)),
            pl.BlockSpec((slots, 1), lambda p, t: (0, 0)),
            pl.BlockSpec((tile_rows, 1), lambda p, t: (t, 0)),
            pl.BlockSpec((1, tile_rows), lambda p, t: (0, t)),
            row_spec,
            col_spec,
            row_spec,
            col_spec,
            wide_spec,
            wide_t_spec,
            wide_spec,
            wide_t_spec,
            glob_spec,
            glob_t_spec,
            glob_spec,
            glob_t_spec,
        ],
        out_specs=[col_spec, col_spec, wide_spec, wide_spec, glob_spec, glob_spec],
        out_shape=[
            jax.ShapeDtypeStruct((D, rows), f32),
            jax.ShapeDtypeStruct((D, rows), f32),
            jax.ShapeDtypeStruct((wide_rows, D), f32),
            jax.ShapeDtypeStruct((wide_rows, D), f32),
            jax.ShapeDtypeStruct((slots, D), f32),
            jax.ShapeDtypeStruct((slots, D), f32),
        ],
        compiler_params=pltpu.CompilerParams(dimension_semantics=("arbitrary", "arbitrary")),
        interpret=interpret,
    )(
        jnp.transpose(mask, (0, 2, 1)),
        jnp.transpose(gmask),
        keep,
        jnp.transpose(keep),
        queries,
        jnp.transpose(queries),
        d_out,
        jnp.transpose(d_out),
        key_wide,
        jnp.transpose(key_wide),
        value_wide,
        jnp.transpose(value_wide),
        key_glob,
        jnp.transpose(key_glob),
        value_glob,
        jnp.transpose(value_glob),
    )
    return jnp.transpose(out_t), jnp.transpose(dq_t), dkw, dvw, dkg, dvg


def glob_row_kernel(bias_ref, lse_ref, delta_ref, qg_ref, dog_ref, k_ref, v_ref, dq_ref, dk_ref, dv_ref):
    scale = HEAD_DIM ** (-0.5)
    pair = pl.program_id(0)
    f32 = jnp.float32
    bf16 = jnp.bfloat16
    bias = bias_ref[...]
    heads = qg_ref.shape[1] // HEAD_DIM
    for head in range(heads):
        lanes = slice(head * HEAD_DIM, (head + 1) * HEAD_DIM)
        row = pl.ds(pair * heads + head, 1)
        qg_wide = qg_ref[:, lanes].astype(f32) * scale
        dog_wide = dog_ref[:, lanes].astype(f32)
        qg = qg_wide.astype(bf16)
        qgt = jnp.transpose(qg_wide).astype(bf16)
        dog = dog_wide.astype(bf16)
        dogt = jnp.transpose(dog_wide).astype(bf16)
        k = k_ref[:, lanes]
        kt = jnp.transpose(k.astype(f32)).astype(bf16)
        v = v_ref[:, lanes]
        s = jnp.dot(k, qgt, preferred_element_type=f32) + bias
        p = jnp.exp(s - lse_ref[row, :])
        w = p.astype(bf16)
        dp = jnp.dot(v, dogt, preferred_element_type=f32)
        ds = (p * (dp - delta_ref[row, :])).astype(bf16)
        dq_t = jnp.dot(kt, ds, preferred_element_type=f32)
        dq_ref[:, lanes] = jnp.transpose(dq_t) * scale
        dk_ref[:, lanes] = jnp.dot(ds, qg, preferred_element_type=f32)
        dv_ref[:, lanes] = jnp.dot(w, dog, preferred_element_type=f32)


def glob_row_call(bias, lse, delta, query_glob, dout_glob, keys, values):
    rows = keys.shape[0]
    slots = query_glob.shape[0]
    lanes = 2 * HEAD_DIM
    f32 = jnp.float32
    glob_spec = pl.BlockSpec((slots, lanes), lambda p: (0, p))
    row_spec = pl.BlockSpec((rows, lanes), lambda p: (0, p))
    return pl.pallas_call(
        glob_row_kernel,
        grid=(D // lanes,),
        in_specs=[
            pl.BlockSpec((rows, 1), lambda p: (0, 0)),
            pl.BlockSpec((HEADS, slots), lambda p: (0, 0)),
            pl.BlockSpec((HEADS, slots), lambda p: (0, 0)),
            glob_spec,
            glob_spec,
            row_spec,
            row_spec,
        ],
        out_specs=[glob_spec, row_spec, row_spec],
        out_shape=[
            jax.ShapeDtypeStruct((slots, D), f32),
            jax.ShapeDtypeStruct((rows, D), f32),
            jax.ShapeDtypeStruct((rows, D), f32),
        ],
        compiler_params=pltpu.CompilerParams(dimension_semantics=("arbitrary",)),
    )(bias, lse, delta, query_glob, dout_glob, keys, values)


def local(queries, keys, values, d_out, glob_pos, block_len):
    scale = HEAD_DIM ** (-0.5)
    rows = queries.shape[0]
    reach_rows = REACH * BLOCK
    tile_rows = TILE_BLOCKS * BLOCK
    tiles = rows // tile_rows
    win_rows = tile_rows + 2 * reach_rows
    wide_rows = rows + 2 * reach_rows
    first_row = lax.axis_index("seq") * rows
    lens_wide = jnp.pad(block_len, 2 * REACH)

    places = first_row + jnp.arange(rows, dtype=jnp.int32)
    marked_rows = jnp.any(glob_pos[:, None] == places[None, :], axis=0)
    local_pos = glob_pos - first_row
    is_local = (local_pos >= 0) & (local_pos < rows)
    local_index = jnp.where(is_local, local_pos, rows)
    inside_rows, _ = key_flags(first_row, rows, glob_pos, lens_wide)

    count = lax.axis_size("seq")
    own_blocks = rows // BLOCK
    slots = own_blocks * count
    glob_block = glob_pos // BLOCK
    slot_valid = jnp.zeros((slots,), bool).at[glob_block].set(True, mode="drop")
    own_slot = lax.axis_index("seq") * own_blocks + jnp.arange(own_blocks, dtype=jnp.int32)
    own_match = glob_block[None, :] == own_slot[:, None]
    own_has = jnp.any(own_match, axis=1)
    own_pos = jnp.sum(jnp.where(own_match, glob_pos[None, :], 0), axis=1) - first_row
    own_offset = own_pos - BLOCK * jnp.arange(own_blocks, dtype=jnp.int32)
    own_row = own_has[:, None] & (jnp.arange(BLOCK, dtype=jnp.int32)[None, :] == own_offset[:, None])

    def place(base, extra):
        shaped = base.reshape(own_blocks, BLOCK, D)
        return jnp.where(own_row[:, :, None], shaped + extra[:, None, :], shaped).reshape(rows, D)

    own_pick = (
        own_has[:, None] & (jnp.arange(rows, dtype=jnp.int32)[None, :] == own_pos[:, None])
    ).astype(jnp.bfloat16)
    picked = jnp.stack(
        [
            jnp.dot(own_pick, source, preferred_element_type=jnp.float32).astype(jnp.bfloat16)
            for source in (queries, keys, values, d_out)
        ]
    )
    shared = jnp.transpose(gather_small(picked), (1, 0, 2, 3)).reshape(4, slots, D)
    qg = to_heads(shared[0])
    kg = to_heads(shared[1])
    vg = to_heads(shared[2])
    dog = to_heads(shared[3])

    pair = jnp.stack([keys, values])
    from_left, from_right = halo(pair, reach_rows)
    pair_wide = jnp.concatenate([from_left, pair, from_right], axis=1)
    k_h = to_heads(keys)
    v_h = to_heads(values)

    inside_wide, marked_wide = key_flags(first_row - reach_rows, wide_rows, glob_pos, lens_wide)
    allowed_wide = inside_wide & jnp.logical_not(marked_wide)

    allowed_t = jnp.stack(
        [lax.slice_in_dim(allowed_wide, t * tile_rows, t * tile_rows + win_rows) for t in range(tiles)]
    )
    q_block = (jnp.arange(rows, dtype=jnp.int32) // BLOCK).reshape(tiles, tile_rows)
    k_block = jnp.stack(
        [t * TILE_BLOCKS + jnp.arange(win_rows, dtype=jnp.int32) // BLOCK - REACH for t in range(tiles)]
    )
    near = jnp.abs(q_block[:, :, None] - k_block[:, None, :]) <= REACH
    band_mask = near & allowed_t[:, None, :]
    band_out, band_dq, dk_wide, dv_wide, dk_glob, dv_glob = band_call_t(
        jnp.where(band_mask, 0.0, neg_large).astype(jnp.float32),
        jnp.where(slot_valid, 0.0, neg_large).astype(jnp.float32)[None, :],
        jnp.logical_not(marked_rows).astype(jnp.float32)[:, None],
        queries,
        d_out,
        pair_wide[0],
        pair_wide[1],
        shared[1],
        shared[2],
    )

    g_score = mixed("hge,hre->hgr", qg, k_h) * scale
    g_score = jnp.where(inside_rows[None, None, :], g_score, neg_large)
    g_top = jnp.max(g_score, axis=-1)
    g_sum = jnp.sum(jnp.exp(g_score - g_top[..., None]), axis=-1)
    stats = gather_small(jnp.stack([g_top, g_sum]))
    all_top = stats[:, 0]
    top_glob = jnp.max(all_top, axis=0)
    sum_glob = jnp.sum(stats[:, 1] * jnp.exp(all_top - top_glob[None]), axis=0)
    lse_glob = top_glob + jnp.log(sum_glob)
    g_prob = jnp.where(slot_valid[None, :, None], jnp.exp(g_score - lse_glob[..., None]), 0.0)
    g_weight = g_prob.astype(jnp.bfloat16)
    out_own = reduce_own(from_heads(mixed("hgr,hre->hge", g_weight, v_h)))
    out_own16 = out_own.astype(jnp.bfloat16)
    delta_own = jnp.sum(
        by_head(picked[3]).astype(jnp.float32) * by_head(out_own16).astype(jnp.float32), axis=-1
    )
    delta_g = jnp.transpose(gather_small(delta_own).reshape(slots, HEADS))
    band_out16 = band_out.astype(jnp.bfloat16)
    out_full = jnp.where(
        own_row[:, :, None], out_own16[:, None, :], band_out16.reshape(own_blocks, BLOCK, D)
    ).reshape(rows, D)

    grad_wide = jnp.stack([dk_wide, dv_wide])
    rims = jnp.concatenate(
        [grad_wide[:, :reach_rows], grad_wide[:, wide_rows - reach_rows :]], axis=1
    )
    back_left, back_right = halo(rims, reach_rows)
    center = grad_wide[:, reach_rows : reach_rows + rows]
    center = center.at[:, :reach_rows].add(back_left).at[:, rows - reach_rows :].add(back_right)

    row_dq, part_dk, part_dv = glob_row_call(
        jnp.where(inside_rows, 0.0, neg_large).astype(jnp.float32)[:, None],
        jnp.where(slot_valid[None, :], lse_glob, -neg_large),
        delta_g,
        shared[0],
        shared[3],
        keys,
        values,
    )

    totals = reduce_own(
        jnp.concatenate([row_dq, dk_glob, dv_glob], axis=1)
    )
    d_queries = place(band_dq, totals[:, :D])
    d_keys = place(center[0] + part_dk, totals[:, D : 2 * D])
    d_values = place(center[1] + part_dv, totals[:, 2 * D :])
    return (
        out_full,
        d_queries.astype(jnp.bfloat16),
        d_keys.astype(jnp.bfloat16),
        d_values.astype(jnp.bfloat16),
    )


def solution(mesh):
    rows = P(("groups", "seq"), None)
    return jax.shard_map(
        local,
        mesh=mesh,
        in_specs=(rows, rows, rows, rows, P("groups"), P("groups")),
        out_specs=(rows, rows, rows, rows),
        check_vma=False,
    )
```

```python
import jax
import jax.numpy as jnp
from jax import lax
from jax.sharding import PartitionSpec as P
from jax.experimental import pallas as pl
from jax.experimental.pallas import tpu as pltpu

D = 768
HEADS = 12
BLOCK = 64
REACH = 3
GLOBALS = 128
HEAD_DIM = 64
TILE_BLOCKS = 2

neg_large = -1e30


def mixed(form, left, right):
    return jnp.einsum(form, left, right, preferred_element_type=jnp.float32)


def to_heads(array):
    rows = array.shape[0]
    return jnp.transpose(array.reshape(rows, HEADS, HEAD_DIM), (1, 0, 2))


def from_heads(array):
    rows = array.shape[1]
    return jnp.transpose(array, (1, 0, 2)).reshape(rows, D)


def halo(cells, width):
    count = lax.axis_size("seq")
    ends = count - 1
    head = lax.slice_in_dim(cells, 0, width, axis=1)
    tail = lax.slice_in_dim(cells, cells.shape[1] - width, cells.shape[1], axis=1)
    from_left = lax.ppermute(tail, "seq", [(i, i + 1) for i in range(ends)])
    from_right = lax.ppermute(head, "seq", [(i + 1, i) for i in range(ends)])
    return from_left, from_right


def by_head(array):
    return array.reshape(array.shape[:-1] + (HEADS, HEAD_DIM))


def gather_small(part):
    count = lax.axis_size("seq")
    spread = jnp.broadcast_to(part[None], (count,) + part.shape)
    return lax.all_to_all(spread, "seq", 0, 0)


def reduce_own(full):
    count = lax.axis_size("seq")
    split = full.reshape((count, full.shape[0] // count) + full.shape[1:])
    return jnp.sum(lax.all_to_all(split, "seq", 0, 0), axis=0)


def key_flags(first_pos, span_len, glob_pos, lens_wide):
    places = first_pos + jnp.arange(span_len, dtype=jnp.int32)
    begin = jnp.asarray(first_pos // BLOCK + 2 * REACH, dtype=jnp.int32)
    lens = lax.dynamic_slice_in_dim(lens_wide, begin, span_len // BLOCK)
    inside = (jnp.arange(BLOCK, dtype=jnp.int32)[None, :] < lens[:, None]).reshape(span_len)
    marked = jnp.any(glob_pos[:, None] == places[None, :], axis=0)
    return (inside, marked)


def band_kernel(mask_ref, gmask_ref, keep_ref, q_ref, do_ref, kw_ref, vw_ref, kg_ref, vg_ref,
                out_ref, dq_ref, dkw_ref, dvw_ref, dkg_ref, dvg_ref):
    scale = HEAD_DIM ** (-0.5)
    tile = pl.program_id(1)
    tile_rows = q_ref.shape[0]
    win_rows = mask_ref.shape[2]
    start = pl.multiple_of(tile * tile_rows, tile_rows)
    f32 = jnp.float32
    bf16 = jnp.bfloat16
    nt = (((1,), (1,)), ((), ()))
    tn = (((0,), (0,)), ((), ()))

    @pl.when(tile == 0)
    def _():
        dkw_ref[...] = jnp.zeros_like(dkw_ref)
        dvw_ref[...] = jnp.zeros_like(dvw_ref)
        dkg_ref[...] = jnp.zeros_like(dkg_ref)
        dvg_ref[...] = jnp.zeros_like(dvg_ref)

    band_bias = mask_ref[0]
    glob_bias = gmask_ref[...]
    keep = keep_ref[...].astype(bf16)
    for head in range(q_ref.shape[1] // HEAD_DIM):
        lanes = slice(head * HEAD_DIM, (head + 1) * HEAD_DIM)
        q = q_ref[:, lanes] * jnp.asarray(scale, bf16)
        do = do_ref[:, lanes] * keep
        kwin = kw_ref[pl.ds(start, win_rows), lanes]
        vwin = vw_ref[pl.ds(start, win_rows), lanes]
        kg = kg_ref[:, lanes]
        vg = vg_ref[:, lanes]
        s_b = lax.dot_general(q, kwin, nt, preferred_element_type=f32) + band_bias
        s_g = lax.dot_general(q, kg, nt, preferred_element_type=f32) + glob_bias
        top = jnp.maximum(jnp.max(s_b, axis=1, keepdims=True), jnp.max(s_g, axis=1, keepdims=True))
        e_b = jnp.exp(s_b - top)
        e_g = jnp.exp(s_g - top)
        inv = 1.0 / (jnp.sum(e_b, axis=1, keepdims=True) + jnp.sum(e_g, axis=1, keepdims=True))
        p_b = e_b * inv
        p_g = e_g * inv
        w_b = p_b.astype(bf16)
        w_g = p_g.astype(bf16)
        out = jnp.dot(w_b, vwin, preferred_element_type=f32) + jnp.dot(
            w_g, vg, preferred_element_type=f32
        )
        out_ref[:, lanes] = out
        delta = jnp.sum(
            do.astype(f32) * out.astype(bf16).astype(f32), axis=1, keepdims=True
        )
        dp_b = lax.dot_general(do, vwin, nt, preferred_element_type=f32)
        dp_g = lax.dot_general(do, vg, nt, preferred_element_type=f32)
        ds_b = (p_b * (dp_b - delta)).astype(bf16)
        ds_g = (p_g * (dp_g - delta)).astype(bf16)
        dq = jnp.dot(ds_b, kwin, preferred_element_type=f32) + jnp.dot(
            ds_g, kg, preferred_element_type=f32
        )
        dq_ref[:, lanes] = dq * scale
        dkw_ref[pl.ds(start, win_rows), lanes] += lax.dot_general(ds_b, q, tn, preferred_element_type=f32)
        dvw_ref[pl.ds(start, win_rows), lanes] += lax.dot_general(w_b, do, tn, preferred_element_type=f32)
        dkg_ref[:, lanes] += lax.dot_general(ds_g, q, tn, preferred_element_type=f32)
        dvg_ref[:, lanes] += lax.dot_general(w_g, do, tn, preferred_element_type=f32)


def band_call(mask, gmask, keep, queries, d_out, key_wide, value_wide, key_glob, value_glob, interpret=False):
    rows = queries.shape[0]
    wide_rows = key_wide.shape[0]
    slots = key_glob.shape[0]
    tiles, tile_rows, win_rows = mask.shape
    lanes = 2 * HEAD_DIM
    pairs = D // lanes
    f32 = jnp.float32
    row_spec = pl.BlockSpec((tile_rows, lanes), lambda p, t: (t, p))
    wide_spec = pl.BlockSpec((wide_rows, lanes), lambda p, t: (0, p))
    glob_spec = pl.BlockSpec((slots, lanes), lambda p, t: (0, p))
    return pl.pallas_call(
        band_kernel,
        grid=(pairs, tiles),
        in_specs=[
            pl.BlockSpec((1, tile_rows, win_rows), lambda p, t: (t, 0, 0)),
            pl.BlockSpec((1, slots), lambda p, t: (0, 0)),
            pl.BlockSpec((tile_rows, 1), lambda p, t: (t, 0)),
            row_spec,
            row_spec,
            wide_spec,
            wide_spec,
            glob_spec,
            glob_spec,
        ],
        out_specs=[row_spec, row_spec, wide_spec, wide_spec, glob_spec, glob_spec],
        out_shape=[
            jax.ShapeDtypeStruct((rows, D), f32),
            jax.ShapeDtypeStruct((rows, D), f32),
            jax.ShapeDtypeStruct((wide_rows, D), f32),
            jax.ShapeDtypeStruct((wide_rows, D), f32),
            jax.ShapeDtypeStruct((slots, D), f32),
            jax.ShapeDtypeStruct((slots, D), f32),
        ],
        compiler_params=pltpu.CompilerParams(dimension_semantics=("arbitrary", "arbitrary")),
        interpret=interpret,
    )(mask, gmask, keep, queries, d_out, key_wide, value_wide, key_glob, value_glob)


def band_kernel_t(mask_ref, gmask_ref, keep_ref, keep_row_ref, q_ref, qt_ref, do_ref, dot_ref,
                  kw_ref, kt_ref, vw_ref, vt_ref, kg_ref, kgt_ref, vg_ref, vgt_ref,
                  out_ref, dq_ref, dkw_ref, dvw_ref, dkg_ref, dvg_ref):
    scale = HEAD_DIM ** (-0.5)
    tile = pl.program_id(1)
    tile_rows = q_ref.shape[0]
    win_rows = mask_ref.shape[1]
    start = pl.multiple_of(tile * tile_rows, tile_rows)
    f32 = jnp.float32
    bf16 = jnp.bfloat16

    @pl.when(tile == 0)
    def _():
        dkw_ref[...] = jnp.zeros_like(dkw_ref)
        dvw_ref[...] = jnp.zeros_like(dvw_ref)
        dkg_ref[...] = jnp.zeros_like(dkg_ref)
        dvg_ref[...] = jnp.zeros_like(dvg_ref)

    band_bias = mask_ref[0]
    glob_bias = gmask_ref[...]
    keep = keep_ref[...].astype(bf16)
    keep_row = keep_row_ref[...].astype(bf16)
    shrink = jnp.asarray(scale, bf16)
    for head in range(q_ref.shape[1] // HEAD_DIM):
        lanes = slice(head * HEAD_DIM, (head + 1) * HEAD_DIM)
        q = q_ref[:, lanes] * shrink
        qt = qt_ref[lanes, :] * shrink
        do = do_ref[:, lanes] * keep
        dot = dot_ref[lanes, :] * keep_row
        kwin = kw_ref[pl.ds(start, win_rows), lanes]
        ktwin = kt_ref[lanes, pl.ds(start, win_rows)]
        vwin = vw_ref[pl.ds(start, win_rows), lanes]
        vtwin = vt_ref[lanes, pl.ds(start, win_rows)]
        kg = kg_ref[:, lanes]
        kgt = kgt_ref[lanes, :]
        vg = vg_ref[:, lanes]
        vgt = vgt_ref[lanes, :]
        s_b = jnp.dot(kwin, qt, preferred_element_type=f32) + band_bias
        s_g = jnp.dot(kg, qt, preferred_element_type=f32) + glob_bias
        top = jnp.maximum(jnp.max(s_b, axis=0, keepdims=True), jnp.max(s_g, axis=0, keepdims=True))
        e_b = jnp.exp(s_b - top)
        e_g = jnp.exp(s_g - top)
        inv = 1.0 / (jnp.sum(e_b, axis=0, keepdims=True) + jnp.sum(e_g, axis=0, keepdims=True))
        p_b = e_b * inv
        p_g = e_g * inv
        w_b = p_b.astype(bf16)
        w_g = p_g.astype(bf16)
        out = jnp.dot(vtwin, w_b, preferred_element_type=f32) + jnp.dot(
            vgt, w_g, preferred_element_type=f32
        )
        out_ref[lanes, :] = out
        delta = jnp.sum(
            dot.astype(f32) * out.astype(bf16).astype(f32), axis=0, keepdims=True
        )
        dp_b = jnp.dot(vwin, dot, preferred_element_type=f32)
        dp_g = jnp.dot(vg, dot, preferred_element_type=f32)
        ds_b = (p_b * (dp_b - delta)).astype(bf16)
        ds_g = (p_g * (dp_g - delta)).astype(bf16)
        dq = jnp.dot(ktwin, ds_b, preferred_element_type=f32) + jnp.dot(
            kgt, ds_g, preferred_element_type=f32
        )
        dq_ref[lanes, :] = dq * scale
        dkw_ref[pl.ds(start, win_rows), lanes] += jnp.dot(ds_b, q, preferred_element_type=f32)
        dvw_ref[pl.ds(start, win_rows), lanes] += jnp.dot(w_b, do, preferred_element_type=f32)
        dkg_ref[:, lanes] += jnp.dot(ds_g, q, preferred_element_type=f32)
        dvg_ref[:, lanes] += jnp.dot(w_g, do, preferred_element_type=f32)


def band_call_t(mask, gmask, keep, queries, d_out, key_wide, value_wide, key_glob, value_glob, interpret=False):
    rows = queries.shape[0]
    wide_rows = key_wide.shape[0]
    slots = key_glob.shape[0]
    tiles, tile_rows, win_rows = mask.shape
    lanes = 2 * HEAD_DIM
    pairs = D // lanes
    f32 = jnp.float32
    row_spec = pl.BlockSpec((tile_rows, lanes), lambda p, t: (t, p))
    col_spec = pl.BlockSpec((lanes, tile_rows), lambda p, t: (p, t))
    wide_spec = pl.BlockSpec((wide_rows, lanes), lambda p, t: (0, p))
    wide_t_spec = pl.BlockSpec((lanes, wide_rows), lambda p, t: (p, 0))
    glob_spec = pl.BlockSpec((slots, lanes), lambda p, t: (0, p))
    glob_t_spec = pl.BlockSpec((lanes, slots), lambda p, t: (p, 0))
    out_t, dq_t, dkw, dvw, dkg, dvg = pl.pallas_call(
        band_kernel_t,
        grid=(pairs, tiles),
        in_specs=[
            pl.BlockSpec((1, win_rows, tile_rows), lambda p, t: (t, 0, 0)),
            pl.BlockSpec((slots, 1), lambda p, t: (0, 0)),
            pl.BlockSpec((tile_rows, 1), lambda p, t: (t, 0)),
            pl.BlockSpec((1, tile_rows), lambda p, t: (0, t)),
            row_spec,
            col_spec,
            row_spec,
            col_spec,
            wide_spec,
            wide_t_spec,
            wide_spec,
            wide_t_spec,
            glob_spec,
            glob_t_spec,
            glob_spec,
            glob_t_spec,
        ],
        out_specs=[col_spec, col_spec, wide_spec, wide_spec, glob_spec, glob_spec],
        out_shape=[
            jax.ShapeDtypeStruct((D, rows), f32),
            jax.ShapeDtypeStruct((D, rows), f32),
            jax.ShapeDtypeStruct((wide_rows, D), f32),
            jax.ShapeDtypeStruct((wide_rows, D), f32),
            jax.ShapeDtypeStruct((slots, D), f32),
            jax.ShapeDtypeStruct((slots, D), f32),
        ],
        compiler_params=pltpu.CompilerParams(dimension_semantics=("arbitrary", "arbitrary")),
        interpret=interpret,
    )(
        jnp.transpose(mask, (0, 2, 1)),
        jnp.transpose(gmask),
        keep,
        jnp.transpose(keep),
        queries,
        jnp.transpose(queries),
        d_out,
        jnp.transpose(d_out),
        key_wide,
        jnp.transpose(key_wide),
        value_wide,
        jnp.transpose(value_wide),
        key_glob,
        jnp.transpose(key_glob),
        value_glob,
        jnp.transpose(value_glob),
    )
    return jnp.transpose(out_t), jnp.transpose(dq_t), dkw, dvw, dkg, dvg


def glob_row_kernel(bias_ref, lse_ref, delta_ref, qg_ref, dog_ref, k_ref, v_ref, dk_ref, dv_ref):
    scale = HEAD_DIM ** (-0.5)
    pair = pl.program_id(0)
    f32 = jnp.float32
    bf16 = jnp.bfloat16
    bias = bias_ref[...]
    heads = qg_ref.shape[1] // HEAD_DIM
    for head in range(heads):
        lanes = slice(head * HEAD_DIM, (head + 1) * HEAD_DIM)
        row = pl.ds(pair * heads + head, 1)
        qg_wide = qg_ref[:, lanes].astype(f32) * scale
        dog_wide = dog_ref[:, lanes].astype(f32)
        qg = qg_wide.astype(bf16)
        qgt = jnp.transpose(qg_wide).astype(bf16)
        dog = dog_wide.astype(bf16)
        dogt = jnp.transpose(dog_wide).astype(bf16)
        k = k_ref[:, lanes]
        v = v_ref[:, lanes]
        s = jnp.dot(k, qgt, preferred_element_type=f32) + bias
        p = jnp.exp(s - lse_ref[row, :])
        w = p.astype(bf16)
        dp = jnp.dot(v, dogt, preferred_element_type=f32)
        ds = (p * (dp - delta_ref[row, :])).astype(bf16)
        dk_ref[:, lanes] = jnp.dot(ds, qg, preferred_element_type=f32)
        dv_ref[:, lanes] = jnp.dot(w, dog, preferred_element_type=f32)


def glob_row_call(bias, lse, delta, query_glob, dout_glob, keys, values):
    rows = keys.shape[0]
    slots = query_glob.shape[0]
    lanes = 2 * HEAD_DIM
    f32 = jnp.float32
    glob_spec = pl.BlockSpec((slots, lanes), lambda p: (0, p))
    row_spec = pl.BlockSpec((rows, lanes), lambda p: (0, p))
    return pl.pallas_call(
        glob_row_kernel,
        grid=(D // lanes,),
        in_specs=[
            pl.BlockSpec((rows, 1), lambda p: (0, 0)),
            pl.BlockSpec((HEADS, slots), lambda p: (0, 0)),
            pl.BlockSpec((HEADS, slots), lambda p: (0, 0)),
            glob_spec,
            glob_spec,
            row_spec,
            row_spec,
        ],
        out_specs=[row_spec, row_spec],
        out_shape=[
            jax.ShapeDtypeStruct((rows, D), f32),
            jax.ShapeDtypeStruct((rows, D), f32),
        ],
        compiler_params=pltpu.CompilerParams(dimension_semantics=("arbitrary",)),
    )(bias, lse, delta, query_glob, dout_glob, keys, values)


def local(queries, keys, values, d_out, glob_pos, block_len):
    scale = HEAD_DIM ** (-0.5)
    rows = queries.shape[0]
    reach_rows = REACH * BLOCK
    tile_rows = TILE_BLOCKS * BLOCK
    tiles = rows // tile_rows
    win_rows = tile_rows + 2 * reach_rows
    wide_rows = rows + 2 * reach_rows
    first_row = lax.axis_index("seq") * rows
    lens_wide = jnp.pad(block_len, 2 * REACH)

    places = first_row + jnp.arange(rows, dtype=jnp.int32)
    marked_rows = jnp.any(glob_pos[:, None] == places[None, :], axis=0)
    local_pos = glob_pos - first_row
    is_local = (local_pos >= 0) & (local_pos < rows)
    local_index = jnp.where(is_local, local_pos, rows)
    inside_rows, _ = key_flags(first_row, rows, glob_pos, lens_wide)

    count = lax.axis_size("seq")
    own_blocks = rows // BLOCK
    slots = own_blocks * count
    glob_block = glob_pos // BLOCK
    slot_valid = jnp.zeros((slots,), bool).at[glob_block].set(True, mode="drop")
    own_slot = lax.axis_index("seq") * own_blocks + jnp.arange(own_blocks, dtype=jnp.int32)
    own_match = glob_block[None, :] == own_slot[:, None]
    own_has = jnp.any(own_match, axis=1)
    own_pos = jnp.sum(jnp.where(own_match, glob_pos[None, :], 0), axis=1) - first_row
    own_offset = own_pos - BLOCK * jnp.arange(own_blocks, dtype=jnp.int32)
    own_row = own_has[:, None] & (jnp.arange(BLOCK, dtype=jnp.int32)[None, :] == own_offset[:, None])

    def place(base, extra):
        shaped = base.reshape(own_blocks, BLOCK, D)
        return jnp.where(own_row[:, :, None], shaped + extra[:, None, :], shaped).reshape(rows, D)

    own_pick = (
        own_has[:, None] & (jnp.arange(rows, dtype=jnp.int32)[None, :] == own_pos[:, None])
    ).astype(jnp.bfloat16)
    picked = jnp.stack(
        [
            jnp.dot(own_pick, source, preferred_element_type=jnp.float32).astype(jnp.bfloat16)
            for source in (queries, keys, values, d_out)
        ]
    )
    shared = jnp.transpose(gather_small(picked), (1, 0, 2, 3)).reshape(4, slots, D)
    qg = to_heads(shared[0])
    kg = to_heads(shared[1])
    vg = to_heads(shared[2])
    dog = to_heads(shared[3])

    pair = jnp.stack([keys, values])
    from_left, from_right = halo(pair, reach_rows)
    pair_wide = jnp.concatenate([from_left, pair, from_right], axis=1)
    k_h = to_heads(keys)
    v_h = to_heads(values)

    inside_wide, marked_wide = key_flags(first_row - reach_rows, wide_rows, glob_pos, lens_wide)
    allowed_wide = inside_wide & jnp.logical_not(marked_wide)

    allowed_t = jnp.stack(
        [lax.slice_in_dim(allowed_wide, t * tile_rows, t * tile_rows + win_rows) for t in range(tiles)]
    )
    q_block = (jnp.arange(rows, dtype=jnp.int32) // BLOCK).reshape(tiles, tile_rows)
    k_block = jnp.stack(
        [t * TILE_BLOCKS + jnp.arange(win_rows, dtype=jnp.int32) // BLOCK - REACH for t in range(tiles)]
    )
    near = jnp.abs(q_block[:, :, None] - k_block[:, None, :]) <= REACH
    band_mask = near & allowed_t[:, None, :]
    band_out, band_dq, dk_wide, dv_wide, dk_glob, dv_glob = band_call_t(
        jnp.where(band_mask, 0.0, neg_large).astype(jnp.float32),
        jnp.where(slot_valid, 0.0, neg_large).astype(jnp.float32)[None, :],
        jnp.logical_not(marked_rows).astype(jnp.float32)[:, None],
        queries,
        d_out,
        pair_wide[0],
        pair_wide[1],
        shared[1],
        shared[2],
    )

    g_score = mixed("hge,hre->hgr", qg, k_h) * scale
    g_score = jnp.where(inside_rows[None, None, :], g_score, neg_large)
    g_top = jnp.max(g_score, axis=-1)
    g_sum = jnp.sum(jnp.exp(g_score - g_top[..., None]), axis=-1)
    stats = gather_small(jnp.stack([g_top, g_sum]))
    all_top = stats[:, 0]
    top_glob = jnp.max(all_top, axis=0)
    sum_glob = jnp.sum(stats[:, 1] * jnp.exp(all_top - top_glob[None]), axis=0)
    lse_glob = top_glob + jnp.log(sum_glob)
    g_prob = jnp.where(slot_valid[None, :, None], jnp.exp(g_score - lse_glob[..., None]), 0.0)
    g_weight = g_prob.astype(jnp.bfloat16)
    out_own = reduce_own(from_heads(mixed("hgr,hre->hge", g_weight, v_h)))
    out_own16 = out_own.astype(jnp.bfloat16)
    delta_own = jnp.sum(
        by_head(picked[3]).astype(jnp.float32) * by_head(out_own16).astype(jnp.float32), axis=-1
    )
    delta_g = jnp.transpose(gather_small(delta_own).reshape(slots, HEADS))
    band_out16 = band_out.astype(jnp.bfloat16)
    out_full = jnp.where(
        own_row[:, :, None], out_own16[:, None, :], band_out16.reshape(own_blocks, BLOCK, D)
    ).reshape(rows, D)

    grad_wide = jnp.stack([dk_wide, dv_wide])
    rims = jnp.concatenate(
        [grad_wide[:, :reach_rows], grad_wide[:, wide_rows - reach_rows :]], axis=1
    )
    back_left, back_right = halo(rims, reach_rows)
    center = grad_wide[:, reach_rows : reach_rows + rows]
    center = center.at[:, :reach_rows].add(back_left).at[:, rows - reach_rows :].add(back_right)

    g_dprob = mixed("hge,hre->hgr", dog, v_h)
    g_dscore = (g_prob * (g_dprob - delta_g[..., None])).astype(jnp.bfloat16)
    row_dq = from_heads(mixed("hgr,hre->hge", g_dscore, k_h) * scale)
    part_dk, part_dv = glob_row_call(
        jnp.where(inside_rows, 0.0, neg_large).astype(jnp.float32)[:, None],
        jnp.where(slot_valid[None, :], lse_glob, -neg_large),
        delta_g,
        shared[0],
        shared[3],
        keys,
        values,
    )

    totals = reduce_own(
        jnp.concatenate([row_dq, dk_glob, dv_glob], axis=1)
    )
    d_queries = place(band_dq, totals[:, :D])
    d_keys = place(center[0] + part_dk, totals[:, D : 2 * D])
    d_values = place(center[1] + part_dv, totals[:, 2 * D :])
    return (
        out_full,
        d_queries.astype(jnp.bfloat16),
        d_keys.astype(jnp.bfloat16),
        d_values.astype(jnp.bfloat16),
    )


def solution(mesh):
    rows = P(("groups", "seq"), None)
    return jax.shard_map(
        local,
        mesh=mesh,
        in_specs=(rows, rows, rows, rows, P("groups"), P("groups")),
        out_specs=(rows, rows, rows, rows),
        check_vma=False,
    )
```

```python
import jax
import jax.numpy as jnp
from jax import lax
from jax.sharding import PartitionSpec as P
from jax.experimental import pallas as pl
from jax.experimental.pallas import tpu as pltpu

D = 768
HEADS = 12
BLOCK = 64
REACH = 3
GLOBALS = 128
HEAD_DIM = 64
TILE_BLOCKS = 2

neg_large = -1e30


def mixed(form, left, right):
    return jnp.einsum(form, left, right, preferred_element_type=jnp.float32)


def to_heads(array):
    rows = array.shape[0]
    return jnp.transpose(array.reshape(rows, HEADS, HEAD_DIM), (1, 0, 2))


def from_heads(array):
    rows = array.shape[1]
    return jnp.transpose(array, (1, 0, 2)).reshape(rows, D)


def halo(cells, width):
    count = lax.axis_size("seq")
    ends = count - 1
    head = lax.slice_in_dim(cells, 0, width, axis=1)
    tail = lax.slice_in_dim(cells, cells.shape[1] - width, cells.shape[1], axis=1)
    from_left = lax.ppermute(tail, "seq", [(i, i + 1) for i in range(ends)])
    from_right = lax.ppermute(head, "seq", [(i + 1, i) for i in range(ends)])
    return from_left, from_right


def by_head(array):
    return array.reshape(array.shape[:-1] + (HEADS, HEAD_DIM))


def gather_small(part):
    count = lax.axis_size("seq")
    spread = jnp.broadcast_to(part[None], (count,) + part.shape)
    return lax.all_to_all(spread, "seq", 0, 0)


def reduce_own(full):
    count = lax.axis_size("seq")
    split = full.reshape((count, full.shape[0] // count) + full.shape[1:])
    return jnp.sum(lax.all_to_all(split, "seq", 0, 0), axis=0)


def key_flags(first_pos, span_len, glob_pos, lens_wide):
    places = first_pos + jnp.arange(span_len, dtype=jnp.int32)
    begin = jnp.asarray(first_pos // BLOCK + 2 * REACH, dtype=jnp.int32)
    lens = lax.dynamic_slice_in_dim(lens_wide, begin, span_len // BLOCK)
    inside = (jnp.arange(BLOCK, dtype=jnp.int32)[None, :] < lens[:, None]).reshape(span_len)
    marked = jnp.any(glob_pos[:, None] == places[None, :], axis=0)
    return (inside, marked)


def band_kernel(mask_ref, gmask_ref, keep_ref, q_ref, do_ref, kw_ref, vw_ref, kg_ref, vg_ref,
                out_ref, dq_ref, dkw_ref, dvw_ref, dkg_ref, dvg_ref):
    scale = HEAD_DIM ** (-0.5)
    tile = pl.program_id(1)
    tile_rows = q_ref.shape[0]
    win_rows = mask_ref.shape[2]
    start = pl.multiple_of(tile * tile_rows, tile_rows)
    f32 = jnp.float32
    bf16 = jnp.bfloat16
    nt = (((1,), (1,)), ((), ()))
    tn = (((0,), (0,)), ((), ()))

    @pl.when(tile == 0)
    def _():
        dkw_ref[...] = jnp.zeros_like(dkw_ref)
        dvw_ref[...] = jnp.zeros_like(dvw_ref)
        dkg_ref[...] = jnp.zeros_like(dkg_ref)
        dvg_ref[...] = jnp.zeros_like(dvg_ref)

    band_bias = mask_ref[0]
    glob_bias = gmask_ref[...]
    keep = keep_ref[...].astype(bf16)
    for head in range(q_ref.shape[1] // HEAD_DIM):
        lanes = slice(head * HEAD_DIM, (head + 1) * HEAD_DIM)
        q = q_ref[:, lanes] * jnp.asarray(scale, bf16)
        do = do_ref[:, lanes] * keep
        kwin = kw_ref[pl.ds(start, win_rows), lanes]
        vwin = vw_ref[pl.ds(start, win_rows), lanes]
        kg = kg_ref[:, lanes]
        vg = vg_ref[:, lanes]
        s_b = lax.dot_general(q, kwin, nt, preferred_element_type=f32) + band_bias
        s_g = lax.dot_general(q, kg, nt, preferred_element_type=f32) + glob_bias
        top = jnp.maximum(jnp.max(s_b, axis=1, keepdims=True), jnp.max(s_g, axis=1, keepdims=True))
        e_b = jnp.exp(s_b - top)
        e_g = jnp.exp(s_g - top)
        inv = 1.0 / (jnp.sum(e_b, axis=1, keepdims=True) + jnp.sum(e_g, axis=1, keepdims=True))
        p_b = e_b * inv
        p_g = e_g * inv
        w_b = p_b.astype(bf16)
        w_g = p_g.astype(bf16)
        out = jnp.dot(w_b, vwin, preferred_element_type=f32) + jnp.dot(
            w_g, vg, preferred_element_type=f32
        )
        out_ref[:, lanes] = out
        delta = jnp.sum(
            do.astype(f32) * out.astype(bf16).astype(f32), axis=1, keepdims=True
        )
        dp_b = lax.dot_general(do, vwin, nt, preferred_element_type=f32)
        dp_g = lax.dot_general(do, vg, nt, preferred_element_type=f32)
        ds_b = (p_b * (dp_b - delta)).astype(bf16)
        ds_g = (p_g * (dp_g - delta)).astype(bf16)
        dq = jnp.dot(ds_b, kwin, preferred_element_type=f32) + jnp.dot(
            ds_g, kg, preferred_element_type=f32
        )
        dq_ref[:, lanes] = dq * scale
        dkw_ref[pl.ds(start, win_rows), lanes] += lax.dot_general(ds_b, q, tn, preferred_element_type=f32)
        dvw_ref[pl.ds(start, win_rows), lanes] += lax.dot_general(w_b, do, tn, preferred_element_type=f32)
        dkg_ref[:, lanes] += lax.dot_general(ds_g, q, tn, preferred_element_type=f32)
        dvg_ref[:, lanes] += lax.dot_general(w_g, do, tn, preferred_element_type=f32)


def band_call(mask, gmask, keep, queries, d_out, key_wide, value_wide, key_glob, value_glob, interpret=False):
    rows = queries.shape[0]
    wide_rows = key_wide.shape[0]
    slots = key_glob.shape[0]
    tiles, tile_rows, win_rows = mask.shape
    lanes = 2 * HEAD_DIM
    pairs = D // lanes
    f32 = jnp.float32
    row_spec = pl.BlockSpec((tile_rows, lanes), lambda p, t: (t, p))
    wide_spec = pl.BlockSpec((wide_rows, lanes), lambda p, t: (0, p))
    glob_spec = pl.BlockSpec((slots, lanes), lambda p, t: (0, p))
    return pl.pallas_call(
        band_kernel,
        grid=(pairs, tiles),
        in_specs=[
            pl.BlockSpec((1, tile_rows, win_rows), lambda p, t: (t, 0, 0)),
            pl.BlockSpec((1, slots), lambda p, t: (0, 0)),
            pl.BlockSpec((tile_rows, 1), lambda p, t: (t, 0)),
            row_spec,
            row_spec,
            wide_spec,
            wide_spec,
            glob_spec,
            glob_spec,
        ],
        out_specs=[row_spec, row_spec, wide_spec, wide_spec, glob_spec, glob_spec],
        out_shape=[
            jax.ShapeDtypeStruct((rows, D), f32),
            jax.ShapeDtypeStruct((rows, D), f32),
            jax.ShapeDtypeStruct((wide_rows, D), f32),
            jax.ShapeDtypeStruct((wide_rows, D), f32),
            jax.ShapeDtypeStruct((slots, D), f32),
            jax.ShapeDtypeStruct((slots, D), f32),
        ],
        compiler_params=pltpu.CompilerParams(dimension_semantics=("arbitrary", "arbitrary")),
        interpret=interpret,
    )(mask, gmask, keep, queries, d_out, key_wide, value_wide, key_glob, value_glob)


def band_kernel_t(mask_ref, gmask_ref, keep_ref, keep_row_ref, q_ref, qt_ref, do_ref, dot_ref,
                  kw_ref, kt_ref, vw_ref, vt_ref, kg_ref, kgt_ref, vg_ref, vgt_ref,
                  out_ref, dq_ref, dkw_ref, dvw_ref, dkg_ref, dvg_ref):
    scale = HEAD_DIM ** (-0.5)
    tile = pl.program_id(1)
    tile_rows = q_ref.shape[0]
    win_rows = mask_ref.shape[1]
    start = pl.multiple_of(tile * tile_rows, tile_rows)
    f32 = jnp.float32
    bf16 = jnp.bfloat16

    @pl.when(tile == 0)
    def _():
        dkw_ref[...] = jnp.zeros_like(dkw_ref)
        dvw_ref[...] = jnp.zeros_like(dvw_ref)
        dkg_ref[...] = jnp.zeros_like(dkg_ref)
        dvg_ref[...] = jnp.zeros_like(dvg_ref)

    band_bias = mask_ref[0]
    glob_bias = gmask_ref[...]
    keep = keep_ref[...].astype(bf16)
    keep_row = keep_row_ref[...].astype(bf16)
    shrink = jnp.asarray(scale, bf16)
    for head in range(q_ref.shape[1] // HEAD_DIM):
        lanes = slice(head * HEAD_DIM, (head + 1) * HEAD_DIM)
        q = q_ref[:, lanes] * shrink
        qt = qt_ref[lanes, :] * shrink
        do = do_ref[:, lanes] * keep
        dot = dot_ref[lanes, :] * keep_row
        kwin = kw_ref[pl.ds(start, win_rows), lanes]
        ktwin = kt_ref[lanes, pl.ds(start, win_rows)]
        vwin = vw_ref[pl.ds(start, win_rows), lanes]
        vtwin = vt_ref[lanes, pl.ds(start, win_rows)]
        kg = kg_ref[:, lanes]
        kgt = kgt_ref[lanes, :]
        vg = vg_ref[:, lanes]
        vgt = vgt_ref[lanes, :]
        s_b = jnp.dot(kwin, qt, preferred_element_type=f32) + band_bias
        s_g = jnp.dot(kg, qt, preferred_element_type=f32) + glob_bias
        top = jnp.maximum(jnp.max(s_b, axis=0, keepdims=True), jnp.max(s_g, axis=0, keepdims=True))
        e_b = jnp.exp(s_b - top)
        e_g = jnp.exp(s_g - top)
        inv = 1.0 / (jnp.sum(e_b, axis=0, keepdims=True) + jnp.sum(e_g, axis=0, keepdims=True))
        p_b = e_b * inv
        p_g = e_g * inv
        w_b = p_b.astype(bf16)
        w_g = p_g.astype(bf16)
        out = jnp.dot(vtwin, w_b, preferred_element_type=f32) + jnp.dot(
            vgt, w_g, preferred_element_type=f32
        )
        out_ref[lanes, :] = out
        delta = jnp.sum(
            dot.astype(f32) * out.astype(bf16).astype(f32), axis=0, keepdims=True
        )
        dp_b = jnp.dot(vwin, dot, preferred_element_type=f32)
        dp_g = jnp.dot(vg, dot, preferred_element_type=f32)
        ds_b = (p_b * (dp_b - delta)).astype(bf16)
        ds_g = (p_g * (dp_g - delta)).astype(bf16)
        dq = jnp.dot(ktwin, ds_b, preferred_element_type=f32) + jnp.dot(
            kgt, ds_g, preferred_element_type=f32
        )
        dq_ref[lanes, :] = dq * scale
        dkw_ref[pl.ds(start, win_rows), lanes] += jnp.dot(ds_b, q, preferred_element_type=f32)
        dvw_ref[pl.ds(start, win_rows), lanes] += jnp.dot(w_b, do, preferred_element_type=f32)
        dkg_ref[:, lanes] += jnp.dot(ds_g, q, preferred_element_type=f32)
        dvg_ref[:, lanes] += jnp.dot(w_g, do, preferred_element_type=f32)


def band_call_t(mask, gmask, keep, queries, d_out, key_wide, value_wide, key_glob, value_glob, interpret=False):
    rows = queries.shape[0]
    wide_rows = key_wide.shape[0]
    slots = key_glob.shape[0]
    tiles, tile_rows, win_rows = mask.shape
    lanes = 2 * HEAD_DIM
    pairs = D // lanes
    f32 = jnp.float32
    row_spec = pl.BlockSpec((tile_rows, lanes), lambda p, t: (t, p))
    col_spec = pl.BlockSpec((lanes, tile_rows), lambda p, t: (p, t))
    wide_spec = pl.BlockSpec((wide_rows, lanes), lambda p, t: (0, p))
    wide_t_spec = pl.BlockSpec((lanes, wide_rows), lambda p, t: (p, 0))
    glob_spec = pl.BlockSpec((slots, lanes), lambda p, t: (0, p))
    glob_t_spec = pl.BlockSpec((lanes, slots), lambda p, t: (p, 0))
    out_t, dq_t, dkw, dvw, dkg, dvg = pl.pallas_call(
        band_kernel_t,
        grid=(pairs, tiles),
        in_specs=[
            pl.BlockSpec((1, win_rows, tile_rows), lambda p, t: (t, 0, 0)),
            pl.BlockSpec((slots, 1), lambda p, t: (0, 0)),
            pl.BlockSpec((tile_rows, 1), lambda p, t: (t, 0)),
            pl.BlockSpec((1, tile_rows), lambda p, t: (0, t)),
            row_spec,
            col_spec,
            row_spec,
            col_spec,
            wide_spec,
            wide_t_spec,
            wide_spec,
            wide_t_spec,
            glob_spec,
            glob_t_spec,
            glob_spec,
            glob_t_spec,
        ],
        out_specs=[col_spec, col_spec, wide_spec, wide_spec, glob_spec, glob_spec],
        out_shape=[
            jax.ShapeDtypeStruct((D, rows), f32),
            jax.ShapeDtypeStruct((D, rows), f32),
            jax.ShapeDtypeStruct((wide_rows, D), f32),
            jax.ShapeDtypeStruct((wide_rows, D), f32),
            jax.ShapeDtypeStruct((slots, D), f32),
            jax.ShapeDtypeStruct((slots, D), f32),
        ],
        compiler_params=pltpu.CompilerParams(dimension_semantics=("arbitrary", "arbitrary")),
        interpret=interpret,
    )(
        jnp.transpose(mask, (0, 2, 1)),
        jnp.transpose(gmask),
        keep,
        jnp.transpose(keep),
        queries,
        jnp.transpose(queries),
        d_out,
        jnp.transpose(d_out),
        key_wide,
        jnp.transpose(key_wide),
        value_wide,
        jnp.transpose(value_wide),
        key_glob,
        jnp.transpose(key_glob),
        value_glob,
        jnp.transpose(value_glob),
    )
    return jnp.transpose(out_t), jnp.transpose(dq_t), dkw, dvw, dkg, dvg


def local(queries, keys, values, d_out, glob_pos, block_len):
    scale = HEAD_DIM ** (-0.5)
    rows = queries.shape[0]
    reach_rows = REACH * BLOCK
    tile_rows = TILE_BLOCKS * BLOCK
    tiles = rows // tile_rows
    win_rows = tile_rows + 2 * reach_rows
    wide_rows = rows + 2 * reach_rows
    first_row = lax.axis_index("seq") * rows
    lens_wide = jnp.pad(block_len, 2 * REACH)

    places = first_row + jnp.arange(rows, dtype=jnp.int32)
    marked_rows = jnp.any(glob_pos[:, None] == places[None, :], axis=0)
    local_pos = glob_pos - first_row
    is_local = (local_pos >= 0) & (local_pos < rows)
    local_index = jnp.where(is_local, local_pos, rows)
    inside_rows, _ = key_flags(first_row, rows, glob_pos, lens_wide)

    count = lax.axis_size("seq")
    own_blocks = rows // BLOCK
    slots = own_blocks * count
    glob_block = glob_pos // BLOCK
    slot_valid = jnp.zeros((slots,), bool).at[glob_block].set(True, mode="drop")
    own_slot = lax.axis_index("seq") * own_blocks + jnp.arange(own_blocks, dtype=jnp.int32)
    own_match = glob_block[None, :] == own_slot[:, None]
    own_has = jnp.any(own_match, axis=1)
    own_pos = jnp.sum(jnp.where(own_match, glob_pos[None, :], 0), axis=1) - first_row
    own_offset = own_pos - BLOCK * jnp.arange(own_blocks, dtype=jnp.int32)
    own_row = own_has[:, None] & (jnp.arange(BLOCK, dtype=jnp.int32)[None, :] == own_offset[:, None])

    def place(base, extra):
        shaped = base.reshape(own_blocks, BLOCK, D)
        return jnp.where(own_row[:, :, None], shaped + extra[:, None, :], shaped).reshape(rows, D)

    picked = jnp.stack(
        [
            jnp.sum(
                jnp.where(own_row[:, :, None], source.reshape(own_blocks, BLOCK, D), jnp.zeros((), source.dtype)),
                axis=1,
            )
            for source in (queries, keys, values, d_out)
        ]
    )
    shared = jnp.transpose(gather_small(picked), (1, 0, 2, 3)).reshape(4, slots, D)
    qg = to_heads(shared[0])
    kg = to_heads(shared[1])
    vg = to_heads(shared[2])
    dog = to_heads(shared[3])

    pair = jnp.stack([keys, values])
    from_left, from_right = halo(pair, reach_rows)
    pair_wide = jnp.concatenate([from_left, pair, from_right], axis=1)
    k_h = to_heads(keys)
    v_h = to_heads(values)

    inside_wide, marked_wide = key_flags(first_row - reach_rows, wide_rows, glob_pos, lens_wide)
    allowed_wide = inside_wide & jnp.logical_not(marked_wide)

    allowed_t = jnp.stack(
        [lax.slice_in_dim(allowed_wide, t * tile_rows, t * tile_rows + win_rows) for t in range(tiles)]
    )
    q_block = (jnp.arange(rows, dtype=jnp.int32) // BLOCK).reshape(tiles, tile_rows)
    k_block = jnp.stack(
        [t * TILE_BLOCKS + jnp.arange(win_rows, dtype=jnp.int32) // BLOCK - REACH for t in range(tiles)]
    )
    near = jnp.abs(q_block[:, :, None] - k_block[:, None, :]) <= REACH
    band_mask = near & allowed_t[:, None, :]
    band_out, band_dq, dk_wide, dv_wide, dk_glob, dv_glob = band_call_t(
        jnp.where(band_mask, 0.0, neg_large).astype(jnp.float32),
        jnp.where(slot_valid, 0.0, neg_large).astype(jnp.float32)[None, :],
        jnp.logical_not(marked_rows).astype(jnp.float32)[:, None],
        queries,
        d_out,
        pair_wide[0],
        pair_wide[1],
        shared[1],
        shared[2],
    )

    g_score = mixed("hge,hre->hgr", qg, k_h) * scale
    g_score = jnp.where(inside_rows[None, None, :], g_score, neg_large)
    g_top = jnp.max(g_score, axis=-1)
    g_sum = jnp.sum(jnp.exp(g_score - g_top[..., None]), axis=-1)
    stats = gather_small(jnp.stack([g_top, g_sum]))
    all_top = stats[:, 0]
    top_glob = jnp.max(all_top, axis=0)
    sum_glob = jnp.sum(stats[:, 1] * jnp.exp(all_top - top_glob[None]), axis=0)
    lse_glob = top_glob + jnp.log(sum_glob)
    g_prob = jnp.where(slot_valid[None, :, None], jnp.exp(g_score - lse_glob[..., None]), 0.0)
    g_weight = g_prob.astype(jnp.bfloat16)
    out_own = reduce_own(from_heads(mixed("hgr,hre->hge", g_weight, v_h)))
    out_own16 = out_own.astype(jnp.bfloat16)
    delta_own = jnp.sum(
        by_head(picked[3]).astype(jnp.float32) * by_head(out_own16).astype(jnp.float32), axis=-1
    )
    delta_g = jnp.transpose(gather_small(delta_own).reshape(slots, HEADS))
    band_out16 = band_out.astype(jnp.bfloat16)
    out_full = jnp.where(
        own_row[:, :, None], out_own16[:, None, :], band_out16.reshape(own_blocks, BLOCK, D)
    ).reshape(rows, D)

    grad_wide = jnp.stack([dk_wide, dv_wide])
    rims = jnp.concatenate(
        [grad_wide[:, :reach_rows], grad_wide[:, wide_rows - reach_rows :]], axis=1
    )
    back_left, back_right = halo(rims, reach_rows)
    center = grad_wide[:, reach_rows : reach_rows + rows]
    center = center.at[:, :reach_rows].add(back_left).at[:, rows - reach_rows :].add(back_right)

    g_dprob = mixed("hge,hre->hgr", dog, v_h)
    g_dscore = (g_prob * (g_dprob - delta_g[..., None])).astype(jnp.bfloat16)
    row_dq = mixed("hgr,hre->hge", g_dscore, k_h) * scale
    part_dk = mixed("hgr,hge->hre", g_dscore, qg) * scale
    part_dv = mixed("hgr,hge->hre", g_weight, dog)

    totals = reduce_own(
        jnp.concatenate([from_heads(row_dq), dk_glob, dv_glob], axis=1)
    )
    d_queries = place(band_dq, totals[:, :D])
    d_keys = place(center[0] + from_heads(part_dk), totals[:, D : 2 * D])
    d_values = place(center[1] + from_heads(part_dv), totals[:, 2 * D :])
    return (
        out_full,
        d_queries.astype(jnp.bfloat16),
        d_keys.astype(jnp.bfloat16),
        d_values.astype(jnp.bfloat16),
    )


def solution(mesh):
    rows = P(("groups", "seq"), None)
    return jax.shard_map(
        local,
        mesh=mesh,
        in_specs=(rows, rows, rows, rows, P("groups"), P("groups")),
        out_specs=(rows, rows, rows, rows),
        check_vma=False,
    )
```

```python
import jax
import jax.numpy as jnp
from jax import lax
from jax.sharding import PartitionSpec as P
from jax.experimental import pallas as pl
from jax.experimental.pallas import tpu as pltpu

D = 768
HEADS = 12
BLOCK = 64
REACH = 3
GLOBALS = 128
HEAD_DIM = 64
TILE_BLOCKS = 2

neg_large = -1e30


def mixed(form, left, right):
    return jnp.einsum(form, left, right, preferred_element_type=jnp.float32)


def to_heads(array):
    rows = array.shape[0]
    return jnp.transpose(array.reshape(rows, HEADS, HEAD_DIM), (1, 0, 2))


def from_heads(array):
    rows = array.shape[1]
    return jnp.transpose(array, (1, 0, 2)).reshape(rows, D)


def halo(cells, width):
    count = lax.axis_size("seq")
    ends = count - 1
    head = lax.slice_in_dim(cells, 0, width, axis=1)
    tail = lax.slice_in_dim(cells, cells.shape[1] - width, cells.shape[1], axis=1)
    from_left = lax.ppermute(tail, "seq", [(i, i + 1) for i in range(ends)])
    from_right = lax.ppermute(head, "seq", [(i + 1, i) for i in range(ends)])
    return from_left, from_right


def by_head(array):
    return array.reshape(array.shape[:-1] + (HEADS, HEAD_DIM))


def gather_small(part):
    count = lax.axis_size("seq")
    spread = jnp.broadcast_to(part[None], (count,) + part.shape)
    return lax.all_to_all(spread, "seq", 0, 0)


def reduce_own(full):
    count = lax.axis_size("seq")
    split = full.reshape((count, full.shape[0] // count) + full.shape[1:])
    return jnp.sum(lax.all_to_all(split, "seq", 0, 0), axis=0)


def key_flags(first_pos, span_len, glob_pos, lens_wide):
    places = first_pos + jnp.arange(span_len, dtype=jnp.int32)
    begin = jnp.asarray(first_pos // BLOCK + 2 * REACH, dtype=jnp.int32)
    lens = lax.dynamic_slice_in_dim(lens_wide, begin, span_len // BLOCK)
    inside = (jnp.arange(BLOCK, dtype=jnp.int32)[None, :] < lens[:, None]).reshape(span_len)
    marked = jnp.any(glob_pos[:, None] == places[None, :], axis=0)
    return (inside, marked)


def band_kernel(mask_ref, gmask_ref, keep_ref, q_ref, do_ref, kw_ref, vw_ref, kg_ref, vg_ref,
                out_ref, dq_ref, dkw_ref, dvw_ref, dkg_ref, dvg_ref):
    scale = HEAD_DIM ** (-0.5)
    tile = pl.program_id(1)
    tile_rows = q_ref.shape[0]
    win_rows = mask_ref.shape[2]
    start = pl.multiple_of(tile * tile_rows, tile_rows)
    f32 = jnp.float32
    bf16 = jnp.bfloat16
    nt = (((1,), (1,)), ((), ()))
    tn = (((0,), (0,)), ((), ()))

    @pl.when(tile == 0)
    def _():
        dkw_ref[...] = jnp.zeros_like(dkw_ref)
        dvw_ref[...] = jnp.zeros_like(dvw_ref)
        dkg_ref[...] = jnp.zeros_like(dkg_ref)
        dvg_ref[...] = jnp.zeros_like(dvg_ref)

    band_bias = mask_ref[0].astype(f32)
    glob_bias = gmask_ref[...]
    keep = keep_ref[...].astype(bf16)
    for head in range(q_ref.shape[1] // HEAD_DIM):
        lanes = slice(head * HEAD_DIM, (head + 1) * HEAD_DIM)
        q = q_ref[:, lanes] * jnp.asarray(scale, bf16)
        do = do_ref[:, lanes] * keep
        kwin = kw_ref[pl.ds(start, win_rows), lanes]
        vwin = vw_ref[pl.ds(start, win_rows), lanes]
        kg = kg_ref[:, lanes]
        vg = vg_ref[:, lanes]
        s_b = lax.dot_general(q, kwin, nt, preferred_element_type=f32) + band_bias
        s_g = lax.dot_general(q, kg, nt, preferred_element_type=f32) + glob_bias
        top = jnp.maximum(jnp.max(s_b, axis=1, keepdims=True), jnp.max(s_g, axis=1, keepdims=True))
        e_b = jnp.exp(s_b - top)
        e_g = jnp.exp(s_g - top)
        inv = 1.0 / (jnp.sum(e_b, axis=1, keepdims=True) + jnp.sum(e_g, axis=1, keepdims=True))
        p_b = e_b * inv
        p_g = e_g * inv
        w_b = p_b.astype(bf16)
        w_g = p_g.astype(bf16)
        out = jnp.dot(w_b, vwin, preferred_element_type=f32) + jnp.dot(
            w_g, vg, preferred_element_type=f32
        )
        out_ref[:, lanes] = out
        delta = jnp.sum(
            do.astype(f32) * out.astype(bf16).astype(f32), axis=1, keepdims=True
        )
        dp_b = lax.dot_general(do, vwin, nt, preferred_element_type=f32)
        dp_g = lax.dot_general(do, vg, nt, preferred_element_type=f32)
        ds_b = (p_b * (dp_b - delta)).astype(bf16)
        ds_g = (p_g * (dp_g - delta)).astype(bf16)
        dq = jnp.dot(ds_b, kwin, preferred_element_type=f32) + jnp.dot(
            ds_g, kg, preferred_element_type=f32
        )
        dq_ref[:, lanes] = dq * scale
        dkw_ref[pl.ds(start, win_rows), lanes] += lax.dot_general(ds_b, q, tn, preferred_element_type=f32)
        dvw_ref[pl.ds(start, win_rows), lanes] += lax.dot_general(w_b, do, tn, preferred_element_type=f32)
        dkg_ref[:, lanes] += lax.dot_general(ds_g, q, tn, preferred_element_type=f32)
        dvg_ref[:, lanes] += lax.dot_general(w_g, do, tn, preferred_element_type=f32)


def band_call(mask, gmask, keep, queries, d_out, key_wide, value_wide, key_glob, value_glob, interpret=False):
    rows = queries.shape[0]
    wide_rows = key_wide.shape[0]
    slots = key_glob.shape[0]
    tiles, tile_rows, win_rows = mask.shape
    lanes = 2 * HEAD_DIM
    pairs = D // lanes
    f32 = jnp.float32
    row_spec = pl.BlockSpec((tile_rows, lanes), lambda p, t: (t, p))
    wide_spec = pl.BlockSpec((wide_rows, lanes), lambda p, t: (0, p))
    glob_spec = pl.BlockSpec((slots, lanes), lambda p, t: (0, p))
    return pl.pallas_call(
        band_kernel,
        grid=(pairs, tiles),
        in_specs=[
            pl.BlockSpec((1, tile_rows, win_rows), lambda p, t: (t, 0, 0)),
            pl.BlockSpec((1, slots), lambda p, t: (0, 0)),
            pl.BlockSpec((tile_rows, 1), lambda p, t: (t, 0)),
            row_spec,
            row_spec,
            wide_spec,
            wide_spec,
            glob_spec,
            glob_spec,
        ],
        out_specs=[row_spec, row_spec, wide_spec, wide_spec, glob_spec, glob_spec],
        out_shape=[
            jax.ShapeDtypeStruct((rows, D), f32),
            jax.ShapeDtypeStruct((rows, D), f32),
            jax.ShapeDtypeStruct((wide_rows, D), f32),
            jax.ShapeDtypeStruct((wide_rows, D), f32),
            jax.ShapeDtypeStruct((slots, D), f32),
            jax.ShapeDtypeStruct((slots, D), f32),
        ],
        compiler_params=pltpu.CompilerParams(dimension_semantics=("arbitrary", "arbitrary")),
        interpret=interpret,
    )(mask, gmask, keep, queries, d_out, key_wide, value_wide, key_glob, value_glob)


def band_kernel_t(mask_ref, gmask_ref, keep_ref, keep_row_ref, q_ref, qt_ref, do_ref, dot_ref,
                  kw_ref, kt_ref, vw_ref, vt_ref, kg_ref, kgt_ref, vg_ref, vgt_ref,
                  out_ref, dq_ref, dkw_ref, dvw_ref, dkg_ref, dvg_ref):
    scale = HEAD_DIM ** (-0.5)
    tile = pl.program_id(1)
    tile_rows = q_ref.shape[0]
    win_rows = mask_ref.shape[1]
    start = pl.multiple_of(tile * tile_rows, tile_rows)
    f32 = jnp.float32
    bf16 = jnp.bfloat16

    @pl.when(tile == 0)
    def _():
        dkw_ref[...] = jnp.zeros_like(dkw_ref)
        dvw_ref[...] = jnp.zeros_like(dvw_ref)
        dkg_ref[...] = jnp.zeros_like(dkg_ref)
        dvg_ref[...] = jnp.zeros_like(dvg_ref)

    band_bias = mask_ref[0].astype(f32)
    glob_bias = gmask_ref[...]
    keep = keep_ref[...].astype(bf16)
    keep_row = keep_row_ref[...].astype(bf16)
    shrink = jnp.asarray(scale, bf16)
    for head in range(q_ref.shape[1] // HEAD_DIM):
        lanes = slice(head * HEAD_DIM, (head + 1) * HEAD_DIM)
        q = q_ref[:, lanes] * shrink
        qt = qt_ref[lanes, :] * shrink
        do = do_ref[:, lanes] * keep
        dot = dot_ref[lanes, :] * keep_row
        kwin = kw_ref[pl.ds(start, win_rows), lanes]
        ktwin = kt_ref[lanes, pl.ds(start, win_rows)]
        vwin = vw_ref[pl.ds(start, win_rows), lanes]
        vtwin = vt_ref[lanes, pl.ds(start, win_rows)]
        kg = kg_ref[:, lanes]
        kgt = kgt_ref[lanes, :]
        vg = vg_ref[:, lanes]
        vgt = vgt_ref[lanes, :]
        s_b = jnp.dot(kwin, qt, preferred_element_type=f32) + band_bias
        s_g = jnp.dot(kg, qt, preferred_element_type=f32) + glob_bias
        top = jnp.maximum(jnp.max(s_b, axis=0, keepdims=True), jnp.max(s_g, axis=0, keepdims=True))
        e_b = jnp.exp(s_b - top)
        e_g = jnp.exp(s_g - top)
        inv = 1.0 / (jnp.sum(e_b, axis=0, keepdims=True) + jnp.sum(e_g, axis=0, keepdims=True))
        p_b = e_b * inv
        p_g = e_g * inv
        w_b = p_b.astype(bf16)
        w_g = p_g.astype(bf16)
        out = jnp.dot(vtwin, w_b, preferred_element_type=f32) + jnp.dot(
            vgt, w_g, preferred_element_type=f32
        )
        out_ref[lanes, :] = out
        delta = jnp.sum(
            dot.astype(f32) * out.astype(bf16).astype(f32), axis=0, keepdims=True
        )
        dp_b = jnp.dot(vwin, dot, preferred_element_type=f32)
        dp_g = jnp.dot(vg, dot, preferred_element_type=f32)
        ds_b = (p_b * (dp_b - delta)).astype(bf16)
        ds_g = (p_g * (dp_g - delta)).astype(bf16)
        dq = jnp.dot(ktwin, ds_b, preferred_element_type=f32) + jnp.dot(
            kgt, ds_g, preferred_element_type=f32
        )
        dq_ref[lanes, :] = dq * scale
        dkw_ref[pl.ds(start, win_rows), lanes] += jnp.dot(ds_b, q, preferred_element_type=f32)
        dvw_ref[pl.ds(start, win_rows), lanes] += jnp.dot(w_b, do, preferred_element_type=f32)
        dkg_ref[:, lanes] += jnp.dot(ds_g, q, preferred_element_type=f32)
        dvg_ref[:, lanes] += jnp.dot(w_g, do, preferred_element_type=f32)


def band_call_t(mask, gmask, keep, queries, d_out, key_wide, value_wide, key_glob, value_glob, interpret=False):
    rows = queries.shape[0]
    wide_rows = key_wide.shape[0]
    slots = key_glob.shape[0]
    tiles, tile_rows, win_rows = mask.shape
    lanes = 2 * HEAD_DIM
    pairs = D // lanes
    f32 = jnp.float32
    row_spec = pl.BlockSpec((tile_rows, lanes), lambda p, t: (t, p))
    col_spec = pl.BlockSpec((lanes, tile_rows), lambda p, t: (p, t))
    wide_spec = pl.BlockSpec((wide_rows, lanes), lambda p, t: (0, p))
    wide_t_spec = pl.BlockSpec((lanes, wide_rows), lambda p, t: (p, 0))
    glob_spec = pl.BlockSpec((slots, lanes), lambda p, t: (0, p))
    glob_t_spec = pl.BlockSpec((lanes, slots), lambda p, t: (p, 0))
    out_t, dq_t, dkw, dvw, dkg, dvg = pl.pallas_call(
        band_kernel_t,
        grid=(pairs, tiles),
        in_specs=[
            pl.BlockSpec((1, win_rows, tile_rows), lambda p, t: (t, 0, 0)),
            pl.BlockSpec((slots, 1), lambda p, t: (0, 0)),
            pl.BlockSpec((tile_rows, 1), lambda p, t: (t, 0)),
            pl.BlockSpec((1, tile_rows), lambda p, t: (0, t)),
            row_spec,
            col_spec,
            row_spec,
            col_spec,
            wide_spec,
            wide_t_spec,
            wide_spec,
            wide_t_spec,
            glob_spec,
            glob_t_spec,
            glob_spec,
            glob_t_spec,
        ],
        out_specs=[col_spec, col_spec, wide_spec, wide_spec, glob_spec, glob_spec],
        out_shape=[
            jax.ShapeDtypeStruct((D, rows), f32),
            jax.ShapeDtypeStruct((D, rows), f32),
            jax.ShapeDtypeStruct((wide_rows, D), f32),
            jax.ShapeDtypeStruct((wide_rows, D), f32),
            jax.ShapeDtypeStruct((slots, D), f32),
            jax.ShapeDtypeStruct((slots, D), f32),
        ],
        compiler_params=pltpu.CompilerParams(dimension_semantics=("arbitrary", "arbitrary")),
        interpret=interpret,
    )(
        jnp.transpose(mask, (0, 2, 1)),
        jnp.transpose(gmask),
        keep,
        jnp.transpose(keep),
        queries,
        jnp.transpose(queries),
        d_out,
        jnp.transpose(d_out),
        key_wide,
        jnp.transpose(key_wide),
        value_wide,
        jnp.transpose(value_wide),
        key_glob,
        jnp.transpose(key_glob),
        value_glob,
        jnp.transpose(value_glob),
    )
    return jnp.transpose(out_t), jnp.transpose(dq_t), dkw, dvw, dkg, dvg


def local(queries, keys, values, d_out, glob_pos, block_len):
    scale = HEAD_DIM ** (-0.5)
    rows = queries.shape[0]
    reach_rows = REACH * BLOCK
    tile_rows = TILE_BLOCKS * BLOCK
    tiles = rows // tile_rows
    win_rows = tile_rows + 2 * reach_rows
    wide_rows = rows + 2 * reach_rows
    first_row = lax.axis_index("seq") * rows
    lens_wide = jnp.pad(block_len, 2 * REACH)

    places = first_row + jnp.arange(rows, dtype=jnp.int32)
    marked_rows = jnp.any(glob_pos[:, None] == places[None, :], axis=0)
    local_pos = glob_pos - first_row
    is_local = (local_pos >= 0) & (local_pos < rows)
    local_index = jnp.where(is_local, local_pos, rows)
    inside_rows, _ = key_flags(first_row, rows, glob_pos, lens_wide)

    count = lax.axis_size("seq")
    own_blocks = rows // BLOCK
    slots = own_blocks * count
    glob_block = glob_pos // BLOCK
    slot_valid = jnp.zeros((slots,), bool).at[glob_block].set(True, mode="drop")
    own_slot = lax.axis_index("seq") * own_blocks + jnp.arange(own_blocks, dtype=jnp.int32)
    own_match = glob_block[None, :] == own_slot[:, None]
    own_has = jnp.any(own_match, axis=1)
    own_pos = jnp.sum(jnp.where(own_match, glob_pos[None, :], 0), axis=1) - first_row
    own_offset = own_pos - BLOCK * jnp.arange(own_blocks, dtype=jnp.int32)
    own_row = own_has[:, None] & (jnp.arange(BLOCK, dtype=jnp.int32)[None, :] == own_offset[:, None])

    def place(base, extra):
        shaped = base.reshape(own_blocks, BLOCK, D)
        return jnp.where(own_row[:, :, None], shaped + extra[:, None, :], shaped).reshape(rows, D)

    own_pick = (
        own_has[:, None] & (jnp.arange(rows, dtype=jnp.int32)[None, :] == own_pos[:, None])
    ).astype(jnp.bfloat16)
    picked = jnp.stack(
        [
            jnp.dot(own_pick, source, preferred_element_type=jnp.float32).astype(jnp.bfloat16)
            for source in (queries, keys, values, d_out)
        ]
    )
    shared = jnp.transpose(gather_small(picked), (1, 0, 2, 3)).reshape(4, slots, D)
    qg = to_heads(shared[0])
    kg = to_heads(shared[1])
    vg = to_heads(shared[2])
    dog = to_heads(shared[3])

    pair = jnp.stack([keys, values])
    from_left, from_right = halo(pair, reach_rows)
    pair_wide = jnp.concatenate([from_left, pair, from_right], axis=1)
    k_h = to_heads(keys)
    v_h = to_heads(values)

    inside_wide, marked_wide = key_flags(first_row - reach_rows, wide_rows, glob_pos, lens_wide)
    allowed_wide = inside_wide & jnp.logical_not(marked_wide)

    allowed_t = jnp.stack(
        [lax.slice_in_dim(allowed_wide, t * tile_rows, t * tile_rows + win_rows) for t in range(tiles)]
    )
    q_block = (jnp.arange(rows, dtype=jnp.int32) // BLOCK).reshape(tiles, tile_rows)
    k_block = jnp.stack(
        [t * TILE_BLOCKS + jnp.arange(win_rows, dtype=jnp.int32) // BLOCK - REACH for t in range(tiles)]
    )
    near = jnp.abs(q_block[:, :, None] - k_block[:, None, :]) <= REACH
    band_mask = near & allowed_t[:, None, :]
    band_out, band_dq, dk_wide, dv_wide, dk_glob, dv_glob = band_call_t(
        jnp.where(band_mask, 0.0, neg_large).astype(jnp.bfloat16),
        jnp.where(slot_valid, 0.0, neg_large).astype(jnp.float32)[None, :],
        jnp.logical_not(marked_rows).astype(jnp.float32)[:, None],
        queries,
        d_out,
        pair_wide[0],
        pair_wide[1],
        shared[1],
        shared[2],
    )

    g_score = mixed("hge,hre->hgr", qg, k_h) * scale
    g_score = jnp.where(inside_rows[None, None, :], g_score, neg_large)
    g_top = jnp.max(g_score, axis=-1)
    g_sum = jnp.sum(jnp.exp(g_score - g_top[..., None]), axis=-1)
    stats = gather_small(jnp.stack([g_top, g_sum]))
    all_top = stats[:, 0]
    top_glob = jnp.max(all_top, axis=0)
    sum_glob = jnp.sum(stats[:, 1] * jnp.exp(all_top - top_glob[None]), axis=0)
    lse_glob = top_glob + jnp.log(sum_glob)
    g_prob = jnp.where(slot_valid[None, :, None], jnp.exp(g_score - lse_glob[..., None]), 0.0)
    g_weight = g_prob.astype(jnp.bfloat16)
    out_own = reduce_own(from_heads(mixed("hgr,hre->hge", g_weight, v_h)))
    out_own16 = out_own.astype(jnp.bfloat16)
    delta_own = jnp.sum(
        by_head(picked[3]).astype(jnp.float32) * by_head(out_own16).astype(jnp.float32), axis=-1
    )
    delta_g = jnp.transpose(gather_small(delta_own).reshape(slots, HEADS))
    band_out16 = band_out.astype(jnp.bfloat16)
    out_full = jnp.where(
        own_row[:, :, None], out_own16[:, None, :], band_out16.reshape(own_blocks, BLOCK, D)
    ).reshape(rows, D)

    grad_wide = jnp.stack([dk_wide, dv_wide])
    rims = jnp.concatenate(
        [grad_wide[:, :reach_rows], grad_wide[:, wide_rows - reach_rows :]], axis=1
    )
    back_left, back_right = halo(rims, reach_rows)
    center = grad_wide[:, reach_rows : reach_rows + rows]
    center = center.at[:, :reach_rows].add(back_left).at[:, rows - reach_rows :].add(back_right)

    g_dprob = mixed("hge,hre->hgr", dog, v_h)
    g_dscore = (g_prob * (g_dprob - delta_g[..., None])).astype(jnp.bfloat16)
    row_dq = mixed("hgr,hre->hge", g_dscore, k_h) * scale
    part_dk = mixed("hgr,hge->hre", g_dscore, qg) * scale
    part_dv = mixed("hgr,hge->hre", g_weight, dog)

    totals = reduce_own(
        jnp.concatenate([from_heads(row_dq), dk_glob, dv_glob], axis=1)
    )
    d_queries = place(band_dq, totals[:, :D])
    d_keys = place(center[0] + from_heads(part_dk), totals[:, D : 2 * D])
    d_values = place(center[1] + from_heads(part_dv), totals[:, 2 * D :])
    return (
        out_full,
        d_queries.astype(jnp.bfloat16),
        d_keys.astype(jnp.bfloat16),
        d_values.astype(jnp.bfloat16),
    )


def solution(mesh):
    rows = P(("groups", "seq"), None)
    return jax.shard_map(
        local,
        mesh=mesh,
        in_specs=(rows, rows, rows, rows, P("groups"), P("groups")),
        out_specs=(rows, rows, rows, rows),
        check_vma=False,
    )
```

```python
import jax
import jax.numpy as jnp
from jax import lax
from jax.sharding import PartitionSpec as P
from jax.experimental import pallas as pl
from jax.experimental.pallas import tpu as pltpu

D = 768
HEADS = 12
BLOCK = 64
REACH = 3
GLOBALS = 128
HEAD_DIM = 64
TILE_BLOCKS = 4

neg_large = -1e30


def mixed(form, left, right):
    return jnp.einsum(form, left, right, preferred_element_type=jnp.float32)


def to_heads(array):
    rows = array.shape[0]
    return jnp.transpose(array.reshape(rows, HEADS, HEAD_DIM), (1, 0, 2))


def from_heads(array):
    rows = array.shape[1]
    return jnp.transpose(array, (1, 0, 2)).reshape(rows, D)


def halo(cells, width):
    count = lax.axis_size("seq")
    ends = count - 1
    head = lax.slice_in_dim(cells, 0, width, axis=1)
    tail = lax.slice_in_dim(cells, cells.shape[1] - width, cells.shape[1], axis=1)
    from_left = lax.ppermute(tail, "seq", [(i, i + 1) for i in range(ends)])
    from_right = lax.ppermute(head, "seq", [(i + 1, i) for i in range(ends)])
    return from_left, from_right


def by_head(array):
    return array.reshape(array.shape[:-1] + (HEADS, HEAD_DIM))


def gather_small(part):
    count = lax.axis_size("seq")
    spread = jnp.broadcast_to(part[None], (count,) + part.shape)
    return lax.all_to_all(spread, "seq", 0, 0)


def reduce_own(full):
    count = lax.axis_size("seq")
    split = full.reshape((count, full.shape[0] // count) + full.shape[1:])
    return jnp.sum(lax.all_to_all(split, "seq", 0, 0), axis=0)


def key_flags(first_pos, span_len, glob_pos, lens_wide):
    places = first_pos + jnp.arange(span_len, dtype=jnp.int32)
    begin = jnp.asarray(first_pos // BLOCK + 2 * REACH, dtype=jnp.int32)
    lens = lax.dynamic_slice_in_dim(lens_wide, begin, span_len // BLOCK)
    inside = (jnp.arange(BLOCK, dtype=jnp.int32)[None, :] < lens[:, None]).reshape(span_len)
    marked = jnp.any(glob_pos[:, None] == places[None, :], axis=0)
    return (inside, marked)


def band_kernel(mask_ref, gmask_ref, keep_ref, q_ref, do_ref, kw_ref, vw_ref, kg_ref, vg_ref,
                out_ref, dq_ref, dkw_ref, dvw_ref, dkg_ref, dvg_ref):
    scale = HEAD_DIM ** (-0.5)
    tile = pl.program_id(1)
    tile_rows = q_ref.shape[0]
    win_rows = mask_ref.shape[2]
    start = pl.multiple_of(tile * tile_rows, tile_rows)
    f32 = jnp.float32
    bf16 = jnp.bfloat16
    nt = (((1,), (1,)), ((), ()))
    tn = (((0,), (0,)), ((), ()))

    @pl.when(tile == 0)
    def _():
        dkw_ref[...] = jnp.zeros_like(dkw_ref)
        dvw_ref[...] = jnp.zeros_like(dvw_ref)
        dkg_ref[...] = jnp.zeros_like(dkg_ref)
        dvg_ref[...] = jnp.zeros_like(dvg_ref)

    band_bias = mask_ref[0]
    glob_bias = gmask_ref[...]
    keep = keep_ref[...].astype(bf16)
    for head in range(q_ref.shape[1] // HEAD_DIM):
        lanes = slice(head * HEAD_DIM, (head + 1) * HEAD_DIM)
        q = q_ref[:, lanes] * jnp.asarray(scale, bf16)
        do = do_ref[:, lanes] * keep
        kwin = kw_ref[pl.ds(start, win_rows), lanes]
        vwin = vw_ref[pl.ds(start, win_rows), lanes]
        kg = kg_ref[:, lanes]
        vg = vg_ref[:, lanes]
        s_b = lax.dot_general(q, kwin, nt, preferred_element_type=f32) + band_bias
        s_g = lax.dot_general(q, kg, nt, preferred_element_type=f32) + glob_bias
        top = jnp.maximum(jnp.max(s_b, axis=1, keepdims=True), jnp.max(s_g, axis=1, keepdims=True))
        e_b = jnp.exp(s_b - top)
        e_g = jnp.exp(s_g - top)
        inv = 1.0 / (jnp.sum(e_b, axis=1, keepdims=True) + jnp.sum(e_g, axis=1, keepdims=True))
        p_b = e_b * inv
        p_g = e_g * inv
        w_b = p_b.astype(bf16)
        w_g = p_g.astype(bf16)
        out = jnp.dot(w_b, vwin, preferred_element_type=f32) + jnp.dot(
            w_g, vg, preferred_element_type=f32
        )
        out_ref[:, lanes] = out
        delta = jnp.sum(
            do.astype(f32) * out.astype(bf16).astype(f32), axis=1, keepdims=True
        )
        dp_b = lax.dot_general(do, vwin, nt, preferred_element_type=f32)
        dp_g = lax.dot_general(do, vg, nt, preferred_element_type=f32)
        ds_b = (p_b * (dp_b - delta)).astype(bf16)
        ds_g = (p_g * (dp_g - delta)).astype(bf16)
        dq = jnp.dot(ds_b, kwin, preferred_element_type=f32) + jnp.dot(
            ds_g, kg, preferred_element_type=f32
        )
        dq_ref[:, lanes] = dq * scale
        dkw_ref[pl.ds(start, win_rows), lanes] += lax.dot_general(ds_b, q, tn, preferred_element_type=f32)
        dvw_ref[pl.ds(start, win_rows), lanes] += lax.dot_general(w_b, do, tn, preferred_element_type=f32)
        dkg_ref[:, lanes] += lax.dot_general(ds_g, q, tn, preferred_element_type=f32)
        dvg_ref[:, lanes] += lax.dot_general(w_g, do, tn, preferred_element_type=f32)


def band_call(mask, gmask, keep, queries, d_out, key_wide, value_wide, key_glob, value_glob, interpret=False):
    rows = queries.shape[0]
    wide_rows = key_wide.shape[0]
    slots = key_glob.shape[0]
    tiles, tile_rows, win_rows = mask.shape
    lanes = 2 * HEAD_DIM
    pairs = D // lanes
    f32 = jnp.float32
    row_spec = pl.BlockSpec((tile_rows, lanes), lambda p, t: (t, p))
    wide_spec = pl.BlockSpec((wide_rows, lanes), lambda p, t: (0, p))
    glob_spec = pl.BlockSpec((slots, lanes), lambda p, t: (0, p))
    return pl.pallas_call(
        band_kernel,
        grid=(pairs, tiles),
        in_specs=[
            pl.BlockSpec((1, tile_rows, win_rows), lambda p, t: (t, 0, 0)),
            pl.BlockSpec((1, slots), lambda p, t: (0, 0)),
            pl.BlockSpec((tile_rows, 1), lambda p, t: (t, 0)),
            row_spec,
            row_spec,
            wide_spec,
            wide_spec,
            glob_spec,
            glob_spec,
        ],
        out_specs=[row_spec, row_spec, wide_spec, wide_spec, glob_spec, glob_spec],
        out_shape=[
            jax.ShapeDtypeStruct((rows, D), f32),
            jax.ShapeDtypeStruct((rows, D), f32),
            jax.ShapeDtypeStruct((wide_rows, D), f32),
            jax.ShapeDtypeStruct((wide_rows, D), f32),
            jax.ShapeDtypeStruct((slots, D), f32),
            jax.ShapeDtypeStruct((slots, D), f32),
        ],
        compiler_params=pltpu.CompilerParams(dimension_semantics=("arbitrary", "arbitrary")),
        interpret=interpret,
    )(mask, gmask, keep, queries, d_out, key_wide, value_wide, key_glob, value_glob)


def band_kernel_t(mask_ref, gmask_ref, keep_ref, keep_row_ref, q_ref, qt_ref, do_ref, dot_ref,
                  kw_ref, kt_ref, vw_ref, vt_ref, kg_ref, kgt_ref, vg_ref, vgt_ref,
                  out_ref, dq_ref, dkw_ref, dvw_ref, dkg_ref, dvg_ref):
    scale = HEAD_DIM ** (-0.5)
    tile = pl.program_id(1)
    tile_rows = q_ref.shape[0]
    win_rows = mask_ref.shape[1]
    start = pl.multiple_of(tile * tile_rows, tile_rows)
    f32 = jnp.float32
    bf16 = jnp.bfloat16

    @pl.when(tile == 0)
    def _():
        dkw_ref[...] = jnp.zeros_like(dkw_ref)
        dvw_ref[...] = jnp.zeros_like(dvw_ref)
        dkg_ref[...] = jnp.zeros_like(dkg_ref)
        dvg_ref[...] = jnp.zeros_like(dvg_ref)

    band_bias = mask_ref[0]
    glob_bias = gmask_ref[...]
    keep = keep_ref[...].astype(bf16)
    keep_row = keep_row_ref[...].astype(bf16)
    shrink = jnp.asarray(scale, bf16)
    for head in range(q_ref.shape[1] // HEAD_DIM):
        lanes = slice(head * HEAD_DIM, (head + 1) * HEAD_DIM)
        q = q_ref[:, lanes] * shrink
        qt = qt_ref[lanes, :] * shrink
        do = do_ref[:, lanes] * keep
        dot = dot_ref[lanes, :] * keep_row
        kwin = kw_ref[pl.ds(start, win_rows), lanes]
        ktwin = kt_ref[lanes, pl.ds(start, win_rows)]
        vwin = vw_ref[pl.ds(start, win_rows), lanes]
        vtwin = vt_ref[lanes, pl.ds(start, win_rows)]
        kg = kg_ref[:, lanes]
        kgt = kgt_ref[lanes, :]
        vg = vg_ref[:, lanes]
        vgt = vgt_ref[lanes, :]
        s_b = jnp.dot(kwin, qt, preferred_element_type=f32) + band_bias
        s_g = jnp.dot(kg, qt, preferred_element_type=f32) + glob_bias
        top = jnp.maximum(jnp.max(s_b, axis=0, keepdims=True), jnp.max(s_g, axis=0, keepdims=True))
        e_b = jnp.exp(s_b - top)
        e_g = jnp.exp(s_g - top)
        inv = 1.0 / (jnp.sum(e_b, axis=0, keepdims=True) + jnp.sum(e_g, axis=0, keepdims=True))
        p_b = e_b * inv
        p_g = e_g * inv
        w_b = p_b.astype(bf16)
        w_g = p_g.astype(bf16)
        out = jnp.dot(vtwin, w_b, preferred_element_type=f32) + jnp.dot(
            vgt, w_g, preferred_element_type=f32
        )
        out_ref[lanes, :] = out
        delta = jnp.sum(
            dot.astype(f32) * out.astype(bf16).astype(f32), axis=0, keepdims=True
        )
        dp_b = jnp.dot(vwin, dot, preferred_element_type=f32)
        dp_g = jnp.dot(vg, dot, preferred_element_type=f32)
        ds_b = (p_b * (dp_b - delta)).astype(bf16)
        ds_g = (p_g * (dp_g - delta)).astype(bf16)
        dq = jnp.dot(ktwin, ds_b, preferred_element_type=f32) + jnp.dot(
            kgt, ds_g, preferred_element_type=f32
        )
        dq_ref[lanes, :] = dq * scale
        dkw_ref[pl.ds(start, win_rows), lanes] += jnp.dot(ds_b, q, preferred_element_type=f32)
        dvw_ref[pl.ds(start, win_rows), lanes] += jnp.dot(w_b, do, preferred_element_type=f32)
        dkg_ref[:, lanes] += jnp.dot(ds_g, q, preferred_element_type=f32)
        dvg_ref[:, lanes] += jnp.dot(w_g, do, preferred_element_type=f32)


def band_call_t(mask, gmask, keep, queries, d_out, key_wide, value_wide, key_glob, value_glob, interpret=False):
    rows = queries.shape[0]
    wide_rows = key_wide.shape[0]
    slots = key_glob.shape[0]
    tiles, tile_rows, win_rows = mask.shape
    lanes = 2 * HEAD_DIM
    pairs = D // lanes
    f32 = jnp.float32
    row_spec = pl.BlockSpec((tile_rows, lanes), lambda p, t: (t, p))
    col_spec = pl.BlockSpec((lanes, tile_rows), lambda p, t: (p, t))
    wide_spec = pl.BlockSpec((wide_rows, lanes), lambda p, t: (0, p))
    wide_t_spec = pl.BlockSpec((lanes, wide_rows), lambda p, t: (p, 0))
    glob_spec = pl.BlockSpec((slots, lanes), lambda p, t: (0, p))
    glob_t_spec = pl.BlockSpec((lanes, slots), lambda p, t: (p, 0))
    out_t, dq_t, dkw, dvw, dkg, dvg = pl.pallas_call(
        band_kernel_t,
        grid=(pairs, tiles),
        in_specs=[
            pl.BlockSpec((1, win_rows, tile_rows), lambda p, t: (t, 0, 0)),
            pl.BlockSpec((slots, 1), lambda p, t: (0, 0)),
            pl.BlockSpec((tile_rows, 1), lambda p, t: (t, 0)),
            pl.BlockSpec((1, tile_rows), lambda p, t: (0, t)),
            row_spec,
            col_spec,
            row_spec,
            col_spec,
            wide_spec,
            wide_t_spec,
            wide_spec,
            wide_t_spec,
            glob_spec,
            glob_t_spec,
            glob_spec,
            glob_t_spec,
        ],
        out_specs=[col_spec, col_spec, wide_spec, wide_spec, glob_spec, glob_spec],
        out_shape=[
            jax.ShapeDtypeStruct((D, rows), f32),
            jax.ShapeDtypeStruct((D, rows), f32),
            jax.ShapeDtypeStruct((wide_rows, D), f32),
            jax.ShapeDtypeStruct((wide_rows, D), f32),
            jax.ShapeDtypeStruct((slots, D), f32),
            jax.ShapeDtypeStruct((slots, D), f32),
        ],
        compiler_params=pltpu.CompilerParams(dimension_semantics=("arbitrary", "arbitrary")),
        interpret=interpret,
    )(
        jnp.transpose(mask, (0, 2, 1)),
        jnp.transpose(gmask),
        keep,
        jnp.transpose(keep),
        queries,
        jnp.transpose(queries),
        d_out,
        jnp.transpose(d_out),
        key_wide,
        jnp.transpose(key_wide),
        value_wide,
        jnp.transpose(value_wide),
        key_glob,
        jnp.transpose(key_glob),
        value_glob,
        jnp.transpose(value_glob),
    )
    return jnp.transpose(out_t), jnp.transpose(dq_t), dkw, dvw, dkg, dvg


def local(queries, keys, values, d_out, glob_pos, block_len):
    scale = HEAD_DIM ** (-0.5)
    rows = queries.shape[0]
    reach_rows = REACH * BLOCK
    tile_rows = TILE_BLOCKS * BLOCK
    tiles = rows // tile_rows
    win_rows = tile_rows + 2 * reach_rows
    wide_rows = rows + 2 * reach_rows
    first_row = lax.axis_index("seq") * rows
    lens_wide = jnp.pad(block_len, 2 * REACH)

    places = first_row + jnp.arange(rows, dtype=jnp.int32)
    marked_rows = jnp.any(glob_pos[:, None] == places[None, :], axis=0)
    local_pos = glob_pos - first_row
    is_local = (local_pos >= 0) & (local_pos < rows)
    local_index = jnp.where(is_local, local_pos, rows)
    inside_rows, _ = key_flags(first_row, rows, glob_pos, lens_wide)

    count = lax.axis_size("seq")
    own_blocks = rows // BLOCK
    slots = own_blocks * count
    glob_block = glob_pos // BLOCK
    slot_valid = jnp.zeros((slots,), bool).at[glob_block].set(True, mode="drop")
    own_slot = lax.axis_index("seq") * own_blocks + jnp.arange(own_blocks, dtype=jnp.int32)
    own_match = glob_block[None, :] == own_slot[:, None]
    own_has = jnp.any(own_match, axis=1)
    own_pos = jnp.sum(jnp.where(own_match, glob_pos[None, :], 0), axis=1) - first_row
    own_offset = own_pos - BLOCK * jnp.arange(own_blocks, dtype=jnp.int32)
    own_row = own_has[:, None] & (jnp.arange(BLOCK, dtype=jnp.int32)[None, :] == own_offset[:, None])

    def place(base, extra):
        shaped = base.reshape(own_blocks, BLOCK, D)
        return jnp.where(own_row[:, :, None], shaped + extra[:, None, :], shaped).reshape(rows, D)

    own_pick = (
        own_has[:, None] & (jnp.arange(rows, dtype=jnp.int32)[None, :] == own_pos[:, None])
    ).astype(jnp.bfloat16)
    picked = jnp.stack(
        [
            jnp.dot(own_pick, source, preferred_element_type=jnp.float32).astype(jnp.bfloat16)
            for source in (queries, keys, values, d_out)
        ]
    )
    shared = jnp.transpose(gather_small(picked), (1, 0, 2, 3)).reshape(4, slots, D)
    qg = to_heads(shared[0])
    kg = to_heads(shared[1])
    vg = to_heads(shared[2])
    dog = to_heads(shared[3])

    pair = jnp.stack([keys, values])
    from_left, from_right = halo(pair, reach_rows)
    pair_wide = jnp.concatenate([from_left, pair, from_right], axis=1)
    k_h = to_heads(keys)
    v_h = to_heads(values)

    inside_wide, marked_wide = key_flags(first_row - reach_rows, wide_rows, glob_pos, lens_wide)
    allowed_wide = inside_wide & jnp.logical_not(marked_wide)

    allowed_t = jnp.stack(
        [lax.slice_in_dim(allowed_wide, t * tile_rows, t * tile_rows + win_rows) for t in range(tiles)]
    )
    q_block = (jnp.arange(rows, dtype=jnp.int32) // BLOCK).reshape(tiles, tile_rows)
    k_block = jnp.stack(
        [t * TILE_BLOCKS + jnp.arange(win_rows, dtype=jnp.int32) // BLOCK - REACH for t in range(tiles)]
    )
    near = jnp.abs(q_block[:, :, None] - k_block[:, None, :]) <= REACH
    band_mask = near & allowed_t[:, None, :]
    band_out, band_dq, dk_wide, dv_wide, dk_glob, dv_glob = band_call_t(
        jnp.where(band_mask, 0.0, neg_large).astype(jnp.float32),
        jnp.where(slot_valid, 0.0, neg_large).astype(jnp.float32)[None, :],
        jnp.logical_not(marked_rows).astype(jnp.float32)[:, None],
        queries,
        d_out,
        pair_wide[0],
        pair_wide[1],
        shared[1],
        shared[2],
    )

    g_score = mixed("hge,hre->hgr", qg, k_h) * scale
    g_score = jnp.where(inside_rows[None, None, :], g_score, neg_large)
    g_top = jnp.max(g_score, axis=-1)
    g_sum = jnp.sum(jnp.exp(g_score - g_top[..., None]), axis=-1)
    stats = gather_small(jnp.stack([g_top, g_sum]))
    all_top = stats[:, 0]
    top_glob = jnp.max(all_top, axis=0)
    sum_glob = jnp.sum(stats[:, 1] * jnp.exp(all_top - top_glob[None]), axis=0)
    lse_glob = top_glob + jnp.log(sum_glob)
    g_prob = jnp.where(slot_valid[None, :, None], jnp.exp(g_score - lse_glob[..., None]), 0.0)
    g_weight = g_prob.astype(jnp.bfloat16)
    out_own = reduce_own(from_heads(mixed("hgr,hre->hge", g_weight, v_h)))
    out_own16 = out_own.astype(jnp.bfloat16)
    delta_own = jnp.sum(
        by_head(picked[3]).astype(jnp.float32) * by_head(out_own16).astype(jnp.float32), axis=-1
    )
    delta_g = jnp.transpose(gather_small(delta_own).reshape(slots, HEADS))
    band_out16 = band_out.astype(jnp.bfloat16)
    out_full = jnp.where(
        own_row[:, :, None], out_own16[:, None, :], band_out16.reshape(own_blocks, BLOCK, D)
    ).reshape(rows, D)

    grad_wide = jnp.stack([dk_wide, dv_wide])
    rims = jnp.concatenate(
        [grad_wide[:, :reach_rows], grad_wide[:, wide_rows - reach_rows :]], axis=1
    )
    back_left, back_right = halo(rims, reach_rows)
    center = grad_wide[:, reach_rows : reach_rows + rows]
    center = center.at[:, :reach_rows].add(back_left).at[:, rows - reach_rows :].add(back_right)

    g_dprob = mixed("hge,hre->hgr", dog, v_h)
    g_dscore = (g_prob * (g_dprob - delta_g[..., None])).astype(jnp.bfloat16)
    row_dq = mixed("hgr,hre->hge", g_dscore, k_h) * scale
    part_dk = mixed("hgr,hge->hre", g_dscore, qg) * scale
    part_dv = mixed("hgr,hge->hre", g_weight, dog)

    totals = reduce_own(
        jnp.concatenate([from_heads(row_dq), dk_glob, dv_glob], axis=1)
    )
    d_queries = place(band_dq, totals[:, :D])
    d_keys = place(center[0] + from_heads(part_dk), totals[:, D : 2 * D])
    d_values = place(center[1] + from_heads(part_dv), totals[:, 2 * D :])
    return (
        out_full,
        d_queries.astype(jnp.bfloat16),
        d_keys.astype(jnp.bfloat16),
        d_values.astype(jnp.bfloat16),
    )


def solution(mesh):
    rows = P(("groups", "seq"), None)
    return jax.shard_map(
        local,
        mesh=mesh,
        in_specs=(rows, rows, rows, rows, P("groups"), P("groups")),
        out_specs=(rows, rows, rows, rows),
        check_vma=False,
    )
```

```python
import jax
import jax.numpy as jnp
from jax import lax
from jax.sharding import PartitionSpec as P
from jax.experimental import pallas as pl
from jax.experimental.pallas import tpu as pltpu

D = 768
HEADS = 12
BLOCK = 64
REACH = 3
GLOBALS = 128
HEAD_DIM = 64
TILE_BLOCKS = 8

neg_large = -1e30


def mixed(form, left, right):
    return jnp.einsum(form, left, right, preferred_element_type=jnp.float32)


def to_heads(array):
    rows = array.shape[0]
    return jnp.transpose(array.reshape(rows, HEADS, HEAD_DIM), (1, 0, 2))


def from_heads(array):
    rows = array.shape[1]
    return jnp.transpose(array, (1, 0, 2)).reshape(rows, D)


def halo(cells, width):
    count = lax.axis_size("seq")
    ends = count - 1
    head = lax.slice_in_dim(cells, 0, width, axis=1)
    tail = lax.slice_in_dim(cells, cells.shape[1] - width, cells.shape[1], axis=1)
    from_left = lax.ppermute(tail, "seq", [(i, i + 1) for i in range(ends)])
    from_right = lax.ppermute(head, "seq", [(i + 1, i) for i in range(ends)])
    return from_left, from_right


def by_head(array):
    return array.reshape(array.shape[:-1] + (HEADS, HEAD_DIM))


def gather_small(part):
    count = lax.axis_size("seq")
    spread = jnp.broadcast_to(part[None], (count,) + part.shape)
    return lax.all_to_all(spread, "seq", 0, 0)


def reduce_own(full):
    count = lax.axis_size("seq")
    split = full.reshape((count, full.shape[0] // count) + full.shape[1:])
    return jnp.sum(lax.all_to_all(split, "seq", 0, 0), axis=0)


def key_flags(first_pos, span_len, glob_pos, lens_wide):
    places = first_pos + jnp.arange(span_len, dtype=jnp.int32)
    begin = jnp.asarray(first_pos // BLOCK + 2 * REACH, dtype=jnp.int32)
    lens = lax.dynamic_slice_in_dim(lens_wide, begin, span_len // BLOCK)
    inside = (jnp.arange(BLOCK, dtype=jnp.int32)[None, :] < lens[:, None]).reshape(span_len)
    marked = jnp.any(glob_pos[:, None] == places[None, :], axis=0)
    return (inside, marked)


def band_kernel(mask_ref, gmask_ref, keep_ref, q_ref, do_ref, kw_ref, vw_ref, kg_ref, vg_ref,
                out_ref, dq_ref, dkw_ref, dvw_ref, dkg_ref, dvg_ref):
    scale = HEAD_DIM ** (-0.5)
    tile = pl.program_id(1)
    tile_rows = q_ref.shape[0]
    win_rows = mask_ref.shape[2]
    start = pl.multiple_of(tile * tile_rows, tile_rows)
    f32 = jnp.float32
    bf16 = jnp.bfloat16
    nt = (((1,), (1,)), ((), ()))
    tn = (((0,), (0,)), ((), ()))

    @pl.when(tile == 0)
    def _():
        dkw_ref[...] = jnp.zeros_like(dkw_ref)
        dvw_ref[...] = jnp.zeros_like(dvw_ref)
        dkg_ref[...] = jnp.zeros_like(dkg_ref)
        dvg_ref[...] = jnp.zeros_like(dvg_ref)

    band_bias = mask_ref[0]
    glob_bias = gmask_ref[...]
    keep = keep_ref[...].astype(bf16)
    for head in range(q_ref.shape[1] // HEAD_DIM):
        lanes = slice(head * HEAD_DIM, (head + 1) * HEAD_DIM)
        q = q_ref[:, lanes] * jnp.asarray(scale, bf16)
        do = do_ref[:, lanes] * keep
        kwin = kw_ref[pl.ds(start, win_rows), lanes]
        vwin = vw_ref[pl.ds(start, win_rows), lanes]
        kg = kg_ref[:, lanes]
        vg = vg_ref[:, lanes]
        s_b = lax.dot_general(q, kwin, nt, preferred_element_type=f32) + band_bias
        s_g = lax.dot_general(q, kg, nt, preferred_element_type=f32) + glob_bias
        top = jnp.maximum(jnp.max(s_b, axis=1, keepdims=True), jnp.max(s_g, axis=1, keepdims=True))
        e_b = jnp.exp(s_b - top)
        e_g = jnp.exp(s_g - top)
        inv = 1.0 / (jnp.sum(e_b, axis=1, keepdims=True) + jnp.sum(e_g, axis=1, keepdims=True))
        p_b = e_b * inv
        p_g = e_g * inv
        w_b = p_b.astype(bf16)
        w_g = p_g.astype(bf16)
        out = jnp.dot(w_b, vwin, preferred_element_type=f32) + jnp.dot(
            w_g, vg, preferred_element_type=f32
        )
        out_ref[:, lanes] = out
        delta = jnp.sum(
            do.astype(f32) * out.astype(bf16).astype(f32), axis=1, keepdims=True
        )
        dp_b = lax.dot_general(do, vwin, nt, preferred_element_type=f32)
        dp_g = lax.dot_general(do, vg, nt, preferred_element_type=f32)
        ds_b = (p_b * (dp_b - delta)).astype(bf16)
        ds_g = (p_g * (dp_g - delta)).astype(bf16)
        dq = jnp.dot(ds_b, kwin, preferred_element_type=f32) + jnp.dot(
            ds_g, kg, preferred_element_type=f32
        )
        dq_ref[:, lanes] = dq * scale
        dkw_ref[pl.ds(start, win_rows), lanes] += lax.dot_general(ds_b, q, tn, preferred_element_type=f32)
        dvw_ref[pl.ds(start, win_rows), lanes] += lax.dot_general(w_b, do, tn, preferred_element_type=f32)
        dkg_ref[:, lanes] += lax.dot_general(ds_g, q, tn, preferred_element_type=f32)
        dvg_ref[:, lanes] += lax.dot_general(w_g, do, tn, preferred_element_type=f32)


def band_call(mask, gmask, keep, queries, d_out, key_wide, value_wide, key_glob, value_glob, interpret=False):
    rows = queries.shape[0]
    wide_rows = key_wide.shape[0]
    slots = key_glob.shape[0]
    tiles, tile_rows, win_rows = mask.shape
    lanes = 2 * HEAD_DIM
    pairs = D // lanes
    f32 = jnp.float32
    row_spec = pl.BlockSpec((tile_rows, lanes), lambda p, t: (t, p))
    wide_spec = pl.BlockSpec((wide_rows, lanes), lambda p, t: (0, p))
    glob_spec = pl.BlockSpec((slots, lanes), lambda p, t: (0, p))
    return pl.pallas_call(
        band_kernel,
        grid=(pairs, tiles),
        in_specs=[
            pl.BlockSpec((1, tile_rows, win_rows), lambda p, t: (t, 0, 0)),
            pl.BlockSpec((1, slots), lambda p, t: (0, 0)),
            pl.BlockSpec((tile_rows, 1), lambda p, t: (t, 0)),
            row_spec,
            row_spec,
            wide_spec,
            wide_spec,
            glob_spec,
            glob_spec,
        ],
        out_specs=[row_spec, row_spec, wide_spec, wide_spec, glob_spec, glob_spec],
        out_shape=[
            jax.ShapeDtypeStruct((rows, D), f32),
            jax.ShapeDtypeStruct((rows, D), f32),
            jax.ShapeDtypeStruct((wide_rows, D), f32),
            jax.ShapeDtypeStruct((wide_rows, D), f32),
            jax.ShapeDtypeStruct((slots, D), f32),
            jax.ShapeDtypeStruct((slots, D), f32),
        ],
        compiler_params=pltpu.CompilerParams(dimension_semantics=("arbitrary", "arbitrary")),
        interpret=interpret,
    )(mask, gmask, keep, queries, d_out, key_wide, value_wide, key_glob, value_glob)


def band_kernel_t(mask_ref, gmask_ref, keep_ref, keep_row_ref, q_ref, qt_ref, do_ref, dot_ref,
                  kw_ref, kt_ref, vw_ref, vt_ref, kg_ref, kgt_ref, vg_ref, vgt_ref,
                  out_ref, dq_ref, dkw_ref, dvw_ref, dkg_ref, dvg_ref):
    scale = HEAD_DIM ** (-0.5)
    tile = pl.program_id(1)
    tile_rows = q_ref.shape[0]
    win_rows = mask_ref.shape[1]
    start = pl.multiple_of(tile * tile_rows, tile_rows)
    f32 = jnp.float32
    bf16 = jnp.bfloat16

    @pl.when(tile == 0)
    def _():
        dkw_ref[...] = jnp.zeros_like(dkw_ref)
        dvw_ref[...] = jnp.zeros_like(dvw_ref)
        dkg_ref[...] = jnp.zeros_like(dkg_ref)
        dvg_ref[...] = jnp.zeros_like(dvg_ref)

    band_bias = mask_ref[0]
    glob_bias = gmask_ref[...]
    keep = keep_ref[...].astype(bf16)
    keep_row = keep_row_ref[...].astype(bf16)
    shrink = jnp.asarray(scale, bf16)
    for head in range(q_ref.shape[1] // HEAD_DIM):
        lanes = slice(head * HEAD_DIM, (head + 1) * HEAD_DIM)
        q = q_ref[:, lanes] * shrink
        qt = qt_ref[lanes, :] * shrink
        do = do_ref[:, lanes] * keep
        dot = dot_ref[lanes, :] * keep_row
        kwin = kw_ref[pl.ds(start, win_rows), lanes]
        ktwin = kt_ref[lanes, pl.ds(start, win_rows)]
        vwin = vw_ref[pl.ds(start, win_rows), lanes]
        vtwin = vt_ref[lanes, pl.ds(start, win_rows)]
        kg = kg_ref[:, lanes]
        kgt = kgt_ref[lanes, :]
        vg = vg_ref[:, lanes]
        vgt = vgt_ref[lanes, :]
        s_b = jnp.dot(kwin, qt, preferred_element_type=f32) + band_bias
        s_g = jnp.dot(kg, qt, preferred_element_type=f32) + glob_bias
        top = jnp.maximum(jnp.max(s_b, axis=0, keepdims=True), jnp.max(s_g, axis=0, keepdims=True))
        e_b = jnp.exp(s_b - top)
        e_g = jnp.exp(s_g - top)
        inv = 1.0 / (jnp.sum(e_b, axis=0, keepdims=True) + jnp.sum(e_g, axis=0, keepdims=True))
        p_b = e_b * inv
        p_g = e_g * inv
        w_b = p_b.astype(bf16)
        w_g = p_g.astype(bf16)
        out = jnp.dot(vtwin, w_b, preferred_element_type=f32) + jnp.dot(
            vgt, w_g, preferred_element_type=f32
        )
        out_ref[lanes, :] = out
        delta = jnp.sum(
            dot.astype(f32) * out.astype(bf16).astype(f32), axis=0, keepdims=True
        )
        dp_b = jnp.dot(vwin, dot, preferred_element_type=f32)
        dp_g = jnp.dot(vg, dot, preferred_element_type=f32)
        ds_b = (p_b * (dp_b - delta)).astype(bf16)
        ds_g = (p_g * (dp_g - delta)).astype(bf16)
        dq = jnp.dot(ktwin, ds_b, preferred_element_type=f32) + jnp.dot(
            kgt, ds_g, preferred_element_type=f32
        )
        dq_ref[lanes, :] = dq * scale
        dkw_ref[pl.ds(start, win_rows), lanes] += jnp.dot(ds_b, q, preferred_element_type=f32)
        dvw_ref[pl.ds(start, win_rows), lanes] += jnp.dot(w_b, do, preferred_element_type=f32)
        dkg_ref[:, lanes] += jnp.dot(ds_g, q, preferred_element_type=f32)
        dvg_ref[:, lanes] += jnp.dot(w_g, do, preferred_element_type=f32)


def band_call_t(mask, gmask, keep, queries, d_out, key_wide, value_wide, key_glob, value_glob, interpret=False):
    rows = queries.shape[0]
    wide_rows = key_wide.shape[0]
    slots = key_glob.shape[0]
    tiles, tile_rows, win_rows = mask.shape
    lanes = 2 * HEAD_DIM
    pairs = D // lanes
    f32 = jnp.float32
    row_spec = pl.BlockSpec((tile_rows, lanes), lambda p, t: (t, p))
    col_spec = pl.BlockSpec((lanes, tile_rows), lambda p, t: (p, t))
    wide_spec = pl.BlockSpec((wide_rows, lanes), lambda p, t: (0, p))
    wide_t_spec = pl.BlockSpec((lanes, wide_rows), lambda p, t: (p, 0))
    glob_spec = pl.BlockSpec((slots, lanes), lambda p, t: (0, p))
    glob_t_spec = pl.BlockSpec((lanes, slots), lambda p, t: (p, 0))
    out_t, dq_t, dkw, dvw, dkg, dvg = pl.pallas_call(
        band_kernel_t,
        grid=(pairs, tiles),
        in_specs=[
            pl.BlockSpec((1, win_rows, tile_rows), lambda p, t: (t, 0, 0)),
            pl.BlockSpec((slots, 1), lambda p, t: (0, 0)),
            pl.BlockSpec((tile_rows, 1), lambda p, t: (t, 0)),
            pl.BlockSpec((1, tile_rows), lambda p, t: (0, t)),
            row_spec,
            col_spec,
            row_spec,
            col_spec,
            wide_spec,
            wide_t_spec,
            wide_spec,
            wide_t_spec,
            glob_spec,
            glob_t_spec,
            glob_spec,
            glob_t_spec,
        ],
        out_specs=[col_spec, col_spec, wide_spec, wide_spec, glob_spec, glob_spec],
        out_shape=[
            jax.ShapeDtypeStruct((D, rows), f32),
            jax.ShapeDtypeStruct((D, rows), f32),
            jax.ShapeDtypeStruct((wide_rows, D), f32),
            jax.ShapeDtypeStruct((wide_rows, D), f32),
            jax.ShapeDtypeStruct((slots, D), f32),
            jax.ShapeDtypeStruct((slots, D), f32),
        ],
        compiler_params=pltpu.CompilerParams(dimension_semantics=("arbitrary", "arbitrary")),
        interpret=interpret,
    )(
        jnp.transpose(mask, (0, 2, 1)),
        jnp.transpose(gmask),
        keep,
        jnp.transpose(keep),
        queries,
        jnp.transpose(queries),
        d_out,
        jnp.transpose(d_out),
        key_wide,
        jnp.transpose(key_wide),
        value_wide,
        jnp.transpose(value_wide),
        key_glob,
        jnp.transpose(key_glob),
        value_glob,
        jnp.transpose(value_glob),
    )
    return jnp.transpose(out_t), jnp.transpose(dq_t), dkw, dvw, dkg, dvg


def local(queries, keys, values, d_out, glob_pos, block_len):
    scale = HEAD_DIM ** (-0.5)
    rows = queries.shape[0]
    reach_rows = REACH * BLOCK
    tile_rows = TILE_BLOCKS * BLOCK
    tiles = rows // tile_rows
    win_rows = tile_rows + 2 * reach_rows
    wide_rows = rows + 2 * reach_rows
    first_row = lax.axis_index("seq") * rows
    lens_wide = jnp.pad(block_len, 2 * REACH)

    places = first_row + jnp.arange(rows, dtype=jnp.int32)
    marked_rows = jnp.any(glob_pos[:, None] == places[None, :], axis=0)
    local_pos = glob_pos - first_row
    is_local = (local_pos >= 0) & (local_pos < rows)
    local_index = jnp.where(is_local, local_pos, rows)
    inside_rows, _ = key_flags(first_row, rows, glob_pos, lens_wide)

    count = lax.axis_size("seq")
    own_blocks = rows // BLOCK
    slots = own_blocks * count
    glob_block = glob_pos // BLOCK
    slot_valid = jnp.zeros((slots,), bool).at[glob_block].set(True, mode="drop")
    own_slot = lax.axis_index("seq") * own_blocks + jnp.arange(own_blocks, dtype=jnp.int32)
    own_match = glob_block[None, :] == own_slot[:, None]
    own_has = jnp.any(own_match, axis=1)
    own_pos = jnp.sum(jnp.where(own_match, glob_pos[None, :], 0), axis=1) - first_row
    own_offset = own_pos - BLOCK * jnp.arange(own_blocks, dtype=jnp.int32)
    own_row = own_has[:, None] & (jnp.arange(BLOCK, dtype=jnp.int32)[None, :] == own_offset[:, None])

    def place(base, extra):
        shaped = base.reshape(own_blocks, BLOCK, D)
        return jnp.where(own_row[:, :, None], shaped + extra[:, None, :], shaped).reshape(rows, D)

    own_pick = (
        own_has[:, None] & (jnp.arange(rows, dtype=jnp.int32)[None, :] == own_pos[:, None])
    ).astype(jnp.bfloat16)
    picked = jnp.stack(
        [
            jnp.dot(own_pick, source, preferred_element_type=jnp.float32).astype(jnp.bfloat16)
            for source in (queries, keys, values, d_out)
        ]
    )
    shared = jnp.transpose(gather_small(picked), (1, 0, 2, 3)).reshape(4, slots, D)
    qg = to_heads(shared[0])
    kg = to_heads(shared[1])
    vg = to_heads(shared[2])
    dog = to_heads(shared[3])

    pair = jnp.stack([keys, values])
    from_left, from_right = halo(pair, reach_rows)
    pair_wide = jnp.concatenate([from_left, pair, from_right], axis=1)
    k_h = to_heads(keys)
    v_h = to_heads(values)

    inside_wide, marked_wide = key_flags(first_row - reach_rows, wide_rows, glob_pos, lens_wide)
    allowed_wide = inside_wide & jnp.logical_not(marked_wide)

    allowed_t = jnp.stack(
        [lax.slice_in_dim(allowed_wide, t * tile_rows, t * tile_rows + win_rows) for t in range(tiles)]
    )
    q_block = (jnp.arange(rows, dtype=jnp.int32) // BLOCK).reshape(tiles, tile_rows)
    k_block = jnp.stack(
        [t * TILE_BLOCKS + jnp.arange(win_rows, dtype=jnp.int32) // BLOCK - REACH for t in range(tiles)]
    )
    near = jnp.abs(q_block[:, :, None] - k_block[:, None, :]) <= REACH
    band_mask = near & allowed_t[:, None, :]
    band_out, band_dq, dk_wide, dv_wide, dk_glob, dv_glob = band_call_t(
        jnp.where(band_mask, 0.0, neg_large).astype(jnp.float32),
        jnp.where(slot_valid, 0.0, neg_large).astype(jnp.float32)[None, :],
        jnp.logical_not(marked_rows).astype(jnp.float32)[:, None],
        queries,
        d_out,
        pair_wide[0],
        pair_wide[1],
        shared[1],
        shared[2],
    )

    g_score = mixed("hge,hre->hgr", qg, k_h) * scale
    g_score = jnp.where(inside_rows[None, None, :], g_score, neg_large)
    g_top = jnp.max(g_score, axis=-1)
    g_sum = jnp.sum(jnp.exp(g_score - g_top[..., None]), axis=-1)
    stats = gather_small(jnp.stack([g_top, g_sum]))
    all_top = stats[:, 0]
    top_glob = jnp.max(all_top, axis=0)
    sum_glob = jnp.sum(stats[:, 1] * jnp.exp(all_top - top_glob[None]), axis=0)
    lse_glob = top_glob + jnp.log(sum_glob)
    g_prob = jnp.where(slot_valid[None, :, None], jnp.exp(g_score - lse_glob[..., None]), 0.0)
    g_weight = g_prob.astype(jnp.bfloat16)
    out_own = reduce_own(from_heads(mixed("hgr,hre->hge", g_weight, v_h)))
    out_own16 = out_own.astype(jnp.bfloat16)
    delta_own = jnp.sum(
        by_head(picked[3]).astype(jnp.float32) * by_head(out_own16).astype(jnp.float32), axis=-1
    )
    delta_g = jnp.transpose(gather_small(delta_own).reshape(slots, HEADS))
    band_out16 = band_out.astype(jnp.bfloat16)
    out_full = jnp.where(
        own_row[:, :, None], out_own16[:, None, :], band_out16.reshape(own_blocks, BLOCK, D)
    ).reshape(rows, D)

    grad_wide = jnp.stack([dk_wide, dv_wide])
    rims = jnp.concatenate(
        [grad_wide[:, :reach_rows], grad_wide[:, wide_rows - reach_rows :]], axis=1
    )
    back_left, back_right = halo(rims, reach_rows)
    center = grad_wide[:, reach_rows : reach_rows + rows]
    center = center.at[:, :reach_rows].add(back_left).at[:, rows - reach_rows :].add(back_right)

    g_dprob = mixed("hge,hre->hgr", dog, v_h)
    g_dscore = (g_prob * (g_dprob - delta_g[..., None])).astype(jnp.bfloat16)
    row_dq = mixed("hgr,hre->hge", g_dscore, k_h) * scale
    part_dk = mixed("hgr,hge->hre", g_dscore, qg) * scale
    part_dv = mixed("hgr,hge->hre", g_weight, dog)

    totals = reduce_own(
        jnp.concatenate([from_heads(row_dq), dk_glob, dv_glob], axis=1)
    )
    d_queries = place(band_dq, totals[:, :D])
    d_keys = place(center[0] + from_heads(part_dk), totals[:, D : 2 * D])
    d_values = place(center[1] + from_heads(part_dv), totals[:, 2 * D :])
    return (
        out_full,
        d_queries.astype(jnp.bfloat16),
        d_keys.astype(jnp.bfloat16),
        d_values.astype(jnp.bfloat16),
    )


def solution(mesh):
    rows = P(("groups", "seq"), None)
    return jax.shard_map(
        local,
        mesh=mesh,
        in_specs=(rows, rows, rows, rows, P("groups"), P("groups")),
        out_specs=(rows, rows, rows, rows),
        check_vma=False,
    )
```
